32 devices in a mesh: gx: 4 (over z), gy: 8 (over y, x, core).
Axes of the slice: x: 2, y: 2, z: 4, core: 2. Of those that a mesh axis runs over, the one named last changes fastest.
Arguments:
- right_side: float32 [1024, 16, 512], P(('gx', 'gy')), may hold values from -6 to 6
- diag_inverse: bfloat16 [1024, 16, 16, 512], P(('gx', 'gy')), may hold values from -0.5 to 1
- face_jac: float32 [6, 16, 16, 1024], P(None, None, None, ('gx', 'gy')), may hold values from -0.9 to 0.9
- level_counts: int32 [32, 12], replicated, may hold values from 1 to 6, 32 in all within a row
Outputs:
- increment: float32 [1024, 16, 512], P(('gx', 'gy'))
The draws below stay inside these ranges and needn't reach their ends.
Inputs may be any that keep to these rules, and one draw needn't show every extreme that they name: `level_counts`: row a 8 + b lists, in slot order, how many of device (a, b)'s blocks belong to each level; each row sums to 32.
All inputs are finite; a program needn't handle non-finite values.
Results may differ from the reference program's by a relative error of at most 0.0003.
Values sent between devices are 32-bit elements; how exact they have to be, the bound alone decides.
No kernel may reach another device: no remote copies, remote signals or barrier semaphores. Data moves between devices by JAX's collectives and lax.ppermute only.
A program may use at most 64 MiB of HBM per device.

```python
import math
import jax
import jax.numpy as jnp
import numpy as np
from jax import lax

NC = 16
SIDE = 8
CB = 512
LEVELS = 12
RX = 2
RY = 2
NBZ = 8
BD = 32
KL = 6
NBLOCKS = 1024
N_GX = 4
N_GY = 8


def draw_diag_inverse(key, part):
    first_key, second_key = jax.random.split(jax.random.fold_in(key, 11), 2)
    shape_full = (NBLOCKS, NC, NC, CB)
    diagonal_values = jnp.exp(jax.random.uniform(first_key, (NBLOCKS, NC, 1, CB), jnp.float32, math.log(0.5), math.log(1.0)))
    spread_values = jnp.clip(jax.random.normal(second_key, shape_full, jnp.float32) * 0.07, -0.5, 0.5)
    identity_mask = (jnp.arange(NC)[:, None] == jnp.arange(NC)[None, :])[None, :, :, None]
    return jnp.where(identity_mask, diagonal_values, spread_values).astype(jnp.bfloat16)


def steps_of(own_key, dims, pieces, low, high):
    gain, own = 1.0, jax.random.fold_in(own_key, 6)
    for position, shards_of in pieces:
        steps = jnp.exp(jax.random.uniform(jax.random.fold_in(own, position), (shards_of,), jnp.float32, low / len(pieces), high / len(pieces)))
        gain = gain * jnp.repeat(steps, dims[position] // shards_of).reshape([-1 if axis == position else 1 for axis in range(len(dims))])
    return gain


def split_up(amount, total, most, skew):
    loads = [(1 << 20) // math.isqrt(grade ** skew) + 1 for grade in range(2, amount + 1)]
    spare, counts = total - most - (amount - 1), [1] * (amount - 1)
    while spare > 0:
        free = [i for i in range(amount - 1) if counts[i] < most]
        whole, remaining = sum([loads[i] for i in free]), spare
        for i in free:
            extra = min(most - counts[i], max(1, remaining * loads[i] // whole), spare)
            counts[i] = counts[i] + extra
            spare = spare - extra
    return np.array([most] + counts)


def ragged(own_key, number_of, total, limit, slope):
    if number_of == 2:
        one = jax.random.randint(own_key, (), max(1, total - limit), min(limit, total - 1) + 1)
        return jnp.stack([one, total - one])
    sizes = jnp.asarray(split_up(number_of, total, limit, slope), jnp.int32)
    twos = (number_of - 1) // 2
    source_of, taker = sizes[1:1 + 2 * twos:2], sizes[2:2 + 2 * twos:2]
    room = jnp.minimum(source_of - 1, limit - taker)
    passed = jax.random.randint(jax.random.fold_in(own_key, 1), (twos,), 0, 1 << 20) % (room + 1)
    sizes = sizes.at[1:1 + 2 * twos:2].set(source_of - passed).at[2:2 + 2 * twos:2].set(taker + passed)
    return sizes[jax.random.permutation(jax.random.fold_in(own_key, 2), number_of)]


def centred(stream_key, dims, width, reach, cuts=(), kind=jnp.bfloat16):
    values = width * jax.random.normal(stream_key, dims, jnp.float32)
    if cuts:
        values = values * steps_of(stream_key, dims, cuts, -0.22, 0.18)
    return jnp.clip(values, -reach, reach).astype(kind)


def setup_inputs(seed: int = 0) -> dict:
    splits = jax.random.split(jax.random.key(seed), 5)
    right_side = centred(splits[0], (NBLOCKS, NC, CB), 1.0, 6.0, ((0, 32),), jnp.float32)
    diag_inverse = draw_diag_inverse(jax.random.fold_in(splits[4], 71), 0)
    face_jac = centred(splits[2], (6, NC, NC, NBLOCKS), 0.15, 0.9, ((3, 32),), jnp.float32)
    level_counts = jax.vmap(lambda own: ragged(own, LEVELS, BD, KL, 2))(jax.random.split(splits[3], (N_GX * N_GY))).reshape((N_GX * N_GY, LEVELS)).astype(jnp.int32)
    return dict(right_side=right_side, diag_inverse=diag_inverse, face_jac=face_jac, level_counts=level_counts)


HIGHEST_PRECISION = lax.Precision.HIGHEST
OPPOSITE = (1, 0, 3, 2, 5, 4)
DIRECTION_MOVES = ((0, 1), (0, -1), (1, 1), (1, -1), (2, 1), (2, -1))


def face_cells(edge_cells):
    cell_ids = np.arange(edge_cells ** 3).reshape(edge_cells, edge_cells, edge_cells)
    layers = [cell_ids[edge_cells - 1], cell_ids[0], cell_ids[:, edge_cells - 1], cell_ids[:, 0], cell_ids[:, :, edge_cells - 1], cell_ids[:, :, 0]]
    outward = np.stack([layer_ids.reshape(-1) for layer_ids in layers]).astype(np.int32)
    inward = outward[list(OPPOSITE)]
    return outward, inward


def slot_layout(step_x, step_y, count_x, count_y, count_z):
    ordering = sorted((step_x * along_x + step_y * along_y + along_z, along_x, along_y, along_z) for along_x in range(count_x) for along_y in range(count_y) for along_z in range(count_z))
    coords = np.array([record[1:] for record in ordering], dtype=np.int64)
    where_slot = np.zeros((count_x, count_y, count_z), dtype=np.int64)
    where_slot[coords[:, 0], coords[:, 1], coords[:, 2]] = np.arange(len(ordering))
    return coords, where_slot


def global_neighbours(coords, where_slot, count_x, count_y):
    shape_blocks = np.array(where_slot.shape)
    device_ids = np.arange(count_x * count_y)
    place_x = device_ids // count_y
    place_y = device_ids % count_y
    global_grid = np.stack([
        place_x[:, None] + count_x * coords[None, :, 0],
        place_y[:, None] + count_y * coords[None, :, 1],
        np.broadcast_to(coords[None, :, 2], (len(device_ids), len(coords)))], axis=-1)
    sizes_global = np.array([count_x * shape_blocks[0], count_y * shape_blocks[1], shape_blocks[2]])
    columns = []
    for dimension, offset_step in DIRECTION_MOVES:
        moved = global_grid.copy()
        moved[..., dimension] += offset_step
        inside = np.all((moved >= 0) & (moved < sizes_global), axis=-1)
        moved = np.clip(moved, 0, sizes_global - 1)
        owner_device = (moved[..., 0] % count_x) * count_y + moved[..., 1] % count_y
        slot_ids = where_slot[moved[..., 0] // count_x, moved[..., 1] // count_y, moved[..., 2]]
        columns.append(np.where(inside, owner_device * len(coords) + slot_ids, -1).reshape(-1))
    return np.stack(columns, axis=1).astype(np.int32)


def apply_inverse(block_inv, vectors):
    return jnp.einsum('bcex,bex->bcx', block_inv, vectors, precision=HIGHEST_PRECISION)


def reference(right_side, diag_inverse, face_jac, level_counts):
    slot_total = RX * RY * NBZ
    device_total = N_GX * N_GY
    coords, where_slot = slot_layout(N_GX, N_GY, RX, RY, NBZ)
    outward, inward = face_cells(SIDE)
    neighbours = jnp.asarray(global_neighbours(coords, where_slot, N_GX, N_GY))
    ends_all = jnp.cumsum(level_counts, axis=1)
    begins_all = ends_all - level_counts
    levels_flat = jnp.sum(jnp.arange(slot_total, dtype=jnp.int32)[None, :, None] >= ends_all[:, None, :], axis=2).astype(jnp.int32).reshape(-1)
    unknowns = right_side.shape[1]
    component_ids = jnp.arange(unknowns, dtype=jnp.int32)[None, :, None]
    device_base = jnp.arange(device_total, dtype=jnp.int32) * slot_total
    offsets = jnp.arange(KL, dtype=jnp.int32)
    last_block = levels_flat.shape[0] - 1

    def level_step(level_now, current, accum, forward, base_values):
        window = jnp.clip(begins_all[:, level_now], 0, slot_total - KL).astype(jnp.int32)
        chosen = ((device_base + window)[:, None] + offsets[None, :]).reshape(-1)
        active = levels_flat[chosen] == level_now
        block_inv = diag_inverse[chosen].astype(jnp.float32)
        if forward:
            fresh_values = apply_inverse(block_inv, right_side[chosen] - accum[chosen])
        else:
            fresh_values = base_values[chosen] - apply_inverse(block_inv, accum[chosen])
        updated = jnp.where(active[:, None, None], fresh_values, current[chosen])
        current = current.at[chosen].set(updated)
        jac_part = face_jac[:, :, :, chosen]
        layers = updated[:, :, outward]
        increments = jnp.einsum('dceb,bedk->dbck', jac_part, layers, precision=HIGHEST_PRECISION) * active[None, :, None, None].astype(jnp.float32)
        for direction in range(6):
            target = neighbours[chosen, direction]
            clipped = jnp.clip(target, 0, last_block)
            target_level = levels_flat[clipped]
            ordered = target_level > level_now if forward else target_level < level_now
            accepted = (target >= 0) & ordered
            accum = accum.at[clipped[:, None, None], component_ids, jnp.asarray(inward[direction])[None, None, :]].add(jnp.where(accepted[:, None, None], increments[direction], jnp.float32(0.0)))
        return current, accum

    blank = jnp.zeros(right_side.shape, jnp.float32)
    current, accum = blank, blank
    for level_now in range(LEVELS):
        current, accum = level_step(level_now, current, accum, True, blank)
    half_step = current
    current, accum = half_step, blank
    for level_now in range(LEVELS - 1, -1, -1):
        current, accum = level_step(level_now, current, accum, False, half_step)
    return current
```

```python
import functools

import jax
import jax.numpy as jnp
import numpy as np
from jax import lax
from jax.experimental import pallas as pl
from jax.experimental.pallas import tpu as pltpu
from jax.sharding import PartitionSpec as P

SIDE = 8
LEVELS = 12
RX = 2
RY = 2
NBZ = 8
KL = 6
NF = 6
FW = SIDE * SIDE
TW = 48

OPPOSITE = (1, 0, 3, 2, 5, 4)
DIRECTION_MOVES = ((0, 1), (0, -1), (1, 1), (1, -1), (2, 1), (2, -1))


def slot_layout(step_x, step_y, count_x, count_y, count_z):
    ordering = sorted(
        (
            (step_x * along_x + step_y * along_y + along_z, along_x, along_y, along_z)
            for along_x in range(count_x)
            for along_y in range(count_y)
            for along_z in range(count_z)
        )
    )
    coords = np.array([record[1:] for record in ordering], dtype=np.int64)
    where_slot = np.zeros((count_x, count_y, count_z), dtype=np.int64)
    where_slot[coords[:, 0], coords[:, 1], coords[:, 2]] = np.arange(len(ordering))
    return (coords, where_slot)


def step_table(coords, where_slot, dimension, offset_step):
    moved = coords.copy()
    moved[:, dimension] += offset_step
    bound_size = where_slot.shape[dimension]
    inside = (moved[:, dimension] >= 0) & (moved[:, dimension] < bound_size)
    clipped = np.clip(moved, 0, np.array(where_slot.shape) - 1)
    target = where_slot[clipped[:, 0], clipped[:, 1], clipped[:, 2]]
    return np.where(inside, target, -1).astype(np.int32)


def face_matrices(edge_cells):
    cell_ids = np.arange(edge_cells**3).reshape(edge_cells, edge_cells, edge_cells)
    layers = [
        cell_ids[edge_cells - 1],
        cell_ids[0],
        cell_ids[:, edge_cells - 1],
        cell_ids[:, 0],
        cell_ids[:, :, edge_cells - 1],
        cell_ids[:, :, 0],
    ]
    outward = np.stack([layer_ids.reshape(-1) for layer_ids in layers])
    cell_total = edge_cells**3
    face_width = edge_cells * edge_cells
    gather = np.zeros((cell_total, NF * face_width), dtype=np.float32)
    for face_index in range(NF):
        gather[outward[face_index], face_index * face_width + np.arange(face_width)] = 1.0
    return gather, np.ascontiguousarray(gather.T)


def split3(x):
    hi = x.astype(jnp.bfloat16)
    rest = x - hi.astype(jnp.float32)
    mid = rest.astype(jnp.bfloat16)
    low = (rest - mid.astype(jnp.float32)).astype(jnp.bfloat16)
    return hi, mid, low


def mm(a, b):
    return jnp.dot(a, b, preferred_element_type=jnp.float32)


def dot_exact01(x, table):
    hi, mid, low = split3(x)
    return mm(hi, table) + mm(mid, table) + mm(low, table)


def dot_full(a, b):
    ah, am, al = split3(a)
    bh, bm, bl = split3(b)
    return (
        mm(ah, bh)
        + (mm(ah, bm) + mm(am, bh))
        + (mm(ah, bl) + mm(al, bh) + mm(am, bm))
    )


def level_kernel(forward, lev_ref, tbl_ref, accf_in, base_hbm, cur_hbm, dinv_hbm, jac_hbm,
                 rxp, rxm, ryp, rym, gmat, smat,
                 accf, cur_out, sx, sy,
                 dbuf, jbuf, bbuf, cbuf, sems):
    lvl = lev_ref[0]

    def T(j):
        return tbl_ref[lvl, j]

    win = T(0)
    cp_d = pltpu.make_async_copy(dinv_hbm.at[pl.ds(win, KL)], dbuf, sems.at[0])
    cp_j = pltpu.make_async_copy(jac_hbm.at[pl.ds(win, KL)], jbuf, sems.at[1])
    cp_b = pltpu.make_async_copy(base_hbm.at[pl.ds(win, KL)], bbuf, sems.at[2])
    cp_c = pltpu.make_async_copy(cur_hbm.at[pl.ds(win, KL)], cbuf, sems.at[3])
    cp_d.start()
    cp_j.start()
    cp_b.start()
    cp_c.start()

    accf[...] = accf_in[...]
    lane = lax.broadcasted_iota(jnp.int32, (16, 128), 1)
    low_half = lane < 64

    for src, off, chunk, keep_low in ((rxp, 19, 0, False), (rxm, 25, 0, True),
                                      (ryp, 31, 1, False), (rym, 37, 1, True)):
        for k in range(KL):
            t = T(off + k)

            @pl.when(t >= 0)
            def _():
                moved = pltpu.roll(src[k], 64, 1)
                keep = low_half if keep_low else jnp.logical_not(low_half)
                sl = pl.ds(chunk * 128, 128)
                accf[t, :, sl] = accf[t, :, sl] + jnp.where(keep, moved, 0.0)

    cp_d.wait()
    cp_j.wait()
    cp_b.wait()
    cp_c.wait()

    nr = KL * 16
    acc_win = accf[pl.ds(win, KL)].reshape(nr, NF * FW)
    lower = dot_exact01(acc_win, smat[...])
    base = bbuf[...].reshape(nr, SIDE**3)

    def dinv_apply(v):
        rows = []
        for k in range(KL):
            vk = v[16 * k:16 * (k + 1)]
            parts = []
            for c0 in range(0, 16, 4):
                d = dbuf[k, c0:c0 + 4].astype(jnp.float32)
                parts.append(jnp.sum(d * vk[None], axis=1))
            rows.append(jnp.concatenate(parts, axis=0))
        return jnp.concatenate(rows, axis=0)

    if forward:
        fresh = dinv_apply(base - lower)
    else:
        fresh = base - dinv_apply(lower)
    olds = cbuf[...]
    news = []
    for k in range(KL):
        news.append(jnp.where(T(1 + k) > 0, fresh[16 * k:16 * (k + 1)], olds[k]))
    new = jnp.concatenate(news, axis=0)
    cbuf[...] = new.reshape(KL, 16, SIDE**3)
    cp_o = pltpu.make_async_copy(cbuf, cur_out.at[pl.ds(win, KL)], sems.at[4])
    cp_o.start()

    faces = dot_exact01(new, gmat[...])
    flane = lax.broadcasted_iota(jnp.int32, (16, NF * FW), 1) // FW
    for k in range(KL):
        prod = dot_full(jbuf[k], faces[16 * k:16 * (k + 1)])
        inc = jnp.zeros((16, NF * FW), jnp.float32)
        for d in range(NF):
            inc = inc + jnp.where(flane == d, prod[16 * d:16 * (d + 1)], 0.0)
        sx[k] = inc[:, 0:128]
        sy[k] = inc[:, 128:256]
        zpart = pltpu.roll(inc[:, 256:384], 64, 1)
        tp = T(7 + k)
        tm = T(13 + k)

        @pl.when(tp >= 0)
        def _():
            sl = pl.ds(256, 128)
            accf[tp, :, sl] = accf[tp, :, sl] + jnp.where(low_half, 0.0, zpart)

        @pl.when(tm >= 0)
        def _():
            sl = pl.ds(256, 128)
            accf[tm, :, sl] = accf[tm, :, sl] + jnp.where(low_half, zpart, 0.0)

    cp_o.wait()


def run_level(forward, lev, tbl, accf, base, cur, dinv, jac, recv, gmat, smat):
    n_blocks = accf.shape[0]
    kern = functools.partial(level_kernel, forward)
    smem = pl.BlockSpec(memory_space=pltpu.SMEM)
    vmem = pl.BlockSpec(memory_space=pltpu.VMEM)
    anyspace = pl.BlockSpec(memory_space=pl.ANY)
    out_shape = (
        jax.ShapeDtypeStruct(accf.shape, jnp.float32),
        jax.ShapeDtypeStruct(cur.shape, jnp.float32),
        jax.ShapeDtypeStruct((KL, 16, 128), jnp.float32),
        jax.ShapeDtypeStruct((KL, 16, 128), jnp.float32),
    )
    return pl.pallas_call(
        kern,
        out_shape=out_shape,
        in_specs=[smem, smem, vmem, anyspace, anyspace, anyspace, anyspace,
                  vmem, vmem, vmem, vmem, vmem, vmem],
        out_specs=(vmem, anyspace, vmem, vmem),
        scratch_shapes=[
            pltpu.VMEM((KL,) + dinv.shape[1:], dinv.dtype),
            pltpu.VMEM((KL,) + jac.shape[1:], jnp.float32),
            pltpu.VMEM((KL,) + base.shape[1:], jnp.float32),
            pltpu.VMEM((KL,) + cur.shape[1:], jnp.float32),
            pltpu.SemaphoreType.DMA((5,)),
        ],
        input_output_aliases={2: 0, 4: 1},
        compiler_params=pltpu.CompilerParams(vmem_limit_bytes=48 * 1024 * 1024),
    )(lev, tbl, accf, base, cur, dinv, jac, *recv, gmat, smat)


def shift_along(value, axis, steps):
    count = lax.axis_size(axis)
    pairs = [(source, (source + steps) % count) for source in range(count)]
    return lax.ppermute(value, axis, pairs)


def exchange(sx, sy):
    return (
        shift_along(sx, "gx", 1),
        shift_along(sx, "gx", -1),
        shift_along(sy, "gy", 1),
        shift_along(sy, "gy", -1),
    )


def build_tables(level_counts, slot_count, forward):
    count_x = lax.axis_size("gx")
    count_y = lax.axis_size("gy")
    place_x = lax.axis_index("gx")
    place_y = lax.axis_index("gy")
    coords, where_slot = slot_layout(count_x, count_y, RX, RY, NBZ)
    nbs = [jnp.asarray(step_table(coords, where_slot, dm, st)) for dm, st in DIRECTION_MOVES]
    ends_all = jnp.cumsum(level_counts, axis=1)
    begins_all = ends_all - level_counts
    slots = jnp.arange(slot_count, dtype=jnp.int32)
    all_levels = jnp.sum(slots[None, :, None] >= ends_all[:, None, :], axis=2).astype(jnp.int32)
    own_row = place_x * count_y + place_y
    source_rows = [
        (place_x - 1) % count_x * count_y + place_y,
        (place_x + 1) % count_x * count_y + place_y,
        place_x * count_y + (place_y - 1) % count_y,
        place_x * count_y + (place_y + 1) % count_y,
    ]
    at_edge = [place_x == 0, place_x == count_x - 1, place_y == 0, place_y == count_y - 1]
    my_lv = all_levels[own_row]
    levels = jnp.arange(LEVELS, dtype=jnp.int32)
    offsets = jnp.arange(KL, dtype=jnp.int32)

    def ordered(target_level, now):
        return target_level > now if forward else target_level < now

    def window(row, now):
        begin = jnp.take(begins_all[row], jnp.clip(now, 0, LEVELS - 1))
        return jnp.clip(begin, 0, slot_count - KL)

    win = window(own_row, levels)
    wslots = win[:, None] + offsets[None, :]
    act = my_lv[wslots] == levels[:, None]
    cols = [win[:, None], act.astype(jnp.int32)]
    for d in (4, 5):
        tgt = nbs[d][wslots]
        ok = (tgt >= 0) & ordered(my_lv[jnp.clip(tgt, 0, slot_count - 1)], levels[:, None]) & act
        cols.append(jnp.where(ok, tgt, -1))
    sender_levels = levels - 1 if forward else levels + 1
    for d in range(4):
        row = source_rows[d]
        swin = window(row, sender_levels)
        sslots = swin[:, None] + offsets[None, :]
        s_act = all_levels[row][sslots] == sender_levels[:, None]
        tgt = jnp.where(at_edge[d], nbs[d][sslots], sslots)
        ok = (tgt >= 0) & ordered(my_lv[jnp.clip(tgt, 0, slot_count - 1)], sender_levels[:, None]) & s_act
        cols.append(jnp.where(ok, tgt, -1))
    table = jnp.concatenate(cols, axis=1).astype(jnp.int32)
    return jnp.pad(table, ((0, 0), (0, TW - table.shape[1])), constant_values=-1)


def body(right_side, diag_inverse, face_jac, level_counts):
    slot_count = right_side.shape[0]
    unknowns = right_side.shape[1]
    gather_np, scatter_np = face_matrices(SIDE)
    gmat = jnp.asarray(gather_np, dtype=jnp.bfloat16)
    smat = jnp.asarray(scatter_np, dtype=jnp.bfloat16)
    jac = jnp.transpose(face_jac, (3, 0, 1, 2)).reshape(slot_count, NF * unknowns, unknowns)
    tbl_f = build_tables(level_counts, slot_count, True)
    tbl_b = build_tables(level_counts, slot_count, False)
    zero_recv = tuple(jnp.zeros((KL, 16, 128), jnp.float32) for _ in range(4))

    def lev_arr(v):
        return jnp.reshape(jnp.asarray(v, jnp.int32), (1,))

    accf = jnp.zeros((slot_count, unknowns, NF * FW), jnp.float32)
    cur = jnp.zeros(right_side.shape, jnp.float32)
    accf, cur, sx, sy = run_level(True, lev_arr(0), tbl_f, accf, right_side, cur, diag_inverse,
                                  jac, zero_recv, gmat, smat)

    def fwd(l, carry):
        accf, cur, sx, sy = carry
        recv = exchange(sx, sy)
        return run_level(True, lev_arr(l), tbl_f, accf, right_side, cur, diag_inverse, jac,
                         recv, gmat, smat)

    accf, half, sx, sy = lax.fori_loop(1, LEVELS, fwd, (accf, cur, sx, sy))

    accf = jnp.zeros((slot_count, unknowns, NF * FW), jnp.float32)
    accf, cur, sx, sy = run_level(False, lev_arr(LEVELS - 1), tbl_b, accf, half, half,
                                  diag_inverse, jac, zero_recv, gmat, smat)

    def bwd(i, carry):
        accf, cur, sx, sy = carry
        recv = exchange(sx, sy)
        return run_level(False, lev_arr(LEVELS - 2 - i), tbl_b, accf, half, cur, diag_inverse,
                         jac, recv, gmat, smat)

    accf, result, sx, sy = lax.fori_loop(0, LEVELS - 1, bwd, (accf, cur, sx, sy))
    return result


def solution(mesh):
    return jax.shard_map(
        body,
        mesh=mesh,
        in_specs=(
            P(("gx", "gy"), None, None),
            P(("gx", "gy"), None, None, None),
            P(None, None, None, ("gx", "gy")),
            P(),
        ),
        out_specs=P(("gx", "gy"), None, None),
        check_vma=False,
    )
```

```python
import functools

import jax
import jax.numpy as jnp
import numpy as np
from jax import lax
from jax.experimental import pallas as pl
from jax.experimental.pallas import tpu as pltpu
from jax.sharding import PartitionSpec as P

SIDE = 8
LEVELS = 12
RX = 2
RY = 2
NBZ = 8
KL = 6
NF = 6
FW = SIDE * SIDE
TW = 48

OPPOSITE = (1, 0, 3, 2, 5, 4)
DIRECTION_MOVES = ((0, 1), (0, -1), (1, 1), (1, -1), (2, 1), (2, -1))


def slot_layout(step_x, step_y, count_x, count_y, count_z):
    ordering = sorted(
        (
            (step_x * along_x + step_y * along_y + along_z, along_x, along_y, along_z)
            for along_x in range(count_x)
            for along_y in range(count_y)
            for along_z in range(count_z)
        )
    )
    coords = np.array([record[1:] for record in ordering], dtype=np.int64)
    where_slot = np.zeros((count_x, count_y, count_z), dtype=np.int64)
    where_slot[coords[:, 0], coords[:, 1], coords[:, 2]] = np.arange(len(ordering))
    return (coords, where_slot)


def step_table(coords, where_slot, dimension, offset_step):
    moved = coords.copy()
    moved[:, dimension] += offset_step
    bound_size = where_slot.shape[dimension]
    inside = (moved[:, dimension] >= 0) & (moved[:, dimension] < bound_size)
    clipped = np.clip(moved, 0, np.array(where_slot.shape) - 1)
    target = where_slot[clipped[:, 0], clipped[:, 1], clipped[:, 2]]
    return np.where(inside, target, -1).astype(np.int32)


def face_matrices(edge_cells):
    cell_ids = np.arange(edge_cells**3).reshape(edge_cells, edge_cells, edge_cells)
    layers = [
        cell_ids[edge_cells - 1],
        cell_ids[0],
        cell_ids[:, edge_cells - 1],
        cell_ids[:, 0],
        cell_ids[:, :, edge_cells - 1],
        cell_ids[:, :, 0],
    ]
    outward = np.stack([layer_ids.reshape(-1) for layer_ids in layers])
    cell_total = edge_cells**3
    face_width = edge_cells * edge_cells
    gather = np.zeros((cell_total, NF * face_width), dtype=np.float32)
    for face_index in range(NF):
        gather[outward[face_index], face_index * face_width + np.arange(face_width)] = 1.0
    return gather, np.ascontiguousarray(gather.T)


def split3(x):
    hi = x.astype(jnp.bfloat16)
    rest = x - hi.astype(jnp.float32)
    mid = rest.astype(jnp.bfloat16)
    low = (rest - mid.astype(jnp.float32)).astype(jnp.bfloat16)
    return hi, mid, low


def mm(a, b):
    return jnp.dot(a, b, preferred_element_type=jnp.float32)


def dot_exact01(x, table):
    hi, mid, low = split3(x)
    return mm(hi, table) + mm(mid, table) + mm(low, table)


def split2(x):
    hi = x.astype(jnp.bfloat16)
    return hi, (x - hi.astype(jnp.float32)).astype(jnp.bfloat16)


def dot_full(a, b):
    ah, al = split2(a)
    bh, bl = split2(b)
    return mm(ah, bh) + (mm(ah, bl) + mm(al, bh))


def level_kernel(forward, lev_ref, tbl_ref, accf_in, base_hbm, cur_hbm, dinv_hbm, jac_hbm,
                 rxp, rxm, ryp, rym, gmat, smat,
                 accf, cur_out, sx, sy,
                 dbuf, jbuf, bbuf, cbuf, sems):
    lvl = lev_ref[0]

    def T(j):
        return tbl_ref[lvl, j]

    win = T(0)
    cp_d = pltpu.make_async_copy(dinv_hbm.at[pl.ds(win, KL)], dbuf, sems.at[0])
    cp_j = pltpu.make_async_copy(jac_hbm.at[pl.ds(win, KL)], jbuf, sems.at[1])
    cp_b = pltpu.make_async_copy(base_hbm.at[pl.ds(win, KL)], bbuf, sems.at[2])
    cp_c = pltpu.make_async_copy(cur_hbm.at[pl.ds(win, KL)], cbuf, sems.at[3])
    cp_d.start()
    cp_j.start()
    cp_b.start()
    cp_c.start()

    accf[...] = accf_in[...]
    lane = lax.broadcasted_iota(jnp.int32, (16, 128), 1)
    low_half = lane < 64

    for src, off, chunk, keep_low in ((rxp, 19, 0, False), (rxm, 25, 0, True),
                                      (ryp, 31, 1, False), (rym, 37, 1, True)):
        for k in range(KL):
            t = T(off + k)

            @pl.when(t >= 0)
            def _():
                moved = pltpu.roll(src[k], 64, 1)
                keep = low_half if keep_low else jnp.logical_not(low_half)
                sl = pl.ds(chunk * 128, 128)
                accf[t, :, sl] = accf[t, :, sl] + jnp.where(keep, moved, 0.0)

    cp_d.wait()
    cp_j.wait()
    cp_b.wait()
    cp_c.wait()

    nr = KL * 16
    acc_win = accf[pl.ds(win, KL)].reshape(nr, NF * FW)
    lower = dot_exact01(acc_win, smat[...])
    base = bbuf[...].reshape(nr, SIDE**3)

    def dinv_apply(v):
        rows = []
        for k in range(KL):
            vk = v[16 * k:16 * (k + 1)]
            parts = []
            for c0 in range(0, 16, 4):
                d = dbuf[k, c0:c0 + 4].astype(jnp.float32)
                parts.append(jnp.sum(d * vk[None], axis=1))
            rows.append(jnp.concatenate(parts, axis=0))
        return jnp.concatenate(rows, axis=0)

    if forward:
        fresh = dinv_apply(base - lower)
    else:
        fresh = base - dinv_apply(lower)
    olds = cbuf[...]
    news = []
    for k in range(KL):
        news.append(jnp.where(T(1 + k) > 0, fresh[16 * k:16 * (k + 1)], olds[k]))
    new = jnp.concatenate(news, axis=0)
    cbuf[...] = new.reshape(KL, 16, SIDE**3)
    cp_o = pltpu.make_async_copy(cbuf, cur_out.at[pl.ds(win, KL)], sems.at[4])
    cp_o.start()

    faces = dot_exact01(new, gmat[...])
    flane = lax.broadcasted_iota(jnp.int32, (16, NF * FW), 1) // FW
    for k in range(KL):
        prod = dot_full(jbuf[k], faces[16 * k:16 * (k + 1)])
        inc = jnp.zeros((16, NF * FW), jnp.float32)
        for d in range(NF):
            inc = inc + jnp.where(flane == d, prod[16 * d:16 * (d + 1)], 0.0)
        sx[k] = inc[:, 0:128]
        sy[k] = inc[:, 128:256]
        zpart = pltpu.roll(inc[:, 256:384], 64, 1)
        tp = T(7 + k)
        tm = T(13 + k)

        @pl.when(tp >= 0)
        def _():
            sl = pl.ds(256, 128)
            accf[tp, :, sl] = accf[tp, :, sl] + jnp.where(low_half, 0.0, zpart)

        @pl.when(tm >= 0)
        def _():
            sl = pl.ds(256, 128)
            accf[tm, :, sl] = accf[tm, :, sl] + jnp.where(low_half, zpart, 0.0)

    cp_o.wait()


def run_level(forward, lev, tbl, accf, base, cur, dinv, jac, recv, gmat, smat):
    n_blocks = accf.shape[0]
    kern = functools.partial(level_kernel, forward)
    smem = pl.BlockSpec(memory_space=pltpu.SMEM)
    vmem = pl.BlockSpec(memory_space=pltpu.VMEM)
    anyspace = pl.BlockSpec(memory_space=pl.ANY)
    out_shape = (
        jax.ShapeDtypeStruct(accf.shape, jnp.float32),
        jax.ShapeDtypeStruct(cur.shape, jnp.float32),
        jax.ShapeDtypeStruct((KL, 16, 128), jnp.float32),
        jax.ShapeDtypeStruct((KL, 16, 128), jnp.float32),
    )
    return pl.pallas_call(
        kern,
        out_shape=out_shape,
        in_specs=[smem, smem, vmem, anyspace, anyspace, anyspace, anyspace,
                  vmem, vmem, vmem, vmem, vmem, vmem],
        out_specs=(vmem, anyspace, vmem, vmem),
        scratch_shapes=[
            pltpu.VMEM((KL,) + dinv.shape[1:], dinv.dtype),
            pltpu.VMEM((KL,) + jac.shape[1:], jnp.float32),
            pltpu.VMEM((KL,) + base.shape[1:], jnp.float32),
            pltpu.VMEM((KL,) + cur.shape[1:], jnp.float32),
            pltpu.SemaphoreType.DMA((5,)),
        ],
        input_output_aliases={2: 0, 4: 1},
        compiler_params=pltpu.CompilerParams(vmem_limit_bytes=48 * 1024 * 1024),
    )(lev, tbl, accf, base, cur, dinv, jac, *recv, gmat, smat)


def shift_along(value, axis, steps):
    count = lax.axis_size(axis)
    pairs = [(source, (source + steps) % count) for source in range(count)]
    return lax.ppermute(value, axis, pairs)


def exchange(sx, sy):
    return (
        shift_along(sx, "gx", 1),
        shift_along(sx, "gx", -1),
        shift_along(sy, "gy", 1),
        shift_along(sy, "gy", -1),
    )


def pick(vec, idx):
    ids = jnp.arange(vec.shape[0], dtype=jnp.int32)
    return jnp.sum(jnp.where(idx[..., None] == ids, vec, 0), axis=-1)


def pick_row(mat, row):
    ids = jnp.arange(mat.shape[0], dtype=jnp.int32)
    return jnp.sum(jnp.where(ids[:, None] == row, mat, 0), axis=0)


def build_tables(level_counts, slot_count, forward):
    count_x = lax.axis_size("gx")
    count_y = lax.axis_size("gy")
    place_x = lax.axis_index("gx")
    place_y = lax.axis_index("gy")
    coords, where_slot = slot_layout(count_x, count_y, RX, RY, NBZ)
    nbs = [jnp.asarray(step_table(coords, where_slot, dm, st)) for dm, st in DIRECTION_MOVES]
    ends_all = jnp.cumsum(level_counts, axis=1)
    begins_all = ends_all - level_counts
    slots = jnp.arange(slot_count, dtype=jnp.int32)
    all_levels = jnp.sum(slots[None, :, None] >= ends_all[:, None, :], axis=2).astype(jnp.int32)
    own_row = place_x * count_y + place_y
    source_rows = [
        (place_x - 1) % count_x * count_y + place_y,
        (place_x + 1) % count_x * count_y + place_y,
        place_x * count_y + (place_y - 1) % count_y,
        place_x * count_y + (place_y + 1) % count_y,
    ]
    at_edge = [place_x == 0, place_x == count_x - 1, place_y == 0, place_y == count_y - 1]
    my_lv = pick_row(all_levels, own_row)
    levels = jnp.arange(LEVELS, dtype=jnp.int32)
    offsets = jnp.arange(KL, dtype=jnp.int32)

    def ordered(target_level, now):
        return target_level > now if forward else target_level < now

    def window(row, now):
        begin = pick(pick_row(begins_all, row), jnp.clip(now, 0, LEVELS - 1))
        return jnp.clip(begin, 0, slot_count - KL)

    win = window(own_row, levels)
    wslots = win[:, None] + offsets[None, :]
    act = pick(my_lv, wslots) == levels[:, None]
    cols = [win[:, None], act.astype(jnp.int32)]
    for d in (4, 5):
        tgt = pick(nbs[d], wslots)
        ok = (tgt >= 0) & ordered(pick(my_lv, tgt), levels[:, None]) & act
        cols.append(jnp.where(ok, tgt, -1))
    sender_levels = levels - 1 if forward else levels + 1
    for d in range(4):
        row = source_rows[d]
        swin = window(row, sender_levels)
        sslots = swin[:, None] + offsets[None, :]
        s_act = pick(pick_row(all_levels, row), sslots) == sender_levels[:, None]
        tgt = jnp.where(at_edge[d], pick(nbs[d], sslots), sslots)
        ok = (tgt >= 0) & ordered(pick(my_lv, tgt), sender_levels[:, None]) & s_act
        cols.append(jnp.where(ok, tgt, -1))
    table = jnp.concatenate(cols, axis=1).astype(jnp.int32)
    return jnp.pad(table, ((0, 0), (0, TW - table.shape[1])), constant_values=-1)


def body(right_side, diag_inverse, face_jac, level_counts):
    slot_count = right_side.shape[0]
    unknowns = right_side.shape[1]
    gather_np, scatter_np = face_matrices(SIDE)
    gmat = jnp.asarray(gather_np, dtype=jnp.bfloat16)
    smat = jnp.asarray(scatter_np, dtype=jnp.bfloat16)
    jac = jnp.transpose(face_jac, (3, 0, 1, 2)).reshape(slot_count, NF * unknowns, unknowns)
    tbl_f = build_tables(level_counts, slot_count, True)
    tbl_b = build_tables(level_counts, slot_count, False)
    zero_recv = tuple(jnp.zeros((KL, 16, 128), jnp.float32) for _ in range(4))

    def lev_arr(v):
        return jnp.reshape(jnp.asarray(v, jnp.int32), (1,))

    accf = jnp.zeros((slot_count, unknowns, NF * FW), jnp.float32)
    cur = jnp.zeros(right_side.shape, jnp.float32)
    accf, cur, sx, sy = run_level(True, lev_arr(0), tbl_f, accf, right_side, cur, diag_inverse,
                                  jac, zero_recv, gmat, smat)

    def fwd(l, carry):
        accf, cur, sx, sy = carry
        recv = exchange(sx, sy)
        return run_level(True, lev_arr(l), tbl_f, accf, right_side, cur, diag_inverse, jac,
                         recv, gmat, smat)

    accf, half, sx, sy = lax.fori_loop(1, LEVELS, fwd, (accf, cur, sx, sy))

    accf = jnp.zeros((slot_count, unknowns, NF * FW), jnp.float32)
    accf, cur, sx, sy = run_level(False, lev_arr(LEVELS - 1), tbl_b, accf, half, half,
                                  diag_inverse, jac, zero_recv, gmat, smat)

    def bwd(i, carry):
        accf, cur, sx, sy = carry
        recv = exchange(sx, sy)
        return run_level(False, lev_arr(LEVELS - 2 - i), tbl_b, accf, half, cur, diag_inverse,
                         jac, recv, gmat, smat)

    accf, result, sx, sy = lax.fori_loop(0, LEVELS - 1, bwd, (accf, cur, sx, sy))
    return result


def solution(mesh):
    return jax.shard_map(
        body,
        mesh=mesh,
        in_specs=(
            P(("gx", "gy"), None, None),
            P(("gx", "gy"), None, None, None),
            P(None, None, None, ("gx", "gy")),
            P(),
        ),
        out_specs=P(("gx", "gy"), None, None),
        check_vma=False,
    )
```

```python
import functools

import jax
import jax.numpy as jnp
import numpy as np
from jax import lax
from jax.experimental import pallas as pl
from jax.experimental.pallas import tpu as pltpu
from jax.sharding import PartitionSpec as P

SIDE = 8
LEVELS = 12
RX = 2
RY = 2
NBZ = 8
KL = 6
NF = 6
FW = SIDE * SIDE
TW = 48

OPPOSITE = (1, 0, 3, 2, 5, 4)
DIRECTION_MOVES = ((0, 1), (0, -1), (1, 1), (1, -1), (2, 1), (2, -1))


def slot_layout(step_x, step_y, count_x, count_y, count_z):
    ordering = sorted(
        (
            (step_x * along_x + step_y * along_y + along_z, along_x, along_y, along_z)
            for along_x in range(count_x)
            for along_y in range(count_y)
            for along_z in range(count_z)
        )
    )
    coords = np.array([record[1:] for record in ordering], dtype=np.int64)
    where_slot = np.zeros((count_x, count_y, count_z), dtype=np.int64)
    where_slot[coords[:, 0], coords[:, 1], coords[:, 2]] = np.arange(len(ordering))
    return (coords, where_slot)


def step_table(coords, where_slot, dimension, offset_step):
    moved = coords.copy()
    moved[:, dimension] += offset_step
    bound_size = where_slot.shape[dimension]
    inside = (moved[:, dimension] >= 0) & (moved[:, dimension] < bound_size)
    clipped = np.clip(moved, 0, np.array(where_slot.shape) - 1)
    target = where_slot[clipped[:, 0], clipped[:, 1], clipped[:, 2]]
    return np.where(inside, target, -1).astype(np.int32)


def face_matrices(edge_cells):
    cell_ids = np.arange(edge_cells**3).reshape(edge_cells, edge_cells, edge_cells)
    layers = [
        cell_ids[edge_cells - 1],
        cell_ids[0],
        cell_ids[:, edge_cells - 1],
        cell_ids[:, 0],
        cell_ids[:, :, edge_cells - 1],
        cell_ids[:, :, 0],
    ]
    outward = np.stack([layer_ids.reshape(-1) for layer_ids in layers])
    cell_total = edge_cells**3
    face_width = edge_cells * edge_cells
    gather = np.zeros((cell_total, NF * face_width), dtype=np.float32)
    for face_index in range(NF):
        gather[outward[face_index], face_index * face_width + np.arange(face_width)] = 1.0
    return gather, np.ascontiguousarray(gather.T)


def split3(x):
    hi = x.astype(jnp.bfloat16)
    rest = x - hi.astype(jnp.float32)
    mid = rest.astype(jnp.bfloat16)
    low = (rest - mid.astype(jnp.float32)).astype(jnp.bfloat16)
    return hi, mid, low


def mm(a, b):
    return jnp.dot(a, b, preferred_element_type=jnp.float32)


def dot_exact01(x, table):
    hi, mid, low = split3(x)
    return mm(hi, table) + mm(mid, table) + mm(low, table)


def split2(x):
    hi = x.astype(jnp.bfloat16)
    return hi, (x - hi.astype(jnp.float32)).astype(jnp.bfloat16)


def dot_full(a, b):
    ah, al = split2(a)
    bh, bl = split2(b)
    return mm(ah, bh) + (mm(ah, bl) + mm(al, bh))


def level_kernel(forward, lev_ref, tbl_ref, accf_in, base_hbm, cur_hbm, dinv_hbm, jac_hbm,
                 rxp, rxm, ryp, rym, gmat, smat,
                 accf_out, cur_out, sx, sy,
                 accf, dbuf, jbuf, bbuf, cbuf, sems, dsems):
    lvl = lev_ref[0]

    def T(j):
        return tbl_ref[lvl, j]

    win = T(0)
    cp_a = pltpu.make_async_copy(accf_in, accf, sems.at[0])
    cp_a.start()
    cp_d = [pltpu.make_async_copy(dinv_hbm.at[win + k], dbuf.at[k], dsems.at[k])
            for k in range(KL)]
    cp_j = pltpu.make_async_copy(jac_hbm.at[pl.ds(win, KL)], jbuf, sems.at[1])
    cp_b = pltpu.make_async_copy(base_hbm.at[pl.ds(win, KL)], bbuf, sems.at[2])
    cp_c = pltpu.make_async_copy(cur_hbm.at[pl.ds(win, KL)], cbuf, sems.at[3])
    for cp in cp_d:
        cp.start()
    cp_j.start()
    cp_b.start()
    cp_c.start()

    cp_a.wait()
    lane = lax.broadcasted_iota(jnp.int32, (16, 128), 1)
    low_half = lane < 64

    for src, off, chunk, keep_low in ((rxp, 19, 0, False), (rxm, 25, 0, True),
                                      (ryp, 31, 1, False), (rym, 37, 1, True)):
        for k in range(KL):
            t = T(off + k)

            @pl.when(t >= 0)
            def _():
                moved = pltpu.roll(src[k], 64, 1)
                keep = low_half if keep_low else jnp.logical_not(low_half)
                sl = pl.ds(chunk * 128, 128)
                accf[t, :, sl] = accf[t, :, sl] + jnp.where(keep, moved, 0.0)

    cp_j.wait()
    cp_b.wait()
    cp_c.wait()

    nr = KL * 16
    acc_win = accf[pl.ds(win, KL)].reshape(nr, NF * FW)
    lower = dot_exact01(acc_win, smat[...])
    base = bbuf[...].reshape(nr, SIDE**3)

    def dinv_apply(v):
        rows = []
        for k in range(KL):
            vk = v[16 * k:16 * (k + 1)]
            parts = []
            cp_d[k].wait()
            for c0 in range(0, 16, 4):
                d = dbuf[k, c0:c0 + 4].astype(jnp.float32)
                parts.append(jnp.sum(d * vk[None], axis=1))
            rows.append(jnp.concatenate(parts, axis=0))
        return jnp.concatenate(rows, axis=0)

    if forward:
        fresh = dinv_apply(base - lower)
    else:
        fresh = base - dinv_apply(lower)
    olds = cbuf[...]
    news = []
    for k in range(KL):
        news.append(jnp.where(T(1 + k) > 0, fresh[16 * k:16 * (k + 1)], olds[k]))
    new = jnp.concatenate(news, axis=0)
    cbuf[...] = new.reshape(KL, 16, SIDE**3)
    cp_o = pltpu.make_async_copy(cbuf, cur_out.at[pl.ds(win, KL)], sems.at[4])
    cp_o.start()

    faces = dot_exact01(new, gmat[...])
    flane = lax.broadcasted_iota(jnp.int32, (16, NF * FW), 1) // FW
    for k in range(KL):
        prod = dot_full(jbuf[k], faces[16 * k:16 * (k + 1)])
        inc = jnp.zeros((16, NF * FW), jnp.float32)
        for d in range(NF):
            inc = inc + jnp.where(flane == d, prod[16 * d:16 * (d + 1)], 0.0)
        sx[k] = inc[:, 0:128]
        sy[k] = inc[:, 128:256]
        zpart = pltpu.roll(inc[:, 256:384], 64, 1)
        tp = T(7 + k)
        tm = T(13 + k)

        @pl.when(tp >= 0)
        def _():
            sl = pl.ds(256, 128)
            accf[tp, :, sl] = accf[tp, :, sl] + jnp.where(low_half, 0.0, zpart)

        @pl.when(tm >= 0)
        def _():
            sl = pl.ds(256, 128)
            accf[tm, :, sl] = accf[tm, :, sl] + jnp.where(low_half, zpart, 0.0)

    cp_w = pltpu.make_async_copy(accf, accf_out, sems.at[5])
    cp_w.start()
    cp_o.wait()
    cp_w.wait()


def run_level(forward, lev, tbl, accf, base, cur, dinv, jac, recv, gmat, smat):
    n_blocks = accf.shape[0]
    kern = functools.partial(level_kernel, forward)
    smem = pl.BlockSpec(memory_space=pltpu.SMEM)
    vmem = pl.BlockSpec(memory_space=pltpu.VMEM)
    anyspace = pl.BlockSpec(memory_space=pl.ANY)
    out_shape = (
        jax.ShapeDtypeStruct(accf.shape, jnp.float32),
        jax.ShapeDtypeStruct(cur.shape, jnp.float32),
        jax.ShapeDtypeStruct((KL, 16, 128), jnp.float32),
        jax.ShapeDtypeStruct((KL, 16, 128), jnp.float32),
    )
    return pl.pallas_call(
        kern,
        out_shape=out_shape,
        in_specs=[smem, smem, anyspace, anyspace, anyspace, anyspace, anyspace,
                  vmem, vmem, vmem, vmem, vmem, vmem],
        out_specs=(anyspace, anyspace, vmem, vmem),
        scratch_shapes=[
            pltpu.VMEM(accf.shape, jnp.float32),
            pltpu.VMEM((KL,) + dinv.shape[1:], dinv.dtype),
            pltpu.VMEM((KL,) + jac.shape[1:], jnp.float32),
            pltpu.VMEM((KL,) + base.shape[1:], jnp.float32),
            pltpu.VMEM((KL,) + cur.shape[1:], jnp.float32),
            pltpu.SemaphoreType.DMA((6,)),
            pltpu.SemaphoreType.DMA((KL,)),
        ],
        input_output_aliases={2: 0, 4: 1},
        compiler_params=pltpu.CompilerParams(vmem_limit_bytes=48 * 1024 * 1024),
    )(lev, tbl, accf, base, cur, dinv, jac, *recv, gmat, smat)


def shift_along(value, axis, steps):
    count = lax.axis_size(axis)
    pairs = [(source, (source + steps) % count) for source in range(count)]
    return lax.ppermute(value, axis, pairs)


def exchange(sx, sy):
    return (
        shift_along(sx, "gx", 1),
        shift_along(sx, "gx", -1),
        shift_along(sy, "gy", 1),
        shift_along(sy, "gy", -1),
    )


def pick(vec, idx):
    ids = jnp.arange(vec.shape[0], dtype=jnp.int32).reshape((-1,) + (1,) * idx.ndim)
    return jnp.sum(jnp.where(idx[None] == ids, vec.reshape(ids.shape), 0), axis=0)


def pick_row(mat, row):
    ids = jnp.arange(mat.shape[0], dtype=jnp.int32)
    return jnp.sum(jnp.where(ids[:, None] == row, mat, 0), axis=0)


def build_tables(level_counts, slot_count, forward):
    count_x = lax.axis_size("gx")
    count_y = lax.axis_size("gy")
    place_x = lax.axis_index("gx")
    place_y = lax.axis_index("gy")
    coords, where_slot = slot_layout(count_x, count_y, RX, RY, NBZ)
    nbs = [jnp.asarray(step_table(coords, where_slot, dm, st)) for dm, st in DIRECTION_MOVES]
    ends_all = jnp.cumsum(level_counts, axis=1)
    begins_all = ends_all - level_counts
    slots = jnp.arange(slot_count, dtype=jnp.int32)
    all_levels = jnp.sum(slots[None, :, None] >= ends_all[:, None, :], axis=2).astype(jnp.int32)
    own_row = place_x * count_y + place_y
    source_rows = [
        (place_x - 1) % count_x * count_y + place_y,
        (place_x + 1) % count_x * count_y + place_y,
        place_x * count_y + (place_y - 1) % count_y,
        place_x * count_y + (place_y + 1) % count_y,
    ]
    at_edge = [place_x == 0, place_x == count_x - 1, place_y == 0, place_y == count_y - 1]
    my_lv = pick_row(all_levels, own_row)
    levels = jnp.arange(LEVELS, dtype=jnp.int32)
    offsets = jnp.arange(KL, dtype=jnp.int32)

    def ordered(target_level, now):
        return target_level > now if forward else target_level < now

    def window(row, now):
        begin = pick(pick_row(begins_all, row), jnp.clip(now, 0, LEVELS - 1))
        return jnp.clip(begin, 0, slot_count - KL)

    win = window(own_row, levels)
    wslots = win[:, None] + offsets[None, :]
    act = pick(my_lv, wslots) == levels[:, None]
    cols = [win[:, None], act.astype(jnp.int32)]
    for d in (4, 5):
        tgt = pick(nbs[d], wslots)
        ok = (tgt >= 0) & ordered(pick(my_lv, tgt), levels[:, None]) & act
        cols.append(jnp.where(ok, tgt, -1))
    sender_levels = levels - 1 if forward else levels + 1
    for d in range(4):
        row = source_rows[d]
        swin = window(row, sender_levels)
        sslots = swin[:, None] + offsets[None, :]
        s_act = pick(pick_row(all_levels, row), sslots) == sender_levels[:, None]
        tgt = jnp.where(at_edge[d], pick(nbs[d], sslots), sslots)
        ok = (tgt >= 0) & ordered(pick(my_lv, tgt), sender_levels[:, None]) & s_act
        cols.append(jnp.where(ok, tgt, -1))
    table = jnp.concatenate(cols, axis=1).astype(jnp.int32)
    return jnp.pad(table, ((0, 0), (0, TW - table.shape[1])), constant_values=-1)


def body(right_side, diag_inverse, face_jac, level_counts):
    slot_count = right_side.shape[0]
    unknowns = right_side.shape[1]
    gather_np, scatter_np = face_matrices(SIDE)
    gmat = jnp.asarray(gather_np, dtype=jnp.bfloat16)
    smat = jnp.asarray(scatter_np, dtype=jnp.bfloat16)
    jac = jnp.transpose(face_jac, (3, 0, 1, 2)).reshape(slot_count, NF * unknowns, unknowns)
    tbl_f = build_tables(level_counts, slot_count, True)
    tbl_b = build_tables(level_counts, slot_count, False)
    zero_recv = tuple(jnp.zeros((KL, 16, 128), jnp.float32) for _ in range(4))

    def lev_arr(v):
        return jnp.reshape(jnp.asarray(v, jnp.int32), (1,))

    accf = jnp.zeros((slot_count, unknowns, NF * FW), jnp.float32)
    cur = jnp.zeros(right_side.shape, jnp.float32)
    accf, cur, sx, sy = run_level(True, lev_arr(0), tbl_f, accf, right_side, cur, diag_inverse,
                                  jac, zero_recv, gmat, smat)

    def fwd(l, carry):
        accf, cur, sx, sy = carry
        recv = exchange(sx, sy)
        return run_level(True, lev_arr(l), tbl_f, accf, right_side, cur, diag_inverse, jac,
                         recv, gmat, smat)

    accf, half, sx, sy = lax.fori_loop(1, LEVELS, fwd, (accf, cur, sx, sy))

    accf = jnp.zeros((slot_count, unknowns, NF * FW), jnp.float32)
    accf, cur, sx, sy = run_level(False, lev_arr(LEVELS - 1), tbl_b, accf, half, half,
                                  diag_inverse, jac, zero_recv, gmat, smat)

    def bwd(i, carry):
        accf, cur, sx, sy = carry
        recv = exchange(sx, sy)
        return run_level(False, lev_arr(LEVELS - 2 - i), tbl_b, accf, half, cur, diag_inverse,
                         jac, recv, gmat, smat)

    accf, result, sx, sy = lax.fori_loop(0, LEVELS - 1, bwd, (accf, cur, sx, sy))
    return result


def solution(mesh):
    return jax.shard_map(
        body,
        mesh=mesh,
        in_specs=(
            P(("gx", "gy"), None, None),
            P(("gx", "gy"), None, None, None),
            P(None, None, None, ("gx", "gy")),
            P(),
        ),
        out_specs=P(("gx", "gy"), None, None),
        check_vma=False,
    )
```

```python
import functools

import jax
import jax.numpy as jnp
import numpy as np
from jax import lax
from jax.experimental import pallas as pl
from jax.experimental.pallas import tpu as pltpu
from jax.sharding import PartitionSpec as P

SIDE = 8
LEVELS = 12
RX = 2
RY = 2
NBZ = 8
KL = 6
NF = 6
FW = SIDE * SIDE
TW = 48

OPPOSITE = (1, 0, 3, 2, 5, 4)
DIRECTION_MOVES = ((0, 1), (0, -1), (1, 1), (1, -1), (2, 1), (2, -1))


def slot_layout(step_x, step_y, count_x, count_y, count_z):
    ordering = sorted(
        (
            (step_x * along_x + step_y * along_y + along_z, along_x, along_y, along_z)
            for along_x in range(count_x)
            for along_y in range(count_y)
            for along_z in range(count_z)
        )
    )
    coords = np.array([record[1:] for record in ordering], dtype=np.int64)
    where_slot = np.zeros((count_x, count_y, count_z), dtype=np.int64)
    where_slot[coords[:, 0], coords[:, 1], coords[:, 2]] = np.arange(len(ordering))
    return (coords, where_slot)


def step_table(coords, where_slot, dimension, offset_step):
    moved = coords.copy()
    moved[:, dimension] += offset_step
    bound_size = where_slot.shape[dimension]
    inside = (moved[:, dimension] >= 0) & (moved[:, dimension] < bound_size)
    clipped = np.clip(moved, 0, np.array(where_slot.shape) - 1)
    target = where_slot[clipped[:, 0], clipped[:, 1], clipped[:, 2]]
    return np.where(inside, target, -1).astype(np.int32)


def face_matrices(edge_cells):
    cell_ids = np.arange(edge_cells**3).reshape(edge_cells, edge_cells, edge_cells)
    layers = [
        cell_ids[edge_cells - 1],
        cell_ids[0],
        cell_ids[:, edge_cells - 1],
        cell_ids[:, 0],
        cell_ids[:, :, edge_cells - 1],
        cell_ids[:, :, 0],
    ]
    outward = np.stack([layer_ids.reshape(-1) for layer_ids in layers])
    cell_total = edge_cells**3
    face_width = edge_cells * edge_cells
    gather = np.zeros((cell_total, NF * face_width), dtype=np.float32)
    for face_index in range(NF):
        gather[outward[face_index], face_index * face_width + np.arange(face_width)] = 1.0
    return gather, np.ascontiguousarray(gather.T)


def split3(x):
    hi = x.astype(jnp.bfloat16)
    rest = x - hi.astype(jnp.float32)
    mid = rest.astype(jnp.bfloat16)
    low = (rest - mid.astype(jnp.float32)).astype(jnp.bfloat16)
    return hi, mid, low


def mm(a, b):
    return jnp.dot(a, b, preferred_element_type=jnp.float32)


def dot_exact01(x, table):
    hi, mid, low = split3(x)
    return mm(hi, table) + mm(mid, table) + mm(low, table)


def split2(x):
    hi = x.astype(jnp.bfloat16)
    return hi, (x - hi.astype(jnp.float32)).astype(jnp.bfloat16)


def dot_full(a, b):
    ah, al = split2(a)
    bh, bl = split2(b)
    return mm(ah, bh) + (mm(ah, bl) + mm(al, bh))


def level_kernel(forward, lev_ref, tbl_ref, accf_in, base_hbm, cur_hbm, dinv_hbm, jac_hbm,
                 rxp, rxm, ryp, rym, gmat, smat,
                 accf_out, cur_out, sx, sy,
                 accf, dbuf, jbuf, bbuf, cbuf, sems, dsems):
    lvl = lev_ref[0]

    def T(j):
        return tbl_ref[lvl, j]

    win = T(0)
    cp_a = pltpu.make_async_copy(accf_in, accf, sems.at[0])
    cp_a.start()
    cp_d = [pltpu.make_async_copy(dinv_hbm.at[win + k], dbuf.at[k], dsems.at[k])
            for k in range(KL)]
    cp_j = pltpu.make_async_copy(jac_hbm.at[pl.ds(win, KL)], jbuf, sems.at[1])
    cp_b = pltpu.make_async_copy(base_hbm.at[pl.ds(win, KL)], bbuf, sems.at[2])
    cp_c = pltpu.make_async_copy(cur_hbm.at[pl.ds(win, KL)], cbuf, sems.at[3])
    for cp in cp_d:
        cp.start()
    cp_j.start()
    cp_b.start()
    cp_c.start()

    cp_a.wait()
    lane = lax.broadcasted_iota(jnp.int32, (16, 128), 1)
    low_half = lane < 64

    for src, off, chunk, keep_low in ((rxp, 19, 0, False), (rxm, 25, 0, True),
                                      (ryp, 31, 1, False), (rym, 37, 1, True)):
        for k in range(KL):
            t = T(off + k)

            @pl.when(t >= 0)
            def _():
                moved = pltpu.roll(src[k], 64, 1)
                keep = low_half if keep_low else jnp.logical_not(low_half)
                sl = pl.ds(chunk * 128, 128)
                accf[t, :, sl] = accf[t, :, sl] + jnp.where(keep, moved, 0.0)

    cp_j.wait()
    cp_b.wait()
    cp_c.wait()

    nr = KL * 16
    acc_win = accf[pl.ds(win, KL)].reshape(nr, NF * FW)
    lower = dot_exact01(acc_win, smat[...])
    base = bbuf[...].reshape(nr, SIDE**3)

    def dinv_apply(v):
        rows = []
        for k in range(KL):
            vk = v[16 * k:16 * (k + 1)]
            parts = []
            cp_d[k].wait()
            for c0 in range(0, 16, 4):
                d = dbuf[k, c0:c0 + 4].astype(jnp.float32)
                parts.append(jnp.sum(d * vk[None], axis=1))
            rows.append(jnp.concatenate(parts, axis=0))
        return jnp.concatenate(rows, axis=0)

    if forward:
        fresh = dinv_apply(base - lower)
    else:
        fresh = base - dinv_apply(lower)
    olds = cbuf[...]
    news = []
    for k in range(KL):
        news.append(jnp.where(T(1 + k) > 0, fresh[16 * k:16 * (k + 1)], olds[k]))
    new = jnp.concatenate(news, axis=0)
    cbuf[...] = new.reshape(KL, 16, SIDE**3)
    cp_o = pltpu.make_async_copy(cbuf, cur_out.at[pl.ds(win, KL)], sems.at[4])
    cp_o.start()

    faces = dot_exact01(new, gmat[...])
    flane = lax.broadcasted_iota(jnp.int32, (16, NF * FW), 1) // FW
    for k in range(KL):
        prod = dot_full(jbuf[k], faces[16 * k:16 * (k + 1)])
        inc = jnp.zeros((16, NF * FW), jnp.float32)
        for d in range(NF):
            inc = inc + jnp.where(flane == d, prod[16 * d:16 * (d + 1)], 0.0)
        sx[k] = inc[:, 0:128]
        sy[k] = inc[:, 128:256]
        zpart = pltpu.roll(inc[:, 256:384], 64, 1)
        tp = T(7 + k)
        tm = T(13 + k)

        @pl.when(tp >= 0)
        def _():
            sl = pl.ds(256, 128)
            accf[tp, :, sl] = accf[tp, :, sl] + jnp.where(low_half, 0.0, zpart)

        @pl.when(tm >= 0)
        def _():
            sl = pl.ds(256, 128)
            accf[tm, :, sl] = accf[tm, :, sl] + jnp.where(low_half, zpart, 0.0)

    cp_w = pltpu.make_async_copy(accf, accf_out, sems.at[5])
    cp_w.start()
    cp_o.wait()
    cp_w.wait()


def run_level(forward, lev, tbl, accf, base, cur, dinv, jac, recv, gmat, smat):
    n_blocks = accf.shape[0]
    kern = functools.partial(level_kernel, forward)
    smem = pl.BlockSpec(memory_space=pltpu.SMEM)
    vmem = pl.BlockSpec(memory_space=pltpu.VMEM)
    anyspace = pl.BlockSpec(memory_space=pl.ANY)
    out_shape = (
        jax.ShapeDtypeStruct(accf.shape, jnp.float32),
        jax.ShapeDtypeStruct(cur.shape, jnp.float32),
        jax.ShapeDtypeStruct((KL, 16, 128), jnp.float32),
        jax.ShapeDtypeStruct((KL, 16, 128), jnp.float32),
    )
    return pl.pallas_call(
        kern,
        out_shape=out_shape,
        in_specs=[smem, smem, anyspace, anyspace, anyspace, anyspace, anyspace,
                  vmem, vmem, vmem, vmem, vmem, vmem],
        out_specs=(anyspace, anyspace, vmem, vmem),
        scratch_shapes=[
            pltpu.VMEM(accf.shape, jnp.float32),
            pltpu.VMEM((KL,) + dinv.shape[1:], dinv.dtype),
            pltpu.VMEM((KL,) + jac.shape[1:], jnp.float32),
            pltpu.VMEM((KL,) + base.shape[1:], jnp.float32),
            pltpu.VMEM((KL,) + cur.shape[1:], jnp.float32),
            pltpu.SemaphoreType.DMA((6,)),
            pltpu.SemaphoreType.DMA((KL,)),
        ],
        input_output_aliases={2: 0, 4: 1},
        compiler_params=pltpu.CompilerParams(vmem_limit_bytes=48 * 1024 * 1024),
    )(lev, tbl, accf, base, cur, dinv, jac, *recv, gmat, smat)


def shift_along(value, axis, steps):
    count = lax.axis_size(axis)
    pairs = [(source, (source + steps) % count) for source in range(count)]
    return lax.ppermute(value, axis, pairs)


def exchange(sx, sy):
    return (
        shift_along(sx, "gx", 1),
        shift_along(sx, "gx", -1),
        shift_along(sy, "gy", 1),
        shift_along(sy, "gy", -1),
    )


def pick(vec, idx):
    ids = jnp.arange(vec.shape[0], dtype=jnp.int32)
    onehot = (idx[..., None] == ids).astype(jnp.float32)
    got = jnp.einsum("...n,n->...", onehot, vec.astype(jnp.float32),
                     precision=lax.Precision.HIGHEST)
    return jnp.round(got).astype(jnp.int32)


def pick_row(mat, row):
    ids = jnp.arange(mat.shape[0], dtype=jnp.int32)
    onehot = (ids == row).astype(jnp.float32)
    got = jnp.einsum("r,rn->n", onehot, mat.astype(jnp.float32),
                     precision=lax.Precision.HIGHEST)
    return jnp.round(got).astype(jnp.int32)


def build_tables(level_counts, slot_count, forward):
    count_x = lax.axis_size("gx")
    count_y = lax.axis_size("gy")
    place_x = lax.axis_index("gx")
    place_y = lax.axis_index("gy")
    coords, where_slot = slot_layout(count_x, count_y, RX, RY, NBZ)
    nbs = [jnp.asarray(step_table(coords, where_slot, dm, st)) for dm, st in DIRECTION_MOVES]
    ends_all = jnp.cumsum(level_counts, axis=1)
    begins_all = ends_all - level_counts
    slots = jnp.arange(slot_count, dtype=jnp.int32)
    all_levels = jnp.sum(slots[None, :, None] >= ends_all[:, None, :], axis=2).astype(jnp.int32)
    own_row = place_x * count_y + place_y
    source_rows = [
        (place_x - 1) % count_x * count_y + place_y,
        (place_x + 1) % count_x * count_y + place_y,
        place_x * count_y + (place_y - 1) % count_y,
        place_x * count_y + (place_y + 1) % count_y,
    ]
    at_edge = [place_x == 0, place_x == count_x - 1, place_y == 0, place_y == count_y - 1]
    my_lv = pick_row(all_levels, own_row)
    levels = jnp.arange(LEVELS, dtype=jnp.int32)
    offsets = jnp.arange(KL, dtype=jnp.int32)

    def ordered(target_level, now):
        return target_level > now if forward else target_level < now

    def window(row, now):
        begin = pick(pick_row(begins_all, row), jnp.clip(now, 0, LEVELS - 1))
        return jnp.clip(begin, 0, slot_count - KL)

    win = window(own_row, levels)
    wslots = win[:, None] + offsets[None, :]
    act = pick(my_lv, wslots) == levels[:, None]
    cols = [win[:, None], act.astype(jnp.int32)]
    for d in (4, 5):
        tgt = pick(nbs[d], wslots)
        ok = (tgt >= 0) & ordered(pick(my_lv, tgt), levels[:, None]) & act
        cols.append(jnp.where(ok, tgt, -1))
    sender_levels = levels - 1 if forward else levels + 1
    for d in range(4):
        row = source_rows[d]
        swin = window(row, sender_levels)
        sslots = swin[:, None] + offsets[None, :]
        s_act = pick(pick_row(all_levels, row), sslots) == sender_levels[:, None]
        tgt = jnp.where(at_edge[d], pick(nbs[d], sslots), sslots)
        ok = (tgt >= 0) & ordered(pick(my_lv, tgt), sender_levels[:, None]) & s_act
        cols.append(jnp.where(ok, tgt, -1))
    table = jnp.concatenate(cols, axis=1).astype(jnp.int32)
    return jnp.pad(table, ((0, 0), (0, TW - table.shape[1])), constant_values=-1)


def body(right_side, diag_inverse, face_jac, level_counts):
    slot_count = right_side.shape[0]
    unknowns = right_side.shape[1]
    gather_np, scatter_np = face_matrices(SIDE)
    gmat = jnp.asarray(gather_np, dtype=jnp.bfloat16)
    smat = jnp.asarray(scatter_np, dtype=jnp.bfloat16)
    jac = jnp.transpose(face_jac, (3, 0, 1, 2)).reshape(slot_count, NF * unknowns, unknowns)
    tbl_f = build_tables(level_counts, slot_count, True)
    tbl_b = build_tables(level_counts, slot_count, False)
    zero_recv = tuple(jnp.zeros((KL, 16, 128), jnp.float32) for _ in range(4))

    def lev_arr(v):
        return jnp.reshape(jnp.asarray(v, jnp.int32), (1,))

    accf = jnp.zeros((slot_count, unknowns, NF * FW), jnp.float32)
    cur = jnp.zeros(right_side.shape, jnp.float32)
    accf, cur, sx, sy = run_level(True, lev_arr(0), tbl_f, accf, right_side, cur, diag_inverse,
                                  jac, zero_recv, gmat, smat)

    def fwd(l, carry):
        accf, cur, sx, sy = carry
        recv = exchange(sx, sy)
        return run_level(True, lev_arr(l), tbl_f, accf, right_side, cur, diag_inverse, jac,
                         recv, gmat, smat)

    accf, half, sx, sy = lax.fori_loop(1, LEVELS, fwd, (accf, cur, sx, sy))

    accf = jnp.zeros((slot_count, unknowns, NF * FW), jnp.float32)
    accf, cur, sx, sy = run_level(False, lev_arr(LEVELS - 1), tbl_b, accf, half, half,
                                  diag_inverse, jac, zero_recv, gmat, smat)

    def bwd(i, carry):
        accf, cur, sx, sy = carry
        recv = exchange(sx, sy)
        return run_level(False, lev_arr(LEVELS - 2 - i), tbl_b, accf, half, cur, diag_inverse,
                         jac, recv, gmat, smat)

    accf, result, sx, sy = lax.fori_loop(0, LEVELS - 1, bwd, (accf, cur, sx, sy))
    return result


def solution(mesh):
    return jax.shard_map(
        body,
        mesh=mesh,
        in_specs=(
            P(("gx", "gy"), None, None),
            P(("gx", "gy"), None, None, None),
            P(None, None, None, ("gx", "gy")),
            P(),
        ),
        out_specs=P(("gx", "gy"), None, None),
        check_vma=False,
    )
```

```python
import functools

import jax
import jax.numpy as jnp
import numpy as np
from jax import lax
from jax.experimental import pallas as pl
from jax.experimental.pallas import tpu as pltpu
from jax.sharding import PartitionSpec as P

SIDE = 8
LEVELS = 12
RX = 2
RY = 2
NBZ = 8
KL = 6
NF = 6
FW = SIDE * SIDE
TW = 48

OPPOSITE = (1, 0, 3, 2, 5, 4)
DIRECTION_MOVES = ((0, 1), (0, -1), (1, 1), (1, -1), (2, 1), (2, -1))


def slot_layout(step_x, step_y, count_x, count_y, count_z):
    ordering = sorted(
        (
            (step_x * along_x + step_y * along_y + along_z, along_x, along_y, along_z)
            for along_x in range(count_x)
            for along_y in range(count_y)
            for along_z in range(count_z)
        )
    )
    coords = np.array([record[1:] for record in ordering], dtype=np.int64)
    where_slot = np.zeros((count_x, count_y, count_z), dtype=np.int64)
    where_slot[coords[:, 0], coords[:, 1], coords[:, 2]] = np.arange(len(ordering))
    return (coords, where_slot)


def step_table(coords, where_slot, dimension, offset_step):
    moved = coords.copy()
    moved[:, dimension] += offset_step
    bound_size = where_slot.shape[dimension]
    inside = (moved[:, dimension] >= 0) & (moved[:, dimension] < bound_size)
    clipped = np.clip(moved, 0, np.array(where_slot.shape) - 1)
    target = where_slot[clipped[:, 0], clipped[:, 1], clipped[:, 2]]
    return np.where(inside, target, -1).astype(np.int32)


def face_matrices(edge_cells):
    cell_ids = np.arange(edge_cells**3).reshape(edge_cells, edge_cells, edge_cells)
    layers = [
        cell_ids[edge_cells - 1],
        cell_ids[0],
        cell_ids[:, edge_cells - 1],
        cell_ids[:, 0],
        cell_ids[:, :, edge_cells - 1],
        cell_ids[:, :, 0],
    ]
    outward = np.stack([layer_ids.reshape(-1) for layer_ids in layers])
    cell_total = edge_cells**3
    face_width = edge_cells * edge_cells
    gather = np.zeros((cell_total, NF * face_width), dtype=np.float32)
    for face_index in range(NF):
        gather[outward[face_index], face_index * face_width + np.arange(face_width)] = 1.0
    return gather, np.ascontiguousarray(gather.T)


def split3(x):
    hi = x.astype(jnp.bfloat16)
    rest = x - hi.astype(jnp.float32)
    mid = rest.astype(jnp.bfloat16)
    low = (rest - mid.astype(jnp.float32)).astype(jnp.bfloat16)
    return hi, mid, low


def mm(a, b):
    return jnp.dot(a, b, preferred_element_type=jnp.float32)


def dot_exact01(x, table):
    hi, mid, low = split3(x)
    return mm(hi, table) + mm(mid, table) + mm(low, table)


def split2(x):
    hi = x.astype(jnp.bfloat16)
    return hi, (x - hi.astype(jnp.float32)).astype(jnp.bfloat16)


def dot_full(a, b):
    ah, al = split2(a)
    bh, bl = split2(b)
    return mm(ah, bh) + (mm(ah, bl) + mm(al, bh))


def level_kernel(forward, lev_ref, tbl_ref, accf_in, base_hbm, cur_hbm, dinv_hbm, jac_hbm,
                 rxp, rxm, ryp, rym, gmat, smat,
                 accf_out, cur_out, sx, sy,
                 accf, dbuf, jbuf, bbuf, cbuf, sems, dsems):
    lvl = lev_ref[0]

    def T(j):
        return tbl_ref[lvl, j]

    win = T(0)
    cp_a = pltpu.make_async_copy(accf_in, accf, sems.at[0])
    cp_a.start()
    cp_d = [pltpu.make_async_copy(dinv_hbm.at[win + k], dbuf.at[k], dsems.at[k])
            for k in range(KL)]
    cp_j = pltpu.make_async_copy(jac_hbm.at[pl.ds(win, KL)], jbuf, sems.at[1])
    cp_b = pltpu.make_async_copy(base_hbm.at[pl.ds(win, KL)], bbuf, sems.at[2])
    cp_c = pltpu.make_async_copy(cur_hbm.at[pl.ds(win, KL)], cbuf, sems.at[3])
    acts = [T(1 + k) > 0 for k in range(KL)]
    for k in range(KL):
        pl.when(acts[k])(cp_d[k].start)
    cp_j.start()
    cp_b.start()
    cp_c.start()

    cp_a.wait()
    lane = lax.broadcasted_iota(jnp.int32, (16, 128), 1)
    low_half = lane < 64

    for src, off, chunk, keep_low in ((rxp, 19, 0, False), (rxm, 25, 0, True),
                                      (ryp, 31, 1, False), (rym, 37, 1, True)):
        for k in range(KL):
            t = T(off + k)

            @pl.when(t >= 0)
            def _():
                moved = pltpu.roll(src[k], 64, 1)
                keep = low_half if keep_low else jnp.logical_not(low_half)
                sl = pl.ds(chunk * 128, 128)
                accf[t, :, sl] = accf[t, :, sl] + jnp.where(keep, moved, 0.0)

    cp_j.wait()
    cp_b.wait()
    cp_c.wait()

    nr = KL * 16
    acc_win = accf[pl.ds(win, KL)].reshape(nr, NF * FW)
    lower = dot_exact01(acc_win, smat[...])
    base = bbuf[...].reshape(nr, SIDE**3)

    for k in range(KL):

        @pl.when(acts[k])
        def _():
            cp_d[k].wait()
            bk = base[16 * k:16 * (k + 1)]
            lk = lower[16 * k:16 * (k + 1)]
            vk = bk - lk if forward else lk
            parts = []
            for c0 in range(0, 16, 4):
                d = dbuf[k, c0:c0 + 4].astype(jnp.float32)
                parts.append(jnp.sum(d * vk[None], axis=1))
            y = jnp.concatenate(parts, axis=0)
            cbuf[k] = y if forward else bk - y

    cp_o = pltpu.make_async_copy(cbuf, cur_out.at[pl.ds(win, KL)], sems.at[4])
    cp_o.start()
    new = cbuf[...].reshape(nr, SIDE**3)
    sx[...] = jnp.zeros(sx.shape, jnp.float32)
    sy[...] = jnp.zeros(sy.shape, jnp.float32)

    faces = dot_exact01(new, gmat[...])
    flane = lax.broadcasted_iota(jnp.int32, (16, NF * FW), 1) // FW
    for k in range(KL):

        @pl.when(acts[k])
        def _():
            prod = dot_full(jbuf[k], faces[16 * k:16 * (k + 1)])
            inc = jnp.zeros((16, NF * FW), jnp.float32)
            for d in range(NF):
                inc = inc + jnp.where(flane == d, prod[16 * d:16 * (d + 1)], 0.0)
            sx[k] = inc[:, 0:128]
            sy[k] = inc[:, 128:256]
            zpart = pltpu.roll(inc[:, 256:384], 64, 1)
            tp = T(7 + k)
            tm = T(13 + k)

            @pl.when(tp >= 0)
            def _():
                sl = pl.ds(256, 128)
                accf[tp, :, sl] = accf[tp, :, sl] + jnp.where(low_half, 0.0, zpart)

            @pl.when(tm >= 0)
            def _():
                sl = pl.ds(256, 128)
                accf[tm, :, sl] = accf[tm, :, sl] + jnp.where(low_half, zpart, 0.0)

    cp_w = pltpu.make_async_copy(accf, accf_out, sems.at[5])
    cp_w.start()
    cp_o.wait()
    cp_w.wait()


def run_level(forward, lev, tbl, accf, base, cur, dinv, jac, recv, gmat, smat):
    n_blocks = accf.shape[0]
    kern = functools.partial(level_kernel, forward)
    smem = pl.BlockSpec(memory_space=pltpu.SMEM)
    vmem = pl.BlockSpec(memory_space=pltpu.VMEM)
    anyspace = pl.BlockSpec(memory_space=pl.ANY)
    out_shape = (
        jax.ShapeDtypeStruct(accf.shape, jnp.float32),
        jax.ShapeDtypeStruct(cur.shape, jnp.float32),
        jax.ShapeDtypeStruct((KL, 16, 128), jnp.float32),
        jax.ShapeDtypeStruct((KL, 16, 128), jnp.float32),
    )
    return pl.pallas_call(
        kern,
        out_shape=out_shape,
        in_specs=[smem, smem, anyspace, anyspace, anyspace, anyspace, anyspace,
                  vmem, vmem, vmem, vmem, vmem, vmem],
        out_specs=(anyspace, anyspace, vmem, vmem),
        scratch_shapes=[
            pltpu.VMEM(accf.shape, jnp.float32),
            pltpu.VMEM((KL,) + dinv.shape[1:], dinv.dtype),
            pltpu.VMEM((KL,) + jac.shape[1:], jnp.float32),
            pltpu.VMEM((KL,) + base.shape[1:], jnp.float32),
            pltpu.VMEM((KL,) + cur.shape[1:], jnp.float32),
            pltpu.SemaphoreType.DMA((6,)),
            pltpu.SemaphoreType.DMA((KL,)),
        ],
        input_output_aliases={2: 0, 4: 1},
        compiler_params=pltpu.CompilerParams(vmem_limit_bytes=48 * 1024 * 1024),
    )(lev, tbl, accf, base, cur, dinv, jac, *recv, gmat, smat)


def shift_along(value, axis, steps):
    count = lax.axis_size(axis)
    pairs = [(source, (source + steps) % count) for source in range(count)]
    return lax.ppermute(value, axis, pairs)


def exchange(sx, sy):
    return (
        shift_along(sx, "gx", 1),
        shift_along(sx, "gx", -1),
        shift_along(sy, "gy", 1),
        shift_along(sy, "gy", -1),
    )


def pick(vec, idx):
    ids = jnp.arange(vec.shape[0], dtype=jnp.int32).reshape((-1,) + (1,) * idx.ndim)
    return jnp.sum(jnp.where(idx[None] == ids, vec.reshape(ids.shape), 0), axis=0)


def pick_row(mat, row):
    ids = jnp.arange(mat.shape[0], dtype=jnp.int32)
    return jnp.sum(jnp.where(ids[:, None] == row, mat, 0), axis=0)


def build_tables(level_counts, slot_count, forward):
    count_x = lax.axis_size("gx")
    count_y = lax.axis_size("gy")
    place_x = lax.axis_index("gx")
    place_y = lax.axis_index("gy")
    coords, where_slot = slot_layout(count_x, count_y, RX, RY, NBZ)
    nbs = [jnp.asarray(step_table(coords, where_slot, dm, st)) for dm, st in DIRECTION_MOVES]
    ends_all = jnp.cumsum(level_counts, axis=1)
    begins_all = ends_all - level_counts
    slots = jnp.arange(slot_count, dtype=jnp.int32)
    all_levels = jnp.sum(slots[None, :, None] >= ends_all[:, None, :], axis=2).astype(jnp.int32)
    own_row = place_x * count_y + place_y
    source_rows = [
        (place_x - 1) % count_x * count_y + place_y,
        (place_x + 1) % count_x * count_y + place_y,
        place_x * count_y + (place_y - 1) % count_y,
        place_x * count_y + (place_y + 1) % count_y,
    ]
    at_edge = [place_x == 0, place_x == count_x - 1, place_y == 0, place_y == count_y - 1]
    my_lv = pick_row(all_levels, own_row)
    levels = jnp.arange(LEVELS, dtype=jnp.int32)
    offsets = jnp.arange(KL, dtype=jnp.int32)

    def ordered(target_level, now):
        return target_level > now if forward else target_level < now

    def window(row, now):
        begin = pick(pick_row(begins_all, row), jnp.clip(now, 0, LEVELS - 1))
        return jnp.clip(begin, 0, slot_count - KL)

    win = window(own_row, levels)
    wslots = win[:, None] + offsets[None, :]
    act = pick(my_lv, wslots) == levels[:, None]
    cols = [win[:, None], act.astype(jnp.int32)]
    for d in (4, 5):
        tgt = pick(nbs[d], wslots)
        ok = (tgt >= 0) & ordered(pick(my_lv, tgt), levels[:, None]) & act
        cols.append(jnp.where(ok, tgt, -1))
    sender_levels = levels - 1 if forward else levels + 1
    for d in range(4):
        row = source_rows[d]
        swin = window(row, sender_levels)
        sslots = swin[:, None] + offsets[None, :]
        s_act = pick(pick_row(all_levels, row), sslots) == sender_levels[:, None]
        tgt = jnp.where(at_edge[d], pick(nbs[d], sslots), sslots)
        ok = (tgt >= 0) & ordered(pick(my_lv, tgt), sender_levels[:, None]) & s_act
        cols.append(jnp.where(ok, tgt, -1))
    table = jnp.concatenate(cols, axis=1).astype(jnp.int32)
    return jnp.pad(table, ((0, 0), (0, TW - table.shape[1])), constant_values=-1)


def body(right_side, diag_inverse, face_jac, level_counts):
    slot_count = right_side.shape[0]
    unknowns = right_side.shape[1]
    gather_np, scatter_np = face_matrices(SIDE)
    gmat = jnp.asarray(gather_np, dtype=jnp.bfloat16)
    smat = jnp.asarray(scatter_np, dtype=jnp.bfloat16)
    jac = jnp.transpose(face_jac, (3, 0, 1, 2)).reshape(slot_count, NF * unknowns, unknowns)
    tbl_f = build_tables(level_counts, slot_count, True)
    tbl_b = build_tables(level_counts, slot_count, False)
    zero_recv = tuple(jnp.zeros((KL, 16, 128), jnp.float32) for _ in range(4))

    def lev_arr(v):
        return jnp.reshape(jnp.asarray(v, jnp.int32), (1,))

    accf = jnp.zeros((slot_count, unknowns, NF * FW), jnp.float32)
    cur = jnp.zeros(right_side.shape, jnp.float32)
    accf, cur, sx, sy = run_level(True, lev_arr(0), tbl_f, accf, right_side, cur, diag_inverse,
                                  jac, zero_recv, gmat, smat)

    def fwd(l, carry):
        accf, cur, sx, sy = carry
        recv = exchange(sx, sy)
        return run_level(True, lev_arr(l), tbl_f, accf, right_side, cur, diag_inverse, jac,
                         recv, gmat, smat)

    accf, half, sx, sy = lax.fori_loop(1, LEVELS, fwd, (accf, cur, sx, sy))

    accf = jnp.zeros((slot_count, unknowns, NF * FW), jnp.float32)
    accf, cur, sx, sy = run_level(False, lev_arr(LEVELS - 1), tbl_b, accf, half, half,
                                  diag_inverse, jac, zero_recv, gmat, smat)

    def bwd(i, carry):
        accf, cur, sx, sy = carry
        recv = exchange(sx, sy)
        return run_level(False, lev_arr(LEVELS - 2 - i), tbl_b, accf, half, cur, diag_inverse,
                         jac, recv, gmat, smat)

    accf, result, sx, sy = lax.fori_loop(0, LEVELS - 1, bwd, (accf, cur, sx, sy))
    return result


def solution(mesh):
    return jax.shard_map(
        body,
        mesh=mesh,
        in_specs=(
            P(("gx", "gy"), None, None),
            P(("gx", "gy"), None, None, None),
            P(None, None, None, ("gx", "gy")),
            P(),
        ),
        out_specs=P(("gx", "gy"), None, None),
        check_vma=False,
    )
```

```python
import functools

import jax
import jax.numpy as jnp
import numpy as np
from jax import lax
from jax.experimental import pallas as pl
from jax.experimental.pallas import tpu as pltpu
from jax.sharding import PartitionSpec as P

SIDE = 8
LEVELS = 12
RX = 2
RY = 2
NBZ = 8
KL = 6
NF = 6
FW = SIDE * SIDE
TW = 48

OPPOSITE = (1, 0, 3, 2, 5, 4)
DIRECTION_MOVES = ((0, 1), (0, -1), (1, 1), (1, -1), (2, 1), (2, -1))


def slot_layout(step_x, step_y, count_x, count_y, count_z):
    ordering = sorted(
        (
            (step_x * along_x + step_y * along_y + along_z, along_x, along_y, along_z)
            for along_x in range(count_x)
            for along_y in range(count_y)
            for along_z in range(count_z)
        )
    )
    coords = np.array([record[1:] for record in ordering], dtype=np.int64)
    where_slot = np.zeros((count_x, count_y, count_z), dtype=np.int64)
    where_slot[coords[:, 0], coords[:, 1], coords[:, 2]] = np.arange(len(ordering))
    return (coords, where_slot)


def step_table(coords, where_slot, dimension, offset_step):
    moved = coords.copy()
    moved[:, dimension] += offset_step
    bound_size = where_slot.shape[dimension]
    inside = (moved[:, dimension] >= 0) & (moved[:, dimension] < bound_size)
    clipped = np.clip(moved, 0, np.array(where_slot.shape) - 1)
    target = where_slot[clipped[:, 0], clipped[:, 1], clipped[:, 2]]
    return np.where(inside, target, -1).astype(np.int32)


def face_matrices(edge_cells):
    cell_ids = np.arange(edge_cells**3).reshape(edge_cells, edge_cells, edge_cells)
    layers = [
        cell_ids[edge_cells - 1],
        cell_ids[0],
        cell_ids[:, edge_cells - 1],
        cell_ids[:, 0],
        cell_ids[:, :, edge_cells - 1],
        cell_ids[:, :, 0],
    ]
    outward = np.stack([layer_ids.reshape(-1) for layer_ids in layers])
    cell_total = edge_cells**3
    face_width = edge_cells * edge_cells
    gather = np.zeros((cell_total, NF * face_width), dtype=np.float32)
    for face_index in range(NF):
        gather[outward[face_index], face_index * face_width + np.arange(face_width)] = 1.0
    return gather, np.ascontiguousarray(gather.T)


def split3(x):
    hi = x.astype(jnp.bfloat16)
    rest = x - hi.astype(jnp.float32)
    mid = rest.astype(jnp.bfloat16)
    low = (rest - mid.astype(jnp.float32)).astype(jnp.bfloat16)
    return hi, mid, low


def mm(a, b):
    return jnp.dot(a, b, preferred_element_type=jnp.float32)


def dot_exact01(x, table):
    hi, mid, low = split3(x)
    return mm(hi, table) + mm(mid, table) + mm(low, table)


def split2(x):
    hi = x.astype(jnp.bfloat16)
    return hi, (x - hi.astype(jnp.float32)).astype(jnp.bfloat16)


def dot_full(a, b):
    ah, al = split2(a)
    bh, bl = split2(b)
    return mm(ah, bh) + (mm(ah, bl) + mm(al, bh))


def level_kernel(forward, lev_ref, tbl_ref, accf_in, base_hbm, cur_hbm, dinv_hbm, jac_hbm,
                 rxp, rxm, ryp, rym, gmat, smat,
                 accf_out, cur_out, sx, sy,
                 accf, dbuf, jbuf, bbuf, cbuf, sems, dsems):
    lvl = lev_ref[0]

    def T(j):
        return tbl_ref[lvl, j]

    win = T(0)
    cp_a = pltpu.make_async_copy(accf_in, accf, sems.at[0])
    cp_a.start()
    cp_d = [pltpu.make_async_copy(dinv_hbm.at[win + k], dbuf.at[k], dsems.at[k])
            for k in range(KL)]
    cp_j = pltpu.make_async_copy(jac_hbm.at[pl.ds(win, KL)], jbuf, sems.at[1])
    cp_b = pltpu.make_async_copy(base_hbm.at[pl.ds(win, KL)], bbuf, sems.at[2])
    cp_c = pltpu.make_async_copy(cur_hbm.at[pl.ds(win, KL)], cbuf, sems.at[3])
    acts = [T(1 + k) > 0 for k in range(KL)]
    for k in range(KL):
        pl.when(acts[k])(cp_d[k].start)
    cp_j.start()
    cp_b.start()
    cp_c.start()

    cp_a.wait()
    lane = lax.broadcasted_iota(jnp.int32, (16, 128), 1)
    low_half = lane < 64

    for src, off, chunk, keep_low in ((rxp, 19, 0, False), (rxm, 25, 0, True),
                                      (ryp, 31, 1, False), (rym, 37, 1, True)):
        for k in range(KL):
            t = T(off + k)

            @pl.when(t >= 0)
            def _():
                moved = pltpu.roll(src[k], 64, 1)
                keep = low_half if keep_low else jnp.logical_not(low_half)
                sl = pl.ds(chunk * 128, 128)
                accf[t, :, sl] = accf[t, :, sl] + jnp.where(keep, moved, 0.0)

    cp_j.wait()
    cp_b.wait()
    cp_c.wait()

    nr = KL * 16
    acc_win = accf[pl.ds(win, KL)].reshape(nr, NF * FW)
    lower = dot_exact01(acc_win, smat[...])
    base = bbuf[...].reshape(nr, SIDE**3)

    for k in range(KL):

        @pl.when(acts[k])
        def _():
            cp_d[k].wait()
            bk = base[16 * k:16 * (k + 1)]
            lk = lower[16 * k:16 * (k + 1)]
            vk = bk - lk if forward else lk
            parts = []
            for c0 in range(0, 16, 4):
                d = dbuf[k, c0:c0 + 4].astype(jnp.float32)
                parts.append(jnp.sum(d * vk[None], axis=1))
            y = jnp.concatenate(parts, axis=0)
            cbuf[k] = y if forward else bk - y

    cp_o = pltpu.make_async_copy(cbuf, cur_out.at[pl.ds(win, KL)], sems.at[4])
    cp_o.start()
    new = cbuf[...].reshape(nr, SIDE**3)
    sx[...] = jnp.zeros(sx.shape, jnp.float32)
    sy[...] = jnp.zeros(sy.shape, jnp.float32)

    faces = dot_exact01(new, gmat[...])
    flane = lax.broadcasted_iota(jnp.int32, (16, NF * FW), 1) // FW
    for k in range(KL):

        @pl.when(acts[k])
        def _():
            prod = dot_full(jbuf[k], faces[16 * k:16 * (k + 1)])
            inc = jnp.zeros((16, NF * FW), jnp.float32)
            for d in range(NF):
                inc = inc + jnp.where(flane == d, prod[16 * d:16 * (d + 1)], 0.0)
            sx[k] = inc[:, 0:128]
            sy[k] = inc[:, 128:256]
            zpart = pltpu.roll(inc[:, 256:384], 64, 1)
            tp = T(7 + k)
            tm = T(13 + k)

            @pl.when(tp >= 0)
            def _():
                sl = pl.ds(256, 128)
                accf[tp, :, sl] = accf[tp, :, sl] + jnp.where(low_half, 0.0, zpart)

            @pl.when(tm >= 0)
            def _():
                sl = pl.ds(256, 128)
                accf[tm, :, sl] = accf[tm, :, sl] + jnp.where(low_half, zpart, 0.0)

    cp_w = pltpu.make_async_copy(accf, accf_out, sems.at[5])
    cp_w.start()
    cp_o.wait()
    cp_w.wait()


def run_level(forward, lev, tbl, accf, base, cur, dinv, jac, recv, gmat, smat):
    n_blocks = accf.shape[0]
    kern = functools.partial(level_kernel, forward)
    smem = pl.BlockSpec(memory_space=pltpu.SMEM)
    vmem = pl.BlockSpec(memory_space=pltpu.VMEM)
    anyspace = pl.BlockSpec(memory_space=pl.ANY)
    out_shape = (
        jax.ShapeDtypeStruct(accf.shape, jnp.float32),
        jax.ShapeDtypeStruct(cur.shape, jnp.float32),
        jax.ShapeDtypeStruct((KL, 16, 128), jnp.float32),
        jax.ShapeDtypeStruct((KL, 16, 128), jnp.float32),
    )
    return pl.pallas_call(
        kern,
        out_shape=out_shape,
        in_specs=[smem, smem, anyspace, anyspace, anyspace, anyspace, anyspace,
                  vmem, vmem, vmem, vmem, vmem, vmem],
        out_specs=(anyspace, anyspace, vmem, vmem),
        scratch_shapes=[
            pltpu.VMEM(accf.shape, jnp.float32),
            pltpu.VMEM((KL,) + dinv.shape[1:], dinv.dtype),
            pltpu.VMEM((KL,) + jac.shape[1:], jnp.float32),
            pltpu.VMEM((KL,) + base.shape[1:], jnp.float32),
            pltpu.VMEM((KL,) + cur.shape[1:], jnp.float32),
            pltpu.SemaphoreType.DMA((6,)),
            pltpu.SemaphoreType.DMA((KL,)),
        ],
        input_output_aliases={2: 0, 4: 1},
        compiler_params=pltpu.CompilerParams(vmem_limit_bytes=48 * 1024 * 1024),
    )(lev, tbl, accf, base, cur, dinv, jac, *recv, gmat, smat)


def shift_along(value, axis, steps):
    count = lax.axis_size(axis)
    pairs = [(source, (source + steps) % count) for source in range(count)]
    return lax.ppermute(value, axis, pairs)


def exchange(sx, sy):
    return (
        shift_along(sx, "gx", 1),
        shift_along(sx, "gx", -1),
        shift_along(sy, "gy", 1),
        shift_along(sy, "gy", -1),
    )


def pick(vec, idx):
    ids = jnp.arange(vec.shape[0], dtype=jnp.int32).reshape((-1,) + (1,) * idx.ndim)
    return jnp.sum(jnp.where(idx[None] == ids, vec.reshape(ids.shape), 0), axis=0)


def pick_row(mat, row):
    ids = jnp.arange(mat.shape[0], dtype=jnp.int32)
    return jnp.sum(jnp.where(ids[:, None] == row, mat, 0), axis=0)


def build_tables(level_counts, slot_count, forward):
    count_x = lax.axis_size("gx")
    count_y = lax.axis_size("gy")
    place_x = lax.axis_index("gx")
    place_y = lax.axis_index("gy")
    coords, where_slot = slot_layout(count_x, count_y, RX, RY, NBZ)
    nbs = [jnp.asarray(step_table(coords, where_slot, dm, st)) for dm, st in DIRECTION_MOVES]
    ends_all = jnp.cumsum(level_counts, axis=1)
    begins_all = ends_all - level_counts
    slots = jnp.arange(slot_count, dtype=jnp.int32)
    all_levels = jnp.sum(slots[None, :, None] >= ends_all[:, None, :], axis=2).astype(jnp.int32)
    own_row = place_x * count_y + place_y
    source_rows = [
        (place_x - 1) % count_x * count_y + place_y,
        (place_x + 1) % count_x * count_y + place_y,
        place_x * count_y + (place_y - 1) % count_y,
        place_x * count_y + (place_y + 1) % count_y,
    ]
    at_edge = [place_x == 0, place_x == count_x - 1, place_y == 0, place_y == count_y - 1]
    my_lv = pick_row(all_levels, own_row)
    levels = jnp.arange(LEVELS, dtype=jnp.int32)
    offsets = jnp.arange(KL, dtype=jnp.int32)

    def ordered(target_level, now):
        return target_level > now if forward else target_level < now

    def window(row, now):
        begin = pick(pick_row(begins_all, row), jnp.clip(now, 0, LEVELS - 1))
        return jnp.clip(begin, 0, slot_count - KL)

    win = window(own_row, levels)
    wslots = win[:, None] + offsets[None, :]
    act = pick(my_lv, wslots) == levels[:, None]
    cols = [win[:, None], act.astype(jnp.int32)]
    for d in (4, 5):
        tgt = pick(nbs[d], wslots)
        ok = (tgt >= 0) & ordered(pick(my_lv, tgt), levels[:, None]) & act
        cols.append(jnp.where(ok, tgt, -1))
    sender_levels = levels - 1 if forward else levels + 1
    rows = jnp.stack(source_rows)
    row_hot = jnp.arange(all_levels.shape[0], dtype=jnp.int32)[None, :] == rows[:, None]
    src_begins = jnp.sum(jnp.where(row_hot[:, :, None], begins_all[None], 0), axis=1)
    src_levels = jnp.sum(jnp.where(row_hot[:, :, None], all_levels[None], 0), axis=1)
    lv_ids = jnp.arange(LEVELS, dtype=jnp.int32)
    lv_hot = lv_ids[None, :] == jnp.clip(sender_levels, 0, LEVELS - 1)[:, None]
    swin = jnp.sum(jnp.where(lv_hot[None], src_begins[:, None, :], 0), axis=2)
    swin = jnp.clip(swin, 0, slot_count - KL)
    sslots = swin[:, :, None] + offsets[None, None, :]
    slot_hot = sslots[..., None] == slots
    s_lv = jnp.sum(jnp.where(slot_hot, src_levels[:, None, None, :], 0), axis=3)
    s_act = s_lv == sender_levels[None, :, None]
    nb_remote = jnp.stack(nbs[:4])
    stepped = jnp.sum(jnp.where(slot_hot, nb_remote[:, None, None, :], 0), axis=3)
    tgt = jnp.where(jnp.stack(at_edge)[:, None, None], stepped, sslots)
    tgt_hot = tgt[..., None] == slots
    t_lv = jnp.sum(jnp.where(tgt_hot, my_lv[None, None, None, :], 0), axis=3)
    ok = (tgt >= 0) & ordered(t_lv, sender_levels[None, :, None]) & s_act
    remote = jnp.where(ok, tgt, -1)
    for d in range(4):
        cols.append(remote[d])
    table = jnp.concatenate(cols, axis=1).astype(jnp.int32)
    return jnp.pad(table, ((0, 0), (0, TW - table.shape[1])), constant_values=-1)


def body(right_side, diag_inverse, face_jac, level_counts):
    slot_count = right_side.shape[0]
    unknowns = right_side.shape[1]
    gather_np, scatter_np = face_matrices(SIDE)
    gmat = jnp.asarray(gather_np, dtype=jnp.bfloat16)
    smat = jnp.asarray(scatter_np, dtype=jnp.bfloat16)
    jac = jnp.transpose(face_jac, (3, 0, 1, 2)).reshape(slot_count, NF * unknowns, unknowns)
    tbl_f = build_tables(level_counts, slot_count, True)
    tbl_b = build_tables(level_counts, slot_count, False)
    zero_recv = tuple(jnp.zeros((KL, 16, 128), jnp.float32) for _ in range(4))

    def lev_arr(v):
        return jnp.reshape(jnp.asarray(v, jnp.int32), (1,))

    accf = jnp.zeros((slot_count, unknowns, NF * FW), jnp.float32)
    cur = jnp.zeros(right_side.shape, jnp.float32)
    accf, cur, sx, sy = run_level(True, lev_arr(0), tbl_f, accf, right_side, cur, diag_inverse,
                                  jac, zero_recv, gmat, smat)

    def fwd(l, carry):
        accf, cur, sx, sy = carry
        recv = exchange(sx, sy)
        return run_level(True, lev_arr(l), tbl_f, accf, right_side, cur, diag_inverse, jac,
                         recv, gmat, smat)

    accf, half, sx, sy = lax.fori_loop(1, LEVELS, fwd, (accf, cur, sx, sy))

    accf = jnp.zeros((slot_count, unknowns, NF * FW), jnp.float32)
    accf, cur, sx, sy = run_level(False, lev_arr(LEVELS - 1), tbl_b, accf, half, half,
                                  diag_inverse, jac, zero_recv, gmat, smat)

    def bwd(i, carry):
        accf, cur, sx, sy = carry
        recv = exchange(sx, sy)
        return run_level(False, lev_arr(LEVELS - 2 - i), tbl_b, accf, half, cur, diag_inverse,
                         jac, recv, gmat, smat)

    accf, result, sx, sy = lax.fori_loop(0, LEVELS - 1, bwd, (accf, cur, sx, sy))
    return result


def solution(mesh):
    return jax.shard_map(
        body,
        mesh=mesh,
        in_specs=(
            P(("gx", "gy"), None, None),
            P(("gx", "gy"), None, None, None),
            P(None, None, None, ("gx", "gy")),
            P(),
        ),
        out_specs=P(("gx", "gy"), None, None),
        check_vma=False,
    )
```

```python
import functools

import jax
import jax.numpy as jnp
import numpy as np
from jax import lax
from jax.experimental import pallas as pl
from jax.experimental.pallas import tpu as pltpu
from jax.sharding import PartitionSpec as P

SIDE = 8
LEVELS = 12
RX = 2
RY = 2
NBZ = 8
KL = 6
NF = 6
FW = SIDE * SIDE
TW = 48

OPPOSITE = (1, 0, 3, 2, 5, 4)
DIRECTION_MOVES = ((0, 1), (0, -1), (1, 1), (1, -1), (2, 1), (2, -1))


def slot_layout(step_x, step_y, count_x, count_y, count_z):
    ordering = sorted(
        (
            (step_x * along_x + step_y * along_y + along_z, along_x, along_y, along_z)
            for along_x in range(count_x)
            for along_y in range(count_y)
            for along_z in range(count_z)
        )
    )
    coords = np.array([record[1:] for record in ordering], dtype=np.int64)
    where_slot = np.zeros((count_x, count_y, count_z), dtype=np.int64)
    where_slot[coords[:, 0], coords[:, 1], coords[:, 2]] = np.arange(len(ordering))
    return (coords, where_slot)


def step_table(coords, where_slot, dimension, offset_step):
    moved = coords.copy()
    moved[:, dimension] += offset_step
    bound_size = where_slot.shape[dimension]
    inside = (moved[:, dimension] >= 0) & (moved[:, dimension] < bound_size)
    clipped = np.clip(moved, 0, np.array(where_slot.shape) - 1)
    target = where_slot[clipped[:, 0], clipped[:, 1], clipped[:, 2]]
    return np.where(inside, target, -1).astype(np.int32)


def face_matrices(edge_cells):
    cell_ids = np.arange(edge_cells**3).reshape(edge_cells, edge_cells, edge_cells)
    layers = [
        cell_ids[edge_cells - 1],
        cell_ids[0],
        cell_ids[:, edge_cells - 1],
        cell_ids[:, 0],
        cell_ids[:, :, edge_cells - 1],
        cell_ids[:, :, 0],
    ]
    outward = np.stack([layer_ids.reshape(-1) for layer_ids in layers])
    cell_total = edge_cells**3
    face_width = edge_cells * edge_cells
    gather = np.zeros((cell_total, NF * face_width), dtype=np.float32)
    for face_index in range(NF):
        gather[outward[face_index], face_index * face_width + np.arange(face_width)] = 1.0
    return gather, np.ascontiguousarray(gather.T)


def split3(x):
    hi = x.astype(jnp.bfloat16)
    rest = x - hi.astype(jnp.float32)
    mid = rest.astype(jnp.bfloat16)
    low = (rest - mid.astype(jnp.float32)).astype(jnp.bfloat16)
    return hi, mid, low


def mm(a, b):
    return jnp.dot(a, b, preferred_element_type=jnp.float32)


def dot_exact01(x, table):
    hi, mid, low = split3(x)
    return mm(hi, table) + mm(mid, table) + mm(low, table)


def split2(x):
    hi = x.astype(jnp.bfloat16)
    return hi, (x - hi.astype(jnp.float32)).astype(jnp.bfloat16)


def dot_full(a, b):
    ah, al = split2(a)
    bh, bl = split2(b)
    return mm(ah, bh) + (mm(ah, bl) + mm(al, bh))


def level_kernel(forward, lev_ref, tbl_ref, accf_in, base_hbm, cur_hbm, dinv_hbm, jac_hbm,
                 rxp, rxm, ryp, rym, gmat, smat,
                 accf_out, cur_out, sx, sy,
                 accf, dbuf, jbuf, bbuf, cbuf, sems, dsems):
    lvl = lev_ref[0]

    def T(j):
        return tbl_ref[lvl, j]

    win = T(0)
    cp_a = pltpu.make_async_copy(accf_in, accf, sems.at[0])
    cp_a.start()
    cp_d = [pltpu.make_async_copy(dinv_hbm.at[win + k], dbuf.at[k], dsems.at[k])
            for k in range(KL)]
    cp_j = pltpu.make_async_copy(jac_hbm.at[pl.ds(win, KL)], jbuf, sems.at[1])
    cp_b = pltpu.make_async_copy(base_hbm.at[pl.ds(win, KL)], bbuf, sems.at[2])
    cp_c = pltpu.make_async_copy(cur_hbm.at[pl.ds(win, KL)], cbuf, sems.at[3])
    acts = [T(1 + k) > 0 for k in range(KL)]
    for k in range(KL):
        pl.when(acts[k])(cp_d[k].start)
    cp_j.start()
    cp_b.start()
    cp_c.start()

    cp_a.wait()
    lane = lax.broadcasted_iota(jnp.int32, (16, 128), 1)
    low_half = lane < 64

    for src, off, chunk, keep_low in ((rxp, 19, 0, False), (rxm, 25, 0, True),
                                      (ryp, 31, 1, False), (rym, 37, 1, True)):
        for k in range(KL):
            t = T(off + k)

            @pl.when(t >= 0)
            def _():
                moved = pltpu.roll(src[k], 64, 1)
                keep = low_half if keep_low else jnp.logical_not(low_half)
                sl = pl.ds(chunk * 128, 128)
                accf[t, :, sl] = accf[t, :, sl] + jnp.where(keep, moved, 0.0)

    cp_j.wait()
    cp_b.wait()
    cp_c.wait()

    nr = KL * 16
    acc_win = accf[pl.ds(win, KL)].reshape(nr, NF * FW)
    lower = dot_exact01(acc_win, smat[...])
    base = bbuf[...].reshape(nr, SIDE**3)

    for k in range(KL):

        @pl.when(acts[k])
        def _():
            cp_d[k].wait()
            bk = base[16 * k:16 * (k + 1)]
            lk = lower[16 * k:16 * (k + 1)]
            vk = bk - lk if forward else lk
            parts = []
            for c0 in range(0, 16, 4):
                d = dbuf[k, c0:c0 + 4].astype(jnp.float32)
                parts.append(jnp.sum(d * vk[None], axis=1))
            y = jnp.concatenate(parts, axis=0)
            cbuf[k] = y if forward else bk - y

    cp_o = pltpu.make_async_copy(cbuf, cur_out.at[pl.ds(win, KL)], sems.at[4])
    cp_o.start()
    new = cbuf[...].reshape(nr, SIDE**3)
    sx[...] = jnp.zeros(sx.shape, jnp.float32)
    sy[...] = jnp.zeros(sy.shape, jnp.float32)

    faces = dot_exact01(new, gmat[...])
    flane = lax.broadcasted_iota(jnp.int32, (16, NF * FW), 1) // FW
    for k in range(KL):

        @pl.when(acts[k])
        def _():
            prod = dot_full(jbuf[k], faces[16 * k:16 * (k + 1)])
            inc = jnp.zeros((16, NF * FW), jnp.float32)
            for d in range(NF):
                inc = inc + jnp.where(flane == d, prod[16 * d:16 * (d + 1)], 0.0)
            sx[k] = inc[:, 0:128]
            sy[k] = inc[:, 128:256]
            zpart = pltpu.roll(inc[:, 256:384], 64, 1)
            tp = T(7 + k)
            tm = T(13 + k)

            @pl.when(tp >= 0)
            def _():
                sl = pl.ds(256, 128)
                accf[tp, :, sl] = accf[tp, :, sl] + jnp.where(low_half, 0.0, zpart)

            @pl.when(tm >= 0)
            def _():
                sl = pl.ds(256, 128)
                accf[tm, :, sl] = accf[tm, :, sl] + jnp.where(low_half, zpart, 0.0)

    cp_w = pltpu.make_async_copy(accf, accf_out, sems.at[5])
    cp_w.start()
    cp_o.wait()
    cp_w.wait()


def run_level(forward, lev, tbl, accf, base, cur, dinv, jac, recv, gmat, smat):
    n_blocks = accf.shape[0]
    kern = functools.partial(level_kernel, forward)
    smem = pl.BlockSpec(memory_space=pltpu.SMEM)
    vmem = pl.BlockSpec(memory_space=pltpu.VMEM)
    anyspace = pl.BlockSpec(memory_space=pl.ANY)
    out_shape = (
        jax.ShapeDtypeStruct(accf.shape, jnp.float32),
        jax.ShapeDtypeStruct(cur.shape, jnp.float32),
        jax.ShapeDtypeStruct((KL, 16, 128), jnp.float32),
        jax.ShapeDtypeStruct((KL, 16, 128), jnp.float32),
    )
    return pl.pallas_call(
        kern,
        out_shape=out_shape,
        in_specs=[smem, smem, anyspace, anyspace, anyspace, anyspace, anyspace,
                  vmem, vmem, vmem, vmem, vmem, vmem],
        out_specs=(anyspace, anyspace, vmem, vmem),
        scratch_shapes=[
            pltpu.VMEM(accf.shape, jnp.float32),
            pltpu.VMEM((KL,) + dinv.shape[1:], dinv.dtype),
            pltpu.VMEM((KL,) + jac.shape[1:], jnp.float32),
            pltpu.VMEM((KL,) + base.shape[1:], jnp.float32),
            pltpu.VMEM((KL,) + cur.shape[1:], jnp.float32),
            pltpu.SemaphoreType.DMA((6,)),
            pltpu.SemaphoreType.DMA((KL,)),
        ],
        input_output_aliases={2: 0, 4: 1},
        compiler_params=pltpu.CompilerParams(vmem_limit_bytes=48 * 1024 * 1024),
    )(lev, tbl, accf, base, cur, dinv, jac, *recv, gmat, smat)


def shift_along(value, axis, steps):
    count = lax.axis_size(axis)
    pairs = [(source, (source + steps) % count) for source in range(count)]
    return lax.ppermute(value, axis, pairs)


def exchange(sx, sy):
    return (
        shift_along(sx, "gx", 1),
        shift_along(sx, "gx", -1),
        shift_along(sy, "gy", 1),
        shift_along(sy, "gy", -1),
    )


def pick(vec, idx):
    ids = jnp.arange(vec.shape[0], dtype=jnp.int32).reshape((-1,) + (1,) * idx.ndim)
    return jnp.sum(jnp.where(idx[None] == ids, vec.reshape(ids.shape), 0), axis=0)


def pick_row(mat, row):
    ids = jnp.arange(mat.shape[0], dtype=jnp.int32)
    return jnp.sum(jnp.where(ids[:, None] == row, mat, 0), axis=0)


def build_tables(level_counts, slot_count, forward):
    count_x = lax.axis_size("gx")
    count_y = lax.axis_size("gy")
    place_x = lax.axis_index("gx")
    place_y = lax.axis_index("gy")
    coords, where_slot = slot_layout(count_x, count_y, RX, RY, NBZ)
    nbs = [jnp.asarray(step_table(coords, where_slot, dm, st)) for dm, st in DIRECTION_MOVES]
    ends_all = jnp.cumsum(level_counts, axis=1)
    begins_all = ends_all - level_counts
    slots = jnp.arange(slot_count, dtype=jnp.int32)
    own_row = place_x * count_y + place_y
    source_rows = [
        (place_x - 1) % count_x * count_y + place_y,
        (place_x + 1) % count_x * count_y + place_y,
        place_x * count_y + (place_y - 1) % count_y,
        place_x * count_y + (place_y + 1) % count_y,
    ]
    at_edge = [place_x == 0, place_x == count_x - 1, place_y == 0, place_y == count_y - 1]
    own_ends = pick_row(ends_all, own_row)

    def level_of(ends_row, slot):
        return jnp.sum((ends_row <= slot[..., None]).astype(jnp.int32), axis=-1)
    levels = jnp.arange(LEVELS, dtype=jnp.int32)
    offsets = jnp.arange(KL, dtype=jnp.int32)

    def ordered(target_level, now):
        return target_level > now if forward else target_level < now

    def window(row, now):
        begin = pick(pick_row(begins_all, row), jnp.clip(now, 0, LEVELS - 1))
        return jnp.clip(begin, 0, slot_count - KL)

    win = window(own_row, levels)
    wslots = win[:, None] + offsets[None, :]
    act = level_of(own_ends, wslots) == levels[:, None]
    cols = [win[:, None], act.astype(jnp.int32)]
    for d in (4, 5):
        tgt = pick(nbs[d], wslots)
        ok = (tgt >= 0) & ordered(level_of(own_ends, tgt), levels[:, None]) & act
        cols.append(jnp.where(ok, tgt, -1))
    sender_levels = levels - 1 if forward else levels + 1
    rows = jnp.stack(source_rows)
    row_hot = jnp.arange(ends_all.shape[0], dtype=jnp.int32)[None, :] == rows[:, None]
    src_begins = jnp.sum(jnp.where(row_hot[:, :, None], begins_all[None], 0), axis=1)
    src_ends = jnp.sum(jnp.where(row_hot[:, :, None], ends_all[None], 0), axis=1)
    lv_ids = jnp.arange(LEVELS, dtype=jnp.int32)
    lv_hot = lv_ids[None, :] == jnp.clip(sender_levels, 0, LEVELS - 1)[:, None]
    swin = jnp.sum(jnp.where(lv_hot[None], src_begins[:, None, :], 0), axis=2)
    swin = jnp.clip(swin, 0, slot_count - KL)
    sslots = swin[:, :, None] + offsets[None, None, :]
    slot_hot = sslots[..., None] == slots
    s_lv = jnp.sum((src_ends[:, None, None, :] <= sslots[..., None]).astype(jnp.int32), axis=3)
    s_act = s_lv == sender_levels[None, :, None]
    nb_remote = jnp.stack(nbs[:4])
    stepped = jnp.sum(jnp.where(slot_hot, nb_remote[:, None, None, :], 0), axis=3)
    tgt = jnp.where(jnp.stack(at_edge)[:, None, None], stepped, sslots)
    t_lv = level_of(own_ends, tgt)
    ok = (tgt >= 0) & ordered(t_lv, sender_levels[None, :, None]) & s_act
    remote = jnp.where(ok, tgt, -1)
    for d in range(4):
        cols.append(remote[d])
    table = jnp.concatenate(cols, axis=1).astype(jnp.int32)
    return jnp.pad(table, ((0, 0), (0, TW - table.shape[1])), constant_values=-1)


def body(right_side, diag_inverse, face_jac, level_counts):
    slot_count = right_side.shape[0]
    unknowns = right_side.shape[1]
    gather_np, scatter_np = face_matrices(SIDE)
    gmat = jnp.asarray(gather_np, dtype=jnp.bfloat16)
    smat = jnp.asarray(scatter_np, dtype=jnp.bfloat16)
    jac = jnp.transpose(face_jac, (3, 0, 1, 2)).reshape(slot_count, NF * unknowns, unknowns)
    tbl_f = build_tables(level_counts, slot_count, True)
    tbl_b = build_tables(level_counts, slot_count, False)
    zero_recv = tuple(jnp.zeros((KL, 16, 128), jnp.float32) for _ in range(4))

    def lev_arr(v):
        return jnp.reshape(jnp.asarray(v, jnp.int32), (1,))

    accf = jnp.zeros((slot_count, unknowns, NF * FW), jnp.float32)
    cur = jnp.zeros(right_side.shape, jnp.float32)
    accf, cur, sx, sy = run_level(True, lev_arr(0), tbl_f, accf, right_side, cur, diag_inverse,
                                  jac, zero_recv, gmat, smat)

    def fwd(l, carry):
        accf, cur, sx, sy = carry
        recv = exchange(sx, sy)
        return run_level(True, lev_arr(l), tbl_f, accf, right_side, cur, diag_inverse, jac,
                         recv, gmat, smat)

    accf, half, sx, sy = lax.fori_loop(1, LEVELS, fwd, (accf, cur, sx, sy))

    accf = jnp.zeros((slot_count, unknowns, NF * FW), jnp.float32)
    accf, cur, sx, sy = run_level(False, lev_arr(LEVELS - 1), tbl_b, accf, half, half,
                                  diag_inverse, jac, zero_recv, gmat, smat)

    def bwd(i, carry):
        accf, cur, sx, sy = carry
        recv = exchange(sx, sy)
        return run_level(False, lev_arr(LEVELS - 2 - i), tbl_b, accf, half, cur, diag_inverse,
                         jac, recv, gmat, smat)

    accf, result, sx, sy = lax.fori_loop(0, LEVELS - 1, bwd, (accf, cur, sx, sy))
    return result


def solution(mesh):
    return jax.shard_map(
        body,
        mesh=mesh,
        in_specs=(
            P(("gx", "gy"), None, None),
            P(("gx", "gy"), None, None, None),
            P(None, None, None, ("gx", "gy")),
            P(),
        ),
        out_specs=P(("gx", "gy"), None, None),
        check_vma=False,
    )
```

```python
import functools

import jax
import jax.numpy as jnp
import numpy as np
from jax import lax
from jax.experimental import pallas as pl
from jax.experimental.pallas import tpu as pltpu
from jax.sharding import PartitionSpec as P

SIDE = 8
LEVELS = 12
RX = 2
RY = 2
NBZ = 8
KL = 6
NF = 6
FW = SIDE * SIDE
TW = 48

OPPOSITE = (1, 0, 3, 2, 5, 4)
DIRECTION_MOVES = ((0, 1), (0, -1), (1, 1), (1, -1), (2, 1), (2, -1))


def slot_layout(step_x, step_y, count_x, count_y, count_z):
    ordering = sorted(
        (
            (step_x * along_x + step_y * along_y + along_z, along_x, along_y, along_z)
            for along_x in range(count_x)
            for along_y in range(count_y)
            for along_z in range(count_z)
        )
    )
    coords = np.array([record[1:] for record in ordering], dtype=np.int64)
    where_slot = np.zeros((count_x, count_y, count_z), dtype=np.int64)
    where_slot[coords[:, 0], coords[:, 1], coords[:, 2]] = np.arange(len(ordering))
    return (coords, where_slot)


def step_table(coords, where_slot, dimension, offset_step):
    moved = coords.copy()
    moved[:, dimension] += offset_step
    bound_size = where_slot.shape[dimension]
    inside = (moved[:, dimension] >= 0) & (moved[:, dimension] < bound_size)
    clipped = np.clip(moved, 0, np.array(where_slot.shape) - 1)
    target = where_slot[clipped[:, 0], clipped[:, 1], clipped[:, 2]]
    return np.where(inside, target, -1).astype(np.int32)


def face_matrices(edge_cells):
    cell_ids = np.arange(edge_cells**3).reshape(edge_cells, edge_cells, edge_cells)
    layers = [
        cell_ids[edge_cells - 1],
        cell_ids[0],
        cell_ids[:, edge_cells - 1],
        cell_ids[:, 0],
        cell_ids[:, :, edge_cells - 1],
        cell_ids[:, :, 0],
    ]
    outward = np.stack([layer_ids.reshape(-1) for layer_ids in layers])
    cell_total = edge_cells**3
    face_width = edge_cells * edge_cells
    gather = np.zeros((cell_total, NF * face_width), dtype=np.float32)
    for face_index in range(NF):
        gather[outward[face_index], face_index * face_width + np.arange(face_width)] = 1.0
    return gather, np.ascontiguousarray(gather.T)


def split3(x):
    hi = x.astype(jnp.bfloat16)
    rest = x - hi.astype(jnp.float32)
    mid = rest.astype(jnp.bfloat16)
    low = (rest - mid.astype(jnp.float32)).astype(jnp.bfloat16)
    return hi, mid, low


def mm(a, b):
    return jnp.dot(a, b, preferred_element_type=jnp.float32)


def dot_exact01(x, table):
    hi, mid, low = split3(x)
    return mm(hi, table) + mm(mid, table) + mm(low, table)


def split2(x):
    hi = x.astype(jnp.bfloat16)
    return hi, (x - hi.astype(jnp.float32)).astype(jnp.bfloat16)


def dot_full(a, b):
    ah, al = split2(a)
    bh, bl = split2(b)
    return mm(ah, bh) + (mm(ah, bl) + mm(al, bh))


def level_kernel(forward, lev_ref, tbl_ref, accf_in, base_hbm, cur_hbm, dinv_hbm, jac_hbm,
                 rxp, rxm, ryp, rym, gmat, smat,
                 accf_out, cur_out, sx, sy,
                 accf, dbuf, jbuf, bbuf, cbuf, sems, dsems):
    lvl = lev_ref[0]

    def T(j):
        return tbl_ref[lvl, j]

    win = T(0)
    cp_a = pltpu.make_async_copy(accf_in, accf, sems.at[0])
    cp_a.start()
    cp_d = [pltpu.make_async_copy(dinv_hbm.at[win + k], dbuf.at[k], dsems.at[k])
            for k in range(KL)]
    cp_j = pltpu.make_async_copy(jac_hbm.at[pl.ds(win, KL)], jbuf, sems.at[1])
    cp_b = pltpu.make_async_copy(base_hbm.at[pl.ds(win, KL)], bbuf, sems.at[2])
    cp_c = pltpu.make_async_copy(cur_hbm.at[pl.ds(win, KL)], cbuf, sems.at[3])
    acts = [T(1 + k) > 0 for k in range(KL)]
    for k in range(KL):
        pl.when(acts[k])(cp_d[k].start)
    cp_j.start()
    cp_b.start()
    cp_c.start()

    cp_a.wait()
    lane = lax.broadcasted_iota(jnp.int32, (16, 128), 1)
    low_half = lane < 64

    for src, off, chunk, keep_low in ((rxp, 19, 0, False), (rxm, 25, 0, True),
                                      (ryp, 31, 1, False), (rym, 37, 1, True)):
        for k in range(KL):
            t = T(off + k)

            @pl.when(t >= 0)
            def _():
                moved = pltpu.roll(src[k], 64, 1)
                keep = low_half if keep_low else jnp.logical_not(low_half)
                sl = pl.ds(chunk * 128, 128)
                accf[t, :, sl] = accf[t, :, sl] + jnp.where(keep, moved, 0.0)

    cp_j.wait()
    cp_b.wait()
    cp_c.wait()

    nr = KL * 16
    acc_win = accf[pl.ds(win, KL)].reshape(nr, NF * FW)
    lower = dot_exact01(acc_win, smat[...])
    base = bbuf[...].reshape(nr, SIDE**3)

    for k in range(KL):

        @pl.when(acts[k])
        def _():
            cp_d[k].wait()
            bk = base[16 * k:16 * (k + 1)]
            lk = lower[16 * k:16 * (k + 1)]
            vk = bk - lk if forward else lk
            parts = []
            for c0 in range(0, 16, 4):
                d = dbuf[k, c0:c0 + 4].astype(jnp.float32)
                parts.append(jnp.sum(d * vk[None], axis=1))
            y = jnp.concatenate(parts, axis=0)
            cbuf[k] = y if forward else bk - y

    cp_o = pltpu.make_async_copy(cbuf, cur_out.at[pl.ds(win, KL)], sems.at[4])
    cp_o.start()
    new = cbuf[...].reshape(nr, SIDE**3)
    sx[...] = jnp.zeros(sx.shape, jnp.float32)
    sy[...] = jnp.zeros(sy.shape, jnp.float32)

    faces = dot_exact01(new, gmat[...])
    flane = lax.broadcasted_iota(jnp.int32, (16, NF * FW), 1) // FW
    for k in range(KL):

        @pl.when(acts[k])
        def _():
            prod = dot_full(jbuf[k], faces[16 * k:16 * (k + 1)])
            inc = jnp.zeros((16, NF * FW), jnp.float32)
            for d in range(NF):
                inc = inc + jnp.where(flane == d, prod[16 * d:16 * (d + 1)], 0.0)
            sx[k] = inc[:, 0:128]
            sy[k] = inc[:, 128:256]
            zpart = pltpu.roll(inc[:, 256:384], 64, 1)
            tp = T(7 + k)
            tm = T(13 + k)

            @pl.when(tp >= 0)
            def _():
                sl = pl.ds(256, 128)
                accf[tp, :, sl] = accf[tp, :, sl] + jnp.where(low_half, 0.0, zpart)

            @pl.when(tm >= 0)
            def _():
                sl = pl.ds(256, 128)
                accf[tm, :, sl] = accf[tm, :, sl] + jnp.where(low_half, zpart, 0.0)

    cp_w = pltpu.make_async_copy(accf, accf_out, sems.at[5])
    cp_w.start()
    cp_o.wait()
    cp_w.wait()


def run_level(forward, lev, tbl, accf, base, cur, dinv, jac, recv, gmat, smat):
    n_blocks = accf.shape[0]
    kern = functools.partial(level_kernel, forward)
    smem = pl.BlockSpec(memory_space=pltpu.SMEM)
    vmem = pl.BlockSpec(memory_space=pltpu.VMEM)
    anyspace = pl.BlockSpec(memory_space=pl.ANY)
    out_shape = (
        jax.ShapeDtypeStruct(accf.shape, jnp.float32),
        jax.ShapeDtypeStruct(cur.shape, jnp.float32),
        jax.ShapeDtypeStruct((KL, 16, 128), jnp.float32),
        jax.ShapeDtypeStruct((KL, 16, 128), jnp.float32),
    )
    return pl.pallas_call(
        kern,
        out_shape=out_shape,
        in_specs=[smem, smem, anyspace, anyspace, anyspace, anyspace, anyspace,
                  vmem, vmem, vmem, vmem, vmem, vmem],
        out_specs=(anyspace, anyspace, vmem, vmem),
        scratch_shapes=[
            pltpu.VMEM(accf.shape, jnp.float32),
            pltpu.VMEM((KL,) + dinv.shape[1:], dinv.dtype),
            pltpu.VMEM((KL,) + jac.shape[1:], jnp.float32),
            pltpu.VMEM((KL,) + base.shape[1:], jnp.float32),
            pltpu.VMEM((KL,) + cur.shape[1:], jnp.float32),
            pltpu.SemaphoreType.DMA((6,)),
            pltpu.SemaphoreType.DMA((KL,)),
        ],
        input_output_aliases={2: 0, 4: 1},
        compiler_params=pltpu.CompilerParams(vmem_limit_bytes=48 * 1024 * 1024),
    )(lev, tbl, accf, base, cur, dinv, jac, *recv, gmat, smat)


def shift_along(value, axis, steps):
    count = lax.axis_size(axis)
    pairs = [(source, (source + steps) % count) for source in range(count)]
    return lax.ppermute(value, axis, pairs)


def exchange(sx, sy):
    return (
        shift_along(sx, "gx", 1),
        shift_along(sx, "gx", -1),
        shift_along(sy, "gy", 1),
        shift_along(sy, "gy", -1),
    )


def pick(vec, idx):
    ids = jnp.arange(vec.shape[0], dtype=jnp.int32).reshape((-1,) + (1,) * idx.ndim)
    return jnp.sum(jnp.where(idx[None] == ids, vec.reshape(ids.shape), 0), axis=0)


def pick_row(mat, row):
    ids = jnp.arange(mat.shape[0], dtype=jnp.int32)
    return jnp.sum(jnp.where(ids[:, None] == row, mat, 0), axis=0)


def build_tables(level_counts, slot_count):
    count_x = lax.axis_size("gx")
    count_y = lax.axis_size("gy")
    place_x = lax.axis_index("gx")
    place_y = lax.axis_index("gy")
    coords, where_slot = slot_layout(count_x, count_y, RX, RY, NBZ)
    nbs = [jnp.asarray(step_table(coords, where_slot, dm, st)) for dm, st in DIRECTION_MOVES]
    ends_all = jnp.cumsum(level_counts, axis=1)
    begins_all = ends_all - level_counts
    slots = jnp.arange(slot_count, dtype=jnp.int32)
    all_levels = jnp.sum(slots[None, :, None] >= ends_all[:, None, :], axis=2).astype(jnp.int32)
    own_row = place_x * count_y + place_y
    source_rows = [
        (place_x - 1) % count_x * count_y + place_y,
        (place_x + 1) % count_x * count_y + place_y,
        place_x * count_y + (place_y - 1) % count_y,
        place_x * count_y + (place_y + 1) % count_y,
    ]
    at_edge = [place_x == 0, place_x == count_x - 1, place_y == 0, place_y == count_y - 1]
    my_lv = pick_row(all_levels, own_row)
    levels = jnp.arange(LEVELS, dtype=jnp.int32)
    offsets = jnp.arange(KL, dtype=jnp.int32)

    def window(row, now):
        begin = pick(pick_row(begins_all, row), now)
        return jnp.clip(begin, 0, slot_count - KL)

    win = window(own_row, levels)
    wslots = win[:, None] + offsets[None, :]
    act = pick(my_lv, wslots) == levels[:, None]
    head = [win[:, None], act.astype(jnp.int32)]
    cols_f = list(head)
    cols_b = list(head)
    for d in (4, 5):
        tgt = pick(nbs[d], wslots)
        t_lv = pick(my_lv, tgt)
        live = (tgt >= 0) & act
        cols_f.append(jnp.where(live & (t_lv > levels[:, None]), tgt, -1))
        cols_b.append(jnp.where(live & (t_lv < levels[:, None]), tgt, -1))
    rows = jnp.stack(source_rows)
    row_hot = jnp.arange(ends_all.shape[0], dtype=jnp.int32)[None, :] == rows[:, None]
    src_begins = jnp.sum(jnp.where(row_hot[:, :, None], begins_all[None], 0), axis=1)
    src_levels = jnp.sum(jnp.where(row_hot[:, :, None], all_levels[None], 0), axis=1)
    lv_hot = levels[None, :] == levels[:, None]
    swin = jnp.sum(jnp.where(lv_hot[None], src_begins[:, None, :], 0), axis=2)
    swin = jnp.clip(swin, 0, slot_count - KL)
    sslots = swin[:, :, None] + offsets[None, None, :]
    slot_hot = sslots[..., None] == slots
    s_lv = jnp.sum(jnp.where(slot_hot, src_levels[:, None, None, :], 0), axis=3)
    s_act = s_lv == levels[None, :, None]
    nb_remote = jnp.stack(nbs[:4])
    stepped = jnp.sum(jnp.where(slot_hot, nb_remote[:, None, None, :], 0), axis=3)
    tgt = jnp.where(jnp.stack(at_edge)[:, None, None], stepped, sslots)
    tgt_hot = tgt[..., None] == slots
    t_lv = jnp.sum(jnp.where(tgt_hot, my_lv[None, None, None, :], 0), axis=3)
    live = (tgt >= 0) & s_act
    sent = levels[None, :, None]
    remote_f = jnp.where(live & (t_lv > sent), tgt, -1)
    remote_b = jnp.where(live & (t_lv < sent), tgt, -1)
    none_row = jnp.full((4, 1, KL), -1, jnp.int32)
    remote_f = jnp.concatenate([none_row, remote_f[:, :-1]], axis=1)
    remote_b = jnp.concatenate([remote_b[:, 1:], none_row], axis=1)
    for d in range(4):
        cols_f.append(remote_f[d])
        cols_b.append(remote_b[d])

    def finish(cols):
        table = jnp.concatenate(cols, axis=1).astype(jnp.int32)
        return jnp.pad(table, ((0, 0), (0, TW - table.shape[1])), constant_values=-1)

    return finish(cols_f), finish(cols_b)


def body(right_side, diag_inverse, face_jac, level_counts):
    slot_count = right_side.shape[0]
    unknowns = right_side.shape[1]
    gather_np, scatter_np = face_matrices(SIDE)
    gmat = jnp.asarray(gather_np, dtype=jnp.bfloat16)
    smat = jnp.asarray(scatter_np, dtype=jnp.bfloat16)
    jac = jnp.transpose(face_jac, (3, 0, 1, 2)).reshape(slot_count, NF * unknowns, unknowns)
    tbl_f, tbl_b = build_tables(level_counts, slot_count)
    zero_recv = tuple(jnp.zeros((KL, 16, 128), jnp.float32) for _ in range(4))

    def lev_arr(v):
        return jnp.reshape(jnp.asarray(v, jnp.int32), (1,))

    accf = jnp.zeros((slot_count, unknowns, NF * FW), jnp.float32)
    cur = jnp.zeros(right_side.shape, jnp.float32)
    accf, cur, sx, sy = run_level(True, lev_arr(0), tbl_f, accf, right_side, cur, diag_inverse,
                                  jac, zero_recv, gmat, smat)

    def fwd(l, carry):
        accf, cur, sx, sy = carry
        recv = exchange(sx, sy)
        return run_level(True, lev_arr(l), tbl_f, accf, right_side, cur, diag_inverse, jac,
                         recv, gmat, smat)

    accf, half, sx, sy = lax.fori_loop(1, LEVELS, fwd, (accf, cur, sx, sy))

    accf = jnp.zeros((slot_count, unknowns, NF * FW), jnp.float32)
    accf, cur, sx, sy = run_level(False, lev_arr(LEVELS - 1), tbl_b, accf, half, half,
                                  diag_inverse, jac, zero_recv, gmat, smat)

    def bwd(i, carry):
        accf, cur, sx, sy = carry
        recv = exchange(sx, sy)
        return run_level(False, lev_arr(LEVELS - 2 - i), tbl_b, accf, half, cur, diag_inverse,
                         jac, recv, gmat, smat)

    accf, result, sx, sy = lax.fori_loop(0, LEVELS - 1, bwd, (accf, cur, sx, sy))
    return result


def solution(mesh):
    return jax.shard_map(
        body,
        mesh=mesh,
        in_specs=(
            P(("gx", "gy"), None, None),
            P(("gx", "gy"), None, None, None),
            P(None, None, None, ("gx", "gy")),
            P(),
        ),
        out_specs=P(("gx", "gy"), None, None),
        check_vma=False,
    )
```

```python
import functools

import jax
import jax.numpy as jnp
import numpy as np
from jax import lax
from jax.experimental import pallas as pl
from jax.experimental.pallas import tpu as pltpu
from jax.sharding import PartitionSpec as P

SIDE = 8
LEVELS = 12
RX = 2
RY = 2
NBZ = 8
KL = 6
NF = 6
FW = SIDE * SIDE
TW = 48

OPPOSITE = (1, 0, 3, 2, 5, 4)
DIRECTION_MOVES = ((0, 1), (0, -1), (1, 1), (1, -1), (2, 1), (2, -1))


def slot_layout(step_x, step_y, count_x, count_y, count_z):
    ordering = sorted(
        (
            (step_x * along_x + step_y * along_y + along_z, along_x, along_y, along_z)
            for along_x in range(count_x)
            for along_y in range(count_y)
            for along_z in range(count_z)
        )
    )
    coords = np.array([record[1:] for record in ordering], dtype=np.int64)
    where_slot = np.zeros((count_x, count_y, count_z), dtype=np.int64)
    where_slot[coords[:, 0], coords[:, 1], coords[:, 2]] = np.arange(len(ordering))
    return (coords, where_slot)


def step_table(coords, where_slot, dimension, offset_step):
    moved = coords.copy()
    moved[:, dimension] += offset_step
    bound_size = where_slot.shape[dimension]
    inside = (moved[:, dimension] >= 0) & (moved[:, dimension] < bound_size)
    clipped = np.clip(moved, 0, np.array(where_slot.shape) - 1)
    target = where_slot[clipped[:, 0], clipped[:, 1], clipped[:, 2]]
    return np.where(inside, target, -1).astype(np.int32)


def face_matrices(edge_cells):
    cell_ids = np.arange(edge_cells**3).reshape(edge_cells, edge_cells, edge_cells)
    layers = [
        cell_ids[edge_cells - 1],
        cell_ids[0],
        cell_ids[:, edge_cells - 1],
        cell_ids[:, 0],
        cell_ids[:, :, edge_cells - 1],
        cell_ids[:, :, 0],
    ]
    outward = np.stack([layer_ids.reshape(-1) for layer_ids in layers])
    cell_total = edge_cells**3
    face_width = edge_cells * edge_cells
    gather = np.zeros((cell_total, NF * face_width), dtype=np.float32)
    for face_index in range(NF):
        gather[outward[face_index], face_index * face_width + np.arange(face_width)] = 1.0
    return gather, np.ascontiguousarray(gather.T)


def split3(x):
    hi = x.astype(jnp.bfloat16)
    rest = x - hi.astype(jnp.float32)
    mid = rest.astype(jnp.bfloat16)
    low = (rest - mid.astype(jnp.float32)).astype(jnp.bfloat16)
    return hi, mid, low


def mm(a, b):
    return jnp.dot(a, b, preferred_element_type=jnp.float32)


def dot_exact01(x, table):
    rows = x.shape[0]
    got = mm(jnp.concatenate(split3(x), axis=0), table)
    return got[:rows] + got[rows:2 * rows] + got[2 * rows:]


def split2(x):
    hi = x.astype(jnp.bfloat16)
    return hi, (x - hi.astype(jnp.float32)).astype(jnp.bfloat16)


def dot_full(a, b):
    ah, al = split2(a)
    bh, bl = split2(b)
    rows = a.shape[0]
    with_bh = mm(jnp.concatenate([ah, al], axis=0), bh)
    return with_bh[:rows] + (mm(ah, bl) + with_bh[rows:])


def level_kernel(forward, lev_ref, tbl_ref, accf_in, base_hbm, cur_hbm, dinv_hbm, jac_hbm,
                 rxp, rxm, ryp, rym, gmat, smat,
                 accf_out, cur_out, sx, sy,
                 accf, dbuf, jbuf, bbuf, cbuf, sems, dsems):
    lvl = lev_ref[0]

    def T(j):
        return tbl_ref[lvl, j]

    win = T(0)
    cp_a = pltpu.make_async_copy(accf_in, accf, sems.at[0])
    cp_a.start()
    cp_d = [pltpu.make_async_copy(dinv_hbm.at[win + k], dbuf.at[k], dsems.at[k])
            for k in range(KL)]
    cp_j = pltpu.make_async_copy(jac_hbm.at[pl.ds(win, KL)], jbuf, sems.at[1])
    cp_b = pltpu.make_async_copy(base_hbm.at[pl.ds(win, KL)], bbuf, sems.at[2])
    cp_c = pltpu.make_async_copy(cur_hbm.at[pl.ds(win, KL)], cbuf, sems.at[3])
    acts = [T(1 + k) > 0 for k in range(KL)]
    for k in range(KL):
        pl.when(acts[k])(cp_d[k].start)
    cp_j.start()
    cp_b.start()
    cp_c.start()

    cp_a.wait()
    lane = lax.broadcasted_iota(jnp.int32, (16, 128), 1)
    low_half = lane < 64

    for src, off, chunk, keep_low in ((rxp, 19, 0, False), (rxm, 25, 0, True),
                                      (ryp, 31, 1, False), (rym, 37, 1, True)):
        for k in range(KL):
            t = T(off + k)

            @pl.when(t >= 0)
            def _():
                moved = pltpu.roll(src[k], 64, 1)
                keep = low_half if keep_low else jnp.logical_not(low_half)
                sl = pl.ds(chunk * 128, 128)
                accf[t, :, sl] = accf[t, :, sl] + jnp.where(keep, moved, 0.0)

    cp_j.wait()
    cp_b.wait()
    cp_c.wait()

    nr = KL * 16
    acc_win = accf[pl.ds(win, KL)].reshape(nr, NF * FW)
    lower = dot_exact01(acc_win, smat[...])
    base = bbuf[...].reshape(nr, SIDE**3)

    for k in range(KL):

        @pl.when(acts[k])
        def _():
            cp_d[k].wait()
            bk = base[16 * k:16 * (k + 1)]
            lk = lower[16 * k:16 * (k + 1)]
            vk = bk - lk if forward else lk
            parts = []
            for c0 in range(0, 16, 4):
                d = dbuf[k, c0:c0 + 4].astype(jnp.float32)
                parts.append(jnp.sum(d * vk[None], axis=1))
            y = jnp.concatenate(parts, axis=0)
            cbuf[k] = y if forward else bk - y

    cp_o = pltpu.make_async_copy(cbuf, cur_out.at[pl.ds(win, KL)], sems.at[4])
    cp_o.start()
    new = cbuf[...].reshape(nr, SIDE**3)
    sx[...] = jnp.zeros(sx.shape, jnp.float32)
    sy[...] = jnp.zeros(sy.shape, jnp.float32)

    faces = dot_exact01(new, gmat[...])
    flane = lax.broadcasted_iota(jnp.int32, (16, NF * FW), 1) // FW
    for k in range(KL):

        @pl.when(acts[k])
        def _():
            prod = dot_full(jbuf[k], faces[16 * k:16 * (k + 1)])
            inc = jnp.zeros((16, NF * FW), jnp.float32)
            for d in range(NF):
                inc = inc + jnp.where(flane == d, prod[16 * d:16 * (d + 1)], 0.0)
            sx[k] = inc[:, 0:128]
            sy[k] = inc[:, 128:256]
            zpart = pltpu.roll(inc[:, 256:384], 64, 1)
            tp = T(7 + k)
            tm = T(13 + k)

            @pl.when(tp >= 0)
            def _():
                sl = pl.ds(256, 128)
                accf[tp, :, sl] = accf[tp, :, sl] + jnp.where(low_half, 0.0, zpart)

            @pl.when(tm >= 0)
            def _():
                sl = pl.ds(256, 128)
                accf[tm, :, sl] = accf[tm, :, sl] + jnp.where(low_half, zpart, 0.0)

    cp_w = pltpu.make_async_copy(accf, accf_out, sems.at[5])
    cp_w.start()
    cp_o.wait()
    cp_w.wait()


def run_level(forward, lev, tbl, accf, base, cur, dinv, jac, recv, gmat, smat):
    n_blocks = accf.shape[0]
    kern = functools.partial(level_kernel, forward)
    smem = pl.BlockSpec(memory_space=pltpu.SMEM)
    vmem = pl.BlockSpec(memory_space=pltpu.VMEM)
    anyspace = pl.BlockSpec(memory_space=pl.ANY)
    out_shape = (
        jax.ShapeDtypeStruct(accf.shape, jnp.float32),
        jax.ShapeDtypeStruct(cur.shape, jnp.float32),
        jax.ShapeDtypeStruct((KL, 16, 128), jnp.float32),
        jax.ShapeDtypeStruct((KL, 16, 128), jnp.float32),
    )
    return pl.pallas_call(
        kern,
        out_shape=out_shape,
        in_specs=[smem, smem, anyspace, anyspace, anyspace, anyspace, anyspace,
                  vmem, vmem, vmem, vmem, vmem, vmem],
        out_specs=(anyspace, anyspace, vmem, vmem),
        scratch_shapes=[
            pltpu.VMEM(accf.shape, jnp.float32),
            pltpu.VMEM((KL,) + dinv.shape[1:], dinv.dtype),
            pltpu.VMEM((KL,) + jac.shape[1:], jnp.float32),
            pltpu.VMEM((KL,) + base.shape[1:], jnp.float32),
            pltpu.VMEM((KL,) + cur.shape[1:], jnp.float32),
            pltpu.SemaphoreType.DMA((6,)),
            pltpu.SemaphoreType.DMA((KL,)),
        ],
        input_output_aliases={2: 0, 4: 1},
        compiler_params=pltpu.CompilerParams(vmem_limit_bytes=48 * 1024 * 1024),
    )(lev, tbl, accf, base, cur, dinv, jac, *recv, gmat, smat)


def shift_along(value, axis, steps):
    count = lax.axis_size(axis)
    pairs = [(source, (source + steps) % count) for source in range(count)]
    return lax.ppermute(value, axis, pairs)


def exchange(sx, sy):
    return (
        shift_along(sx, "gx", 1),
        shift_along(sx, "gx", -1),
        shift_along(sy, "gy", 1),
        shift_along(sy, "gy", -1),
    )


def pick(vec, idx):
    ids = jnp.arange(vec.shape[0], dtype=jnp.int32).reshape((-1,) + (1,) * idx.ndim)
    return jnp.sum(jnp.where(idx[None] == ids, vec.reshape(ids.shape), 0), axis=0)


def pick_row(mat, row):
    ids = jnp.arange(mat.shape[0], dtype=jnp.int32)
    return jnp.sum(jnp.where(ids[:, None] == row, mat, 0), axis=0)


def build_tables(level_counts, slot_count):
    count_x = lax.axis_size("gx")
    count_y = lax.axis_size("gy")
    place_x = lax.axis_index("gx")
    place_y = lax.axis_index("gy")
    coords, where_slot = slot_layout(count_x, count_y, RX, RY, NBZ)
    nbs = [jnp.asarray(step_table(coords, where_slot, dm, st)) for dm, st in DIRECTION_MOVES]
    ends_all = jnp.cumsum(level_counts, axis=1)
    begins_all = ends_all - level_counts
    slots = jnp.arange(slot_count, dtype=jnp.int32)
    all_levels = jnp.sum(slots[None, :, None] >= ends_all[:, None, :], axis=2).astype(jnp.int32)
    own_row = place_x * count_y + place_y
    source_rows = [
        (place_x - 1) % count_x * count_y + place_y,
        (place_x + 1) % count_x * count_y + place_y,
        place_x * count_y + (place_y - 1) % count_y,
        place_x * count_y + (place_y + 1) % count_y,
    ]
    at_edge = [place_x == 0, place_x == count_x - 1, place_y == 0, place_y == count_y - 1]
    my_lv = pick_row(all_levels, own_row)
    levels = jnp.arange(LEVELS, dtype=jnp.int32)
    offsets = jnp.arange(KL, dtype=jnp.int32)

    def window(row, now):
        begin = pick(pick_row(begins_all, row), now)
        return jnp.clip(begin, 0, slot_count - KL)

    win = window(own_row, levels)
    wslots = win[:, None] + offsets[None, :]
    act = pick(my_lv, wslots) == levels[:, None]
    head = [win[:, None], act.astype(jnp.int32)]
    cols_f = list(head)
    cols_b = list(head)
    for d in (4, 5):
        tgt = pick(nbs[d], wslots)
        t_lv = pick(my_lv, tgt)
        live = (tgt >= 0) & act
        cols_f.append(jnp.where(live & (t_lv > levels[:, None]), tgt, -1))
        cols_b.append(jnp.where(live & (t_lv < levels[:, None]), tgt, -1))
    rows = jnp.stack(source_rows)
    row_hot = jnp.arange(ends_all.shape[0], dtype=jnp.int32)[None, :] == rows[:, None]
    src_begins = jnp.sum(jnp.where(row_hot[:, :, None], begins_all[None], 0), axis=1)
    src_levels = jnp.sum(jnp.where(row_hot[:, :, None], all_levels[None], 0), axis=1)
    lv_hot = levels[None, :] == levels[:, None]
    swin = jnp.sum(jnp.where(lv_hot[None], src_begins[:, None, :], 0), axis=2)
    swin = jnp.clip(swin, 0, slot_count - KL)
    sslots = swin[:, :, None] + offsets[None, None, :]
    slot_hot = sslots[..., None] == slots
    s_lv = jnp.sum(jnp.where(slot_hot, src_levels[:, None, None, :], 0), axis=3)
    s_act = s_lv == levels[None, :, None]
    nb_remote = jnp.stack(nbs[:4])
    stepped = jnp.sum(jnp.where(slot_hot, nb_remote[:, None, None, :], 0), axis=3)
    tgt = jnp.where(jnp.stack(at_edge)[:, None, None], stepped, sslots)
    tgt_hot = tgt[..., None] == slots
    t_lv = jnp.sum(jnp.where(tgt_hot, my_lv[None, None, None, :], 0), axis=3)
    live = (tgt >= 0) & s_act
    sent = levels[None, :, None]
    remote_f = jnp.where(live & (t_lv > sent), tgt, -1)
    remote_b = jnp.where(live & (t_lv < sent), tgt, -1)
    none_row = jnp.full((4, 1, KL), -1, jnp.int32)
    remote_f = jnp.concatenate([none_row, remote_f[:, :-1]], axis=1)
    remote_b = jnp.concatenate([remote_b[:, 1:], none_row], axis=1)
    for d in range(4):
        cols_f.append(remote_f[d])
        cols_b.append(remote_b[d])

    def finish(cols):
        table = jnp.concatenate(cols, axis=1).astype(jnp.int32)
        return jnp.pad(table, ((0, 0), (0, TW - table.shape[1])), constant_values=-1)

    return finish(cols_f), finish(cols_b)


def body(right_side, diag_inverse, face_jac, level_counts):
    slot_count = right_side.shape[0]
    unknowns = right_side.shape[1]
    gather_np, scatter_np = face_matrices(SIDE)
    gmat = jnp.asarray(gather_np, dtype=jnp.bfloat16)
    smat = jnp.asarray(scatter_np, dtype=jnp.bfloat16)
    jac = jnp.transpose(face_jac, (3, 0, 1, 2)).reshape(slot_count, NF * unknowns, unknowns)
    tbl_f, tbl_b = build_tables(level_counts, slot_count)
    zero_recv = tuple(jnp.zeros((KL, 16, 128), jnp.float32) for _ in range(4))

    def lev_arr(v):
        return jnp.reshape(jnp.asarray(v, jnp.int32), (1,))

    accf = jnp.zeros((slot_count, unknowns, NF * FW), jnp.float32)
    cur = jnp.zeros(right_side.shape, jnp.float32)
    accf, cur, sx, sy = run_level(True, lev_arr(0), tbl_f, accf, right_side, cur, diag_inverse,
                                  jac, zero_recv, gmat, smat)

    def fwd(l, carry):
        accf, cur, sx, sy = carry
        recv = exchange(sx, sy)
        return run_level(True, lev_arr(l), tbl_f, accf, right_side, cur, diag_inverse, jac,
                         recv, gmat, smat)

    accf, half, sx, sy = lax.fori_loop(1, LEVELS, fwd, (accf, cur, sx, sy))

    accf = jnp.zeros((slot_count, unknowns, NF * FW), jnp.float32)
    accf, cur, sx, sy = run_level(False, lev_arr(LEVELS - 1), tbl_b, accf, half, half,
                                  diag_inverse, jac, zero_recv, gmat, smat)

    def bwd(i, carry):
        accf, cur, sx, sy = carry
        recv = exchange(sx, sy)
        return run_level(False, lev_arr(LEVELS - 2 - i), tbl_b, accf, half, cur, diag_inverse,
                         jac, recv, gmat, smat)

    accf, result, sx, sy = lax.fori_loop(0, LEVELS - 1, bwd, (accf, cur, sx, sy))
    return result


def solution(mesh):
    return jax.shard_map(
        body,
        mesh=mesh,
        in_specs=(
            P(("gx", "gy"), None, None),
            P(("gx", "gy"), None, None, None),
            P(None, None, None, ("gx", "gy")),
            P(),
        ),
        out_specs=P(("gx", "gy"), None, None),
        check_vma=False,
    )
```

```python
import functools

import jax
import jax.numpy as jnp
import numpy as np
from jax import lax
from jax.experimental import pallas as pl
from jax.experimental.pallas import tpu as pltpu
from jax.sharding import PartitionSpec as P

SIDE = 8
LEVELS = 12
RX = 2
RY = 2
NBZ = 8
KL = 6
NF = 6
FW = SIDE * SIDE
TW = 48

OPPOSITE = (1, 0, 3, 2, 5, 4)
DIRECTION_MOVES = ((0, 1), (0, -1), (1, 1), (1, -1), (2, 1), (2, -1))


def slot_layout(step_x, step_y, count_x, count_y, count_z):
    ordering = sorted(
        (
            (step_x * along_x + step_y * along_y + along_z, along_x, along_y, along_z)
            for along_x in range(count_x)
            for along_y in range(count_y)
            for along_z in range(count_z)
        )
    )
    coords = np.array([record[1:] for record in ordering], dtype=np.int64)
    where_slot = np.zeros((count_x, count_y, count_z), dtype=np.int64)
    where_slot[coords[:, 0], coords[:, 1], coords[:, 2]] = np.arange(len(ordering))
    return (coords, where_slot)


def step_table(coords, where_slot, dimension, offset_step):
    moved = coords.copy()
    moved[:, dimension] += offset_step
    bound_size = where_slot.shape[dimension]
    inside = (moved[:, dimension] >= 0) & (moved[:, dimension] < bound_size)
    clipped = np.clip(moved, 0, np.array(where_slot.shape) - 1)
    target = where_slot[clipped[:, 0], clipped[:, 1], clipped[:, 2]]
    return np.where(inside, target, -1).astype(np.int32)


def face_matrices(edge_cells):
    cell_ids = np.arange(edge_cells**3).reshape(edge_cells, edge_cells, edge_cells)
    layers = [
        cell_ids[edge_cells - 1],
        cell_ids[0],
        cell_ids[:, edge_cells - 1],
        cell_ids[:, 0],
        cell_ids[:, :, edge_cells - 1],
        cell_ids[:, :, 0],
    ]
    outward = np.stack([layer_ids.reshape(-1) for layer_ids in layers])
    cell_total = edge_cells**3
    face_width = edge_cells * edge_cells
    gather = np.zeros((cell_total, NF * face_width), dtype=np.float32)
    for face_index in range(NF):
        gather[outward[face_index], face_index * face_width + np.arange(face_width)] = 1.0
    return gather, np.ascontiguousarray(gather.T)


def split3(x):
    hi = x.astype(jnp.bfloat16)
    rest = x - hi.astype(jnp.float32)
    mid = rest.astype(jnp.bfloat16)
    low = (rest - mid.astype(jnp.float32)).astype(jnp.bfloat16)
    return hi, mid, low


def mm(a, b):
    return jnp.dot(a, b, preferred_element_type=jnp.float32)


def dot_exact01(x, table):
    hi, mid, low = split3(x)
    return mm(hi, table) + mm(mid, table) + mm(low, table)


def split2(x):
    hi = x.astype(jnp.bfloat16)
    return hi, (x - hi.astype(jnp.float32)).astype(jnp.bfloat16)


def dot_full(a, b):
    ah, al = split2(a)
    bh, bl = split2(b)
    return mm(ah, bh) + (mm(ah, bl) + mm(al, bh))


def dinv_rows(dbuf, k, vk):
    sub = lax.broadcasted_iota(jnp.int32, (8, vk.shape[1]), 0)
    groups = []
    for g in range(2):
        xs = []
        for c in range(8):
            prod = dbuf[k, 8 * g + c].astype(jnp.float32) * vk
            xs.append(prod[0:8] + prod[8:16])
        ys = [jnp.where(sub < 4, xs[c] + pltpu.roll(xs[c], 4, 0),
                        xs[c + 4] + pltpu.roll(xs[c + 4], 4, 0)) for c in range(4)]
        zs = [jnp.where(sub % 4 < 2, ys[c] + pltpu.roll(ys[c], 6, 0),
                        ys[c + 2] + pltpu.roll(ys[c + 2], 2, 0)) for c in range(2)]
        groups.append(jnp.where(sub % 2 == 0, zs[0] + pltpu.roll(zs[0], 7, 0),
                                zs[1] + pltpu.roll(zs[1], 1, 0)))
    return jnp.concatenate(groups, axis=0)


def level_kernel(forward, lev_ref, tbl_ref, accf_in, base_hbm, cur_hbm, dinv_hbm, jac_hbm,
                 rxp, rxm, ryp, rym, gmat, smat,
                 accf_out, cur_out, sx, sy,
                 accf, dbuf, jbuf, bbuf, cbuf, sems, dsems):
    lvl = lev_ref[0]

    def T(j):
        return tbl_ref[lvl, j]

    win = T(0)
    cp_a = pltpu.make_async_copy(accf_in, accf, sems.at[0])
    cp_a.start()
    cp_d = [pltpu.make_async_copy(dinv_hbm.at[win + k], dbuf.at[k], dsems.at[k])
            for k in range(KL)]
    cp_j = pltpu.make_async_copy(jac_hbm.at[pl.ds(win, KL)], jbuf, sems.at[1])
    cp_b = pltpu.make_async_copy(base_hbm.at[pl.ds(win, KL)], bbuf, sems.at[2])
    cp_c = pltpu.make_async_copy(cur_hbm.at[pl.ds(win, KL)], cbuf, sems.at[3])
    acts = [T(1 + k) > 0 for k in range(KL)]
    for k in range(KL):
        pl.when(acts[k])(cp_d[k].start)
    cp_j.start()
    cp_b.start()
    cp_c.start()

    cp_a.wait()
    lane = lax.broadcasted_iota(jnp.int32, (16, 128), 1)
    low_half = lane < 64

    for src, off, chunk, keep_low in ((rxp, 19, 0, False), (rxm, 25, 0, True),
                                      (ryp, 31, 1, False), (rym, 37, 1, True)):
        for k in range(KL):
            t = T(off + k)

            @pl.when(t >= 0)
            def _():
                moved = pltpu.roll(src[k], 64, 1)
                keep = low_half if keep_low else jnp.logical_not(low_half)
                sl = pl.ds(chunk * 128, 128)
                accf[t, :, sl] = accf[t, :, sl] + jnp.where(keep, moved, 0.0)

    cp_j.wait()
    cp_b.wait()
    cp_c.wait()

    nr = KL * 16
    acc_win = accf[pl.ds(win, KL)].reshape(nr, NF * FW)
    lower = dot_exact01(acc_win, smat[...])
    base = bbuf[...].reshape(nr, SIDE**3)

    for k in range(KL):

        @pl.when(acts[k])
        def _():
            cp_d[k].wait()
            bk = base[16 * k:16 * (k + 1)]
            lk = lower[16 * k:16 * (k + 1)]
            vk = bk - lk if forward else lk
            y = dinv_rows(dbuf, k, vk)
            cbuf[k] = y if forward else bk - y

    cp_o = pltpu.make_async_copy(cbuf, cur_out.at[pl.ds(win, KL)], sems.at[4])
    cp_o.start()
    new = cbuf[...].reshape(nr, SIDE**3)
    sx[...] = jnp.zeros(sx.shape, jnp.float32)
    sy[...] = jnp.zeros(sy.shape, jnp.float32)

    faces = dot_exact01(new, gmat[...])
    flane = lax.broadcasted_iota(jnp.int32, (16, NF * FW), 1) // FW
    for k in range(KL):

        @pl.when(acts[k])
        def _():
            prod = dot_full(jbuf[k], faces[16 * k:16 * (k + 1)])
            inc = jnp.zeros((16, NF * FW), jnp.float32)
            for d in range(NF):
                inc = inc + jnp.where(flane == d, prod[16 * d:16 * (d + 1)], 0.0)
            sx[k] = inc[:, 0:128]
            sy[k] = inc[:, 128:256]
            zpart = pltpu.roll(inc[:, 256:384], 64, 1)
            tp = T(7 + k)
            tm = T(13 + k)

            @pl.when(tp >= 0)
            def _():
                sl = pl.ds(256, 128)
                accf[tp, :, sl] = accf[tp, :, sl] + jnp.where(low_half, 0.0, zpart)

            @pl.when(tm >= 0)
            def _():
                sl = pl.ds(256, 128)
                accf[tm, :, sl] = accf[tm, :, sl] + jnp.where(low_half, zpart, 0.0)

    cp_w = pltpu.make_async_copy(accf, accf_out, sems.at[5])
    cp_w.start()
    cp_o.wait()
    cp_w.wait()


def run_level(forward, lev, tbl, accf, base, cur, dinv, jac, recv, gmat, smat):
    n_blocks = accf.shape[0]
    kern = functools.partial(level_kernel, forward)
    smem = pl.BlockSpec(memory_space=pltpu.SMEM)
    vmem = pl.BlockSpec(memory_space=pltpu.VMEM)
    anyspace = pl.BlockSpec(memory_space=pl.ANY)
    out_shape = (
        jax.ShapeDtypeStruct(accf.shape, jnp.float32),
        jax.ShapeDtypeStruct(cur.shape, jnp.float32),
        jax.ShapeDtypeStruct((KL, 16, 128), jnp.float32),
        jax.ShapeDtypeStruct((KL, 16, 128), jnp.float32),
    )
    return pl.pallas_call(
        kern,
        out_shape=out_shape,
        in_specs=[smem, smem, anyspace, anyspace, anyspace, anyspace, anyspace,
                  vmem, vmem, vmem, vmem, vmem, vmem],
        out_specs=(anyspace, anyspace, vmem, vmem),
        scratch_shapes=[
            pltpu.VMEM(accf.shape, jnp.float32),
            pltpu.VMEM((KL,) + dinv.shape[1:], dinv.dtype),
            pltpu.VMEM((KL,) + jac.shape[1:], jnp.float32),
            pltpu.VMEM((KL,) + base.shape[1:], jnp.float32),
            pltpu.VMEM((KL,) + cur.shape[1:], jnp.float32),
            pltpu.SemaphoreType.DMA((6,)),
            pltpu.SemaphoreType.DMA((KL,)),
        ],
        input_output_aliases={2: 0, 4: 1},
        compiler_params=pltpu.CompilerParams(vmem_limit_bytes=48 * 1024 * 1024),
    )(lev, tbl, accf, base, cur, dinv, jac, *recv, gmat, smat)


def shift_along(value, axis, steps):
    count = lax.axis_size(axis)
    pairs = [(source, (source + steps) % count) for source in range(count)]
    return lax.ppermute(value, axis, pairs)


def exchange(sx, sy):
    return (
        shift_along(sx, "gx", 1),
        shift_along(sx, "gx", -1),
        shift_along(sy, "gy", 1),
        shift_along(sy, "gy", -1),
    )


def pick(vec, idx):
    ids = jnp.arange(vec.shape[0], dtype=jnp.int32).reshape((-1,) + (1,) * idx.ndim)
    return jnp.sum(jnp.where(idx[None] == ids, vec.reshape(ids.shape), 0), axis=0)


def pick_row(mat, row):
    ids = jnp.arange(mat.shape[0], dtype=jnp.int32)
    return jnp.sum(jnp.where(ids[:, None] == row, mat, 0), axis=0)


def build_tables(level_counts, slot_count):
    count_x = lax.axis_size("gx")
    count_y = lax.axis_size("gy")
    place_x = lax.axis_index("gx")
    place_y = lax.axis_index("gy")
    coords, where_slot = slot_layout(count_x, count_y, RX, RY, NBZ)
    nbs = [jnp.asarray(step_table(coords, where_slot, dm, st)) for dm, st in DIRECTION_MOVES]
    ends_all = jnp.cumsum(level_counts, axis=1)
    begins_all = ends_all - level_counts
    slots = jnp.arange(slot_count, dtype=jnp.int32)
    all_levels = jnp.sum(slots[None, :, None] >= ends_all[:, None, :], axis=2).astype(jnp.int32)
    own_row = place_x * count_y + place_y
    source_rows = [
        (place_x - 1) % count_x * count_y + place_y,
        (place_x + 1) % count_x * count_y + place_y,
        place_x * count_y + (place_y - 1) % count_y,
        place_x * count_y + (place_y + 1) % count_y,
    ]
    at_edge = [place_x == 0, place_x == count_x - 1, place_y == 0, place_y == count_y - 1]
    my_lv = pick_row(all_levels, own_row)
    levels = jnp.arange(LEVELS, dtype=jnp.int32)
    offsets = jnp.arange(KL, dtype=jnp.int32)

    def window(row, now):
        begin = pick(pick_row(begins_all, row), now)
        return jnp.clip(begin, 0, slot_count - KL)

    win = window(own_row, levels)
    wslots = win[:, None] + offsets[None, :]
    act = pick(my_lv, wslots) == levels[:, None]
    head = [win[:, None], act.astype(jnp.int32)]
    cols_f = list(head)
    cols_b = list(head)
    for d in (4, 5):
        tgt = pick(nbs[d], wslots)
        t_lv = pick(my_lv, tgt)
        live = (tgt >= 0) & act
        cols_f.append(jnp.where(live & (t_lv > levels[:, None]), tgt, -1))
        cols_b.append(jnp.where(live & (t_lv < levels[:, None]), tgt, -1))
    rows = jnp.stack(source_rows)
    row_hot = jnp.arange(ends_all.shape[0], dtype=jnp.int32)[None, :] == rows[:, None]
    src_begins = jnp.sum(jnp.where(row_hot[:, :, None], begins_all[None], 0), axis=1)
    src_levels = jnp.sum(jnp.where(row_hot[:, :, None], all_levels[None], 0), axis=1)
    lv_hot = levels[None, :] == levels[:, None]
    swin = jnp.sum(jnp.where(lv_hot[None], src_begins[:, None, :], 0), axis=2)
    swin = jnp.clip(swin, 0, slot_count - KL)
    sslots = swin[:, :, None] + offsets[None, None, :]
    slot_hot = sslots[..., None] == slots
    s_lv = jnp.sum(jnp.where(slot_hot, src_levels[:, None, None, :], 0), axis=3)
    s_act = s_lv == levels[None, :, None]
    nb_remote = jnp.stack(nbs[:4])
    stepped = jnp.sum(jnp.where(slot_hot, nb_remote[:, None, None, :], 0), axis=3)
    tgt = jnp.where(jnp.stack(at_edge)[:, None, None], stepped, sslots)
    tgt_hot = tgt[..., None] == slots
    t_lv = jnp.sum(jnp.where(tgt_hot, my_lv[None, None, None, :], 0), axis=3)
    live = (tgt >= 0) & s_act
    sent = levels[None, :, None]
    remote_f = jnp.where(live & (t_lv > sent), tgt, -1)
    remote_b = jnp.where(live & (t_lv < sent), tgt, -1)
    none_row = jnp.full((4, 1, KL), -1, jnp.int32)
    remote_f = jnp.concatenate([none_row, remote_f[:, :-1]], axis=1)
    remote_b = jnp.concatenate([remote_b[:, 1:], none_row], axis=1)
    for d in range(4):
        cols_f.append(remote_f[d])
        cols_b.append(remote_b[d])

    def finish(cols):
        table = jnp.concatenate(cols, axis=1).astype(jnp.int32)
        return jnp.pad(table, ((0, 0), (0, TW - table.shape[1])), constant_values=-1)

    return finish(cols_f), finish(cols_b)


def body(right_side, diag_inverse, face_jac, level_counts):
    slot_count = right_side.shape[0]
    unknowns = right_side.shape[1]
    gather_np, scatter_np = face_matrices(SIDE)
    gmat = jnp.asarray(gather_np, dtype=jnp.bfloat16)
    smat = jnp.asarray(scatter_np, dtype=jnp.bfloat16)
    jac = jnp.transpose(face_jac, (3, 0, 1, 2)).reshape(slot_count, NF * unknowns, unknowns)
    tbl_f, tbl_b = build_tables(level_counts, slot_count)
    zero_recv = tuple(jnp.zeros((KL, 16, 128), jnp.float32) for _ in range(4))

    def lev_arr(v):
        return jnp.reshape(jnp.asarray(v, jnp.int32), (1,))

    accf = jnp.zeros((slot_count, unknowns, NF * FW), jnp.float32)
    cur = jnp.zeros(right_side.shape, jnp.float32)
    accf, cur, sx, sy = run_level(True, lev_arr(0), tbl_f, accf, right_side, cur, diag_inverse,
                                  jac, zero_recv, gmat, smat)

    def fwd(l, carry):
        accf, cur, sx, sy = carry
        recv = exchange(sx, sy)
        return run_level(True, lev_arr(l), tbl_f, accf, right_side, cur, diag_inverse, jac,
                         recv, gmat, smat)

    accf, half, sx, sy = lax.fori_loop(1, LEVELS, fwd, (accf, cur, sx, sy))

    accf = jnp.zeros((slot_count, unknowns, NF * FW), jnp.float32)
    accf, cur, sx, sy = run_level(False, lev_arr(LEVELS - 1), tbl_b, accf, half, half,
                                  diag_inverse, jac, zero_recv, gmat, smat)

    def bwd(i, carry):
        accf, cur, sx, sy = carry
        recv = exchange(sx, sy)
        return run_level(False, lev_arr(LEVELS - 2 - i), tbl_b, accf, half, cur, diag_inverse,
                         jac, recv, gmat, smat)

    accf, result, sx, sy = lax.fori_loop(0, LEVELS - 1, bwd, (accf, cur, sx, sy))
    return result


def solution(mesh):
    return jax.shard_map(
        body,
        mesh=mesh,
        in_specs=(
            P(("gx", "gy"), None, None),
            P(("gx", "gy"), None, None, None),
            P(None, None, None, ("gx", "gy")),
            P(),
        ),
        out_specs=P(("gx", "gy"), None, None),
        check_vma=False,
    )
```

```python
import functools

import jax
import jax.numpy as jnp
import numpy as np
from jax import lax
from jax.experimental import pallas as pl
from jax.experimental.pallas import tpu as pltpu
from jax.sharding import PartitionSpec as P

SIDE = 8
LEVELS = 12
RX = 2
RY = 2
NBZ = 8
KL = 6
NF = 6
FW = SIDE * SIDE
TW = 48

OPPOSITE = (1, 0, 3, 2, 5, 4)
DIRECTION_MOVES = ((0, 1), (0, -1), (1, 1), (1, -1), (2, 1), (2, -1))


def slot_layout(step_x, step_y, count_x, count_y, count_z):
    ordering = sorted(
        (
            (step_x * along_x + step_y * along_y + along_z, along_x, along_y, along_z)
            for along_x in range(count_x)
            for along_y in range(count_y)
            for along_z in range(count_z)
        )
    )
    coords = np.array([record[1:] for record in ordering], dtype=np.int64)
    where_slot = np.zeros((count_x, count_y, count_z), dtype=np.int64)
    where_slot[coords[:, 0], coords[:, 1], coords[:, 2]] = np.arange(len(ordering))
    return (coords, where_slot)


def step_table(coords, where_slot, dimension, offset_step):
    moved = coords.copy()
    moved[:, dimension] += offset_step
    bound_size = where_slot.shape[dimension]
    inside = (moved[:, dimension] >= 0) & (moved[:, dimension] < bound_size)
    clipped = np.clip(moved, 0, np.array(where_slot.shape) - 1)
    target = where_slot[clipped[:, 0], clipped[:, 1], clipped[:, 2]]
    return np.where(inside, target, -1).astype(np.int32)


def face_matrices(edge_cells):
    cell_ids = np.arange(edge_cells**3).reshape(edge_cells, edge_cells, edge_cells)
    layers = [
        cell_ids[edge_cells - 1],
        cell_ids[0],
        cell_ids[:, edge_cells - 1],
        cell_ids[:, 0],
        cell_ids[:, :, edge_cells - 1],
        cell_ids[:, :, 0],
    ]
    outward = np.stack([layer_ids.reshape(-1) for layer_ids in layers])
    cell_total = edge_cells**3
    face_width = edge_cells * edge_cells
    gather = np.zeros((cell_total, NF * face_width), dtype=np.float32)
    for face_index in range(NF):
        gather[outward[face_index], face_index * face_width + np.arange(face_width)] = 1.0
    return gather, np.ascontiguousarray(gather.T)


def split3(x):
    hi = x.astype(jnp.bfloat16)
    rest = x - hi.astype(jnp.float32)
    mid = rest.astype(jnp.bfloat16)
    low = (rest - mid.astype(jnp.float32)).astype(jnp.bfloat16)
    return hi, mid, low


def mm(a, b):
    return jnp.dot(a, b, preferred_element_type=jnp.float32)


def dot_exact01(x, table):
    hi, mid, low = split3(x)
    return mm(hi, table) + mm(mid, table) + mm(low, table)


def split2(x):
    hi = x.astype(jnp.bfloat16)
    return hi, (x - hi.astype(jnp.float32)).astype(jnp.bfloat16)


def dot_full(a, b):
    ah, al = split2(a)
    bh, bl = split2(b)
    return mm(ah, bh) + (mm(ah, bl) + mm(al, bh))


RECV = ((19, 0, False), (25, 0, True), (31, 1, False), (37, 1, True))


def compute_kernel(forward, lev_ref, tbl_ref, accf_hbm, base_hbm, cur_hbm, dinv_hbm, jac_hbm,
                   rxp, rxm, ryp, rym, gmat, smat,
                   cur_out, sx, sy, zc,
                   accw, dbuf, jbuf, bbuf, cbuf, sems, dsems):
    lvl = lev_ref[0]

    def T(j):
        return tbl_ref[lvl, j]

    win = T(0)
    cp_a = pltpu.make_async_copy(accf_hbm.at[pl.ds(win, KL)], accw, sems.at[0])
    cp_a.start()
    cp_d = [pltpu.make_async_copy(dinv_hbm.at[win + k], dbuf.at[k], dsems.at[k])
            for k in range(KL)]
    cp_j = pltpu.make_async_copy(jac_hbm.at[pl.ds(win, KL)], jbuf, sems.at[1])
    cp_b = pltpu.make_async_copy(base_hbm.at[pl.ds(win, KL)], bbuf, sems.at[2])
    cp_c = pltpu.make_async_copy(cur_hbm.at[pl.ds(win, KL)], cbuf, sems.at[3])
    acts = [T(1 + k) > 0 for k in range(KL)]
    for k in range(KL):
        pl.when(acts[k])(cp_d[k].start)
    cp_j.start()
    cp_b.start()
    cp_c.start()

    cp_a.wait()
    lane = lax.broadcasted_iota(jnp.int32, (16, 128), 1)
    low_half = lane < 64

    for src, (off, chunk, keep_low) in zip((rxp, rxm, ryp, rym), RECV):
        for k in range(KL):
            j = T(off + k) - win

            @pl.when((j >= 0) & (j < KL))
            def _():
                moved = pltpu.roll(src[k], 64, 1)
                keep = low_half if keep_low else jnp.logical_not(low_half)
                sl = pl.ds(chunk * 128, 128)
                accw[j, :, sl] = accw[j, :, sl] + jnp.where(keep, moved, 0.0)

    cp_j.wait()
    cp_b.wait()
    cp_c.wait()

    nr = KL * 16
    acc_win = accw[...].reshape(nr, NF * FW)
    lower = dot_exact01(acc_win, smat[...])
    base = bbuf[...].reshape(nr, SIDE**3)

    for k in range(KL):

        @pl.when(acts[k])
        def _():
            cp_d[k].wait()
            bk = base[16 * k:16 * (k + 1)]
            lk = lower[16 * k:16 * (k + 1)]
            vk = bk - lk if forward else lk
            parts = []
            for c0 in range(0, 16, 4):
                d = dbuf[k, c0:c0 + 4].astype(jnp.float32)
                parts.append(jnp.sum(d * vk[None], axis=1))
            y = jnp.concatenate(parts, axis=0)
            cbuf[k] = y if forward else bk - y

    cp_o = pltpu.make_async_copy(cbuf, cur_out.at[pl.ds(win, KL)], sems.at[4])
    cp_o.start()
    new = cbuf[...].reshape(nr, SIDE**3)
    sx[...] = jnp.zeros(sx.shape, jnp.float32)
    sy[...] = jnp.zeros(sy.shape, jnp.float32)
    zc[...] = jnp.zeros(zc.shape, jnp.float32)

    faces = dot_exact01(new, gmat[...])
    flane = lax.broadcasted_iota(jnp.int32, (16, NF * FW), 1) // FW
    for k in range(KL):

        @pl.when(acts[k])
        def _():
            prod = dot_full(jbuf[k], faces[16 * k:16 * (k + 1)])
            inc = jnp.zeros((16, NF * FW), jnp.float32)
            for d in range(NF):
                inc = inc + jnp.where(flane == d, prod[16 * d:16 * (d + 1)], 0.0)
            sx[k] = inc[:, 0:128]
            sy[k] = inc[:, 128:256]
            zc[k] = pltpu.roll(inc[:, 256:384], 64, 1)

    cp_o.wait()


def update_kernel(lev_ref, tbl_ref, accf_in, rxp, rxm, ryp, rym, zc, accf_out, accf, sems):
    lvl = lev_ref[0]

    def T(j):
        return tbl_ref[lvl, j]

    cp_a = pltpu.make_async_copy(accf_in, accf, sems.at[0])
    cp_a.start()
    cp_a.wait()
    lane = lax.broadcasted_iota(jnp.int32, (16, 128), 1)
    low_half = lane < 64
    for src, (off, chunk, keep_low) in zip((rxp, rxm, ryp, rym), RECV):
        for k in range(KL):
            t = T(off + k)

            @pl.when(t >= 0)
            def _():
                moved = pltpu.roll(src[k], 64, 1)
                keep = low_half if keep_low else jnp.logical_not(low_half)
                sl = pl.ds(chunk * 128, 128)
                accf[t, :, sl] = accf[t, :, sl] + jnp.where(keep, moved, 0.0)

    for k in range(KL):
        for off, keep_low in ((7, False), (13, True)):
            t = T(off + k)

            @pl.when(t >= 0)
            def _():
                keep = low_half if keep_low else jnp.logical_not(low_half)
                sl = pl.ds(256, 128)
                accf[t, :, sl] = accf[t, :, sl] + jnp.where(keep, zc[k], 0.0)

    cp_w = pltpu.make_async_copy(accf, accf_out, sems.at[1])
    cp_w.start()
    cp_w.wait()


SMEM_SPEC = pl.BlockSpec(memory_space=pltpu.SMEM)
VMEM_SPEC = pl.BlockSpec(memory_space=pltpu.VMEM)
ANY_SPEC = pl.BlockSpec(memory_space=pl.ANY)
LIMITS = pltpu.CompilerParams(vmem_limit_bytes=48 * 1024 * 1024)


def run_compute(forward, lev, tbl, accf, base, cur, dinv, jac, recv, gmat, smat):
    face = jax.ShapeDtypeStruct((KL, 16, 128), jnp.float32)
    return pl.pallas_call(
        functools.partial(compute_kernel, forward),
        out_shape=(jax.ShapeDtypeStruct(cur.shape, jnp.float32), face, face, face),
        in_specs=[SMEM_SPEC, SMEM_SPEC] + [ANY_SPEC] * 5 + [VMEM_SPEC] * 6,
        out_specs=(ANY_SPEC, VMEM_SPEC, VMEM_SPEC, VMEM_SPEC),
        scratch_shapes=[
            pltpu.VMEM((KL,) + accf.shape[1:], jnp.float32),
            pltpu.VMEM((KL,) + dinv.shape[1:], dinv.dtype),
            pltpu.VMEM((KL,) + jac.shape[1:], jnp.float32),
            pltpu.VMEM((KL,) + base.shape[1:], jnp.float32),
            pltpu.VMEM((KL,) + cur.shape[1:], jnp.float32),
            pltpu.SemaphoreType.DMA((5,)),
            pltpu.SemaphoreType.DMA((KL,)),
        ],
        input_output_aliases={4: 0},
        compiler_params=LIMITS,
    )(lev, tbl, accf, base, cur, dinv, jac, *recv, gmat, smat)


def run_update(lev, tbl, accf, recv, zc):
    return pl.pallas_call(
        update_kernel,
        out_shape=jax.ShapeDtypeStruct(accf.shape, jnp.float32),
        in_specs=[SMEM_SPEC, SMEM_SPEC, ANY_SPEC] + [VMEM_SPEC] * 5,
        out_specs=ANY_SPEC,
        scratch_shapes=[pltpu.VMEM(accf.shape, jnp.float32), pltpu.SemaphoreType.DMA((2,))],
        input_output_aliases={2: 0},
        compiler_params=LIMITS,
    )(lev, tbl, accf, *recv, zc)


def shift_along(value, axis, steps):
    count = lax.axis_size(axis)
    pairs = [(source, (source + steps) % count) for source in range(count)]
    return lax.ppermute(value, axis, pairs)


def exchange(sx, sy):
    return (
        shift_along(sx, "gx", 1),
        shift_along(sx, "gx", -1),
        shift_along(sy, "gy", 1),
        shift_along(sy, "gy", -1),
    )


def pick(vec, idx):
    ids = jnp.arange(vec.shape[0], dtype=jnp.int32).reshape((-1,) + (1,) * idx.ndim)
    return jnp.sum(jnp.where(idx[None] == ids, vec.reshape(ids.shape), 0), axis=0)


def pick_row(mat, row):
    ids = jnp.arange(mat.shape[0], dtype=jnp.int32)
    return jnp.sum(jnp.where(ids[:, None] == row, mat, 0), axis=0)


def build_tables(level_counts, slot_count):
    count_x = lax.axis_size("gx")
    count_y = lax.axis_size("gy")
    place_x = lax.axis_index("gx")
    place_y = lax.axis_index("gy")
    coords, where_slot = slot_layout(count_x, count_y, RX, RY, NBZ)
    nbs = [jnp.asarray(step_table(coords, where_slot, dm, st)) for dm, st in DIRECTION_MOVES]
    ends_all = jnp.cumsum(level_counts, axis=1)
    begins_all = ends_all - level_counts
    slots = jnp.arange(slot_count, dtype=jnp.int32)
    all_levels = jnp.sum(slots[None, :, None] >= ends_all[:, None, :], axis=2).astype(jnp.int32)
    own_row = place_x * count_y + place_y
    source_rows = [
        (place_x - 1) % count_x * count_y + place_y,
        (place_x + 1) % count_x * count_y + place_y,
        place_x * count_y + (place_y - 1) % count_y,
        place_x * count_y + (place_y + 1) % count_y,
    ]
    at_edge = [place_x == 0, place_x == count_x - 1, place_y == 0, place_y == count_y - 1]
    my_lv = pick_row(all_levels, own_row)
    levels = jnp.arange(LEVELS, dtype=jnp.int32)
    offsets = jnp.arange(KL, dtype=jnp.int32)

    def window(row, now):
        begin = pick(pick_row(begins_all, row), now)
        return jnp.clip(begin, 0, slot_count - KL)

    win = window(own_row, levels)
    wslots = win[:, None] + offsets[None, :]
    act = pick(my_lv, wslots) == levels[:, None]
    head = [win[:, None], act.astype(jnp.int32)]
    cols_f = list(head)
    cols_b = list(head)
    for d in (4, 5):
        tgt = pick(nbs[d], wslots)
        t_lv = pick(my_lv, tgt)
        live = (tgt >= 0) & act
        cols_f.append(jnp.where(live & (t_lv > levels[:, None]), tgt, -1))
        cols_b.append(jnp.where(live & (t_lv < levels[:, None]), tgt, -1))
    rows = jnp.stack(source_rows)
    row_hot = jnp.arange(ends_all.shape[0], dtype=jnp.int32)[None, :] == rows[:, None]
    src_begins = jnp.sum(jnp.where(row_hot[:, :, None], begins_all[None], 0), axis=1)
    src_levels = jnp.sum(jnp.where(row_hot[:, :, None], all_levels[None], 0), axis=1)
    lv_hot = levels[None, :] == levels[:, None]
    swin = jnp.sum(jnp.where(lv_hot[None], src_begins[:, None, :], 0), axis=2)
    swin = jnp.clip(swin, 0, slot_count - KL)
    sslots = swin[:, :, None] + offsets[None, None, :]
    slot_hot = sslots[..., None] == slots
    s_lv = jnp.sum(jnp.where(slot_hot, src_levels[:, None, None, :], 0), axis=3)
    s_act = s_lv == levels[None, :, None]
    nb_remote = jnp.stack(nbs[:4])
    stepped = jnp.sum(jnp.where(slot_hot, nb_remote[:, None, None, :], 0), axis=3)
    tgt = jnp.where(jnp.stack(at_edge)[:, None, None], stepped, sslots)
    tgt_hot = tgt[..., None] == slots
    t_lv = jnp.sum(jnp.where(tgt_hot, my_lv[None, None, None, :], 0), axis=3)
    live = (tgt >= 0) & s_act
    sent = levels[None, :, None]
    remote_f = jnp.where(live & (t_lv > sent), tgt, -1)
    remote_b = jnp.where(live & (t_lv < sent), tgt, -1)
    none_row = jnp.full((4, 1, KL), -1, jnp.int32)
    remote_f = jnp.concatenate([none_row, remote_f[:, :-1]], axis=1)
    remote_b = jnp.concatenate([remote_b[:, 1:], none_row], axis=1)
    for d in range(4):
        cols_f.append(remote_f[d])
        cols_b.append(remote_b[d])

    def finish(cols):
        table = jnp.concatenate(cols, axis=1).astype(jnp.int32)
        return jnp.pad(table, ((0, 0), (0, TW - table.shape[1])), constant_values=-1)

    return finish(cols_f), finish(cols_b)


def body(right_side, diag_inverse, face_jac, level_counts):
    slot_count = right_side.shape[0]
    unknowns = right_side.shape[1]
    gather_np, scatter_np = face_matrices(SIDE)
    gmat = jnp.asarray(gather_np, dtype=jnp.bfloat16)
    smat = jnp.asarray(scatter_np, dtype=jnp.bfloat16)
    jac = jnp.transpose(face_jac, (3, 0, 1, 2)).reshape(slot_count, NF * unknowns, unknowns)
    tbl_f, tbl_b = build_tables(level_counts, slot_count)
    zero_recv = tuple(jnp.zeros((KL, 16, 128), jnp.float32) for _ in range(4))

    def lev_arr(v):
        return jnp.reshape(jnp.asarray(v, jnp.int32), (1,))

    def sweep(forward, tbl, order, base, cur):
        accf = jnp.zeros((slot_count, unknowns, NF * FW), jnp.float32)
        cur, sx, sy, zc = run_compute(forward, lev_arr(order(0)), tbl, accf, base, cur,
                                      diag_inverse, jac, zero_recv, gmat, smat)

        def step(i, carry):
            accf, cur, sx, sy, zc, prev = carry
            recv = exchange(sx, sy)
            accf = run_update(lev_arr(order(i - 1)), tbl, accf, prev, zc)
            cur, sx, sy, zc = run_compute(forward, lev_arr(order(i)), tbl, accf, base, cur,
                                          diag_inverse, jac, recv, gmat, smat)
            return accf, cur, sx, sy, zc, recv

        carry = (accf, cur, sx, sy, zc, zero_recv)
        return lax.fori_loop(1, LEVELS, step, carry)[1]

    cur = jnp.zeros(right_side.shape, jnp.float32)
    half = sweep(True, tbl_f, lambda i: i, right_side, cur)
    result = sweep(False, tbl_b, lambda i: LEVELS - 1 - i, half, half)
    return result


def solution(mesh):
    return jax.shard_map(
        body,
        mesh=mesh,
        in_specs=(
            P(("gx", "gy"), None, None),
            P(("gx", "gy"), None, None, None),
            P(None, None, None, ("gx", "gy")),
            P(),
        ),
        out_specs=P(("gx", "gy"), None, None),
        check_vma=False,
    )
```

```python
import functools

import jax
import jax.numpy as jnp
import numpy as np
from jax import lax
from jax.experimental import pallas as pl
from jax.experimental.pallas import tpu as pltpu
from jax.sharding import PartitionSpec as P

SIDE = 8
LEVELS = 12
RX = 2
RY = 2
NBZ = 8
KL = 6
NF = 6
FW = SIDE * SIDE
TW = 48

OPPOSITE = (1, 0, 3, 2, 5, 4)
DIRECTION_MOVES = ((0, 1), (0, -1), (1, 1), (1, -1), (2, 1), (2, -1))


def slot_layout(step_x, step_y, count_x, count_y, count_z):
    ordering = sorted(
        (
            (step_x * along_x + step_y * along_y + along_z, along_x, along_y, along_z)
            for along_x in range(count_x)
            for along_y in range(count_y)
            for along_z in range(count_z)
        )
    )
    coords = np.array([record[1:] for record in ordering], dtype=np.int64)
    where_slot = np.zeros((count_x, count_y, count_z), dtype=np.int64)
    where_slot[coords[:, 0], coords[:, 1], coords[:, 2]] = np.arange(len(ordering))
    return (coords, where_slot)


def step_table(coords, where_slot, dimension, offset_step):
    moved = coords.copy()
    moved[:, dimension] += offset_step
    bound_size = where_slot.shape[dimension]
    inside = (moved[:, dimension] >= 0) & (moved[:, dimension] < bound_size)
    clipped = np.clip(moved, 0, np.array(where_slot.shape) - 1)
    target = where_slot[clipped[:, 0], clipped[:, 1], clipped[:, 2]]
    return np.where(inside, target, -1).astype(np.int32)


def face_matrices(edge_cells):
    cell_ids = np.arange(edge_cells**3).reshape(edge_cells, edge_cells, edge_cells)
    layers = [
        cell_ids[edge_cells - 1],
        cell_ids[0],
        cell_ids[:, edge_cells - 1],
        cell_ids[:, 0],
        cell_ids[:, :, edge_cells - 1],
        cell_ids[:, :, 0],
    ]
    outward = np.stack([layer_ids.reshape(-1) for layer_ids in layers])
    cell_total = edge_cells**3
    face_width = edge_cells * edge_cells
    gather = np.zeros((cell_total, NF * face_width), dtype=np.float32)
    for face_index in range(NF):
        gather[outward[face_index], face_index * face_width + np.arange(face_width)] = 1.0
    return gather, np.ascontiguousarray(gather.T)


def split3(x):
    hi = x.astype(jnp.bfloat16)
    rest = x - hi.astype(jnp.float32)
    mid = rest.astype(jnp.bfloat16)
    low = (rest - mid.astype(jnp.float32)).astype(jnp.bfloat16)
    return hi, mid, low


def mm(a, b):
    return jnp.dot(a, b, preferred_element_type=jnp.float32)


def dot_exact01(x, table):
    hi, mid, low = split3(x)
    return mm(hi, table) + mm(mid, table) + mm(low, table)


def split2(x):
    hi = x.astype(jnp.bfloat16)
    return hi, (x - hi.astype(jnp.float32)).astype(jnp.bfloat16)


def dot_full(a, b):
    ah, al = split2(a)
    bh, bl = split2(b)
    return mm(ah, bh) + (mm(ah, bl) + mm(al, bh))


RECV = ((19, 0, False), (25, 0, True), (31, 1, False), (37, 1, True))


def compute_kernel(forward, lev_ref, tbl_ref, accf_hbm, base_hbm, cur_hbm, dinv_hbm, jac_hbm,
                   rxp, rxm, ryp, rym, gmat, smat,
                   cur_out, sx, sy, zc,
                   accw, dbuf, jbuf, bbuf, cbuf, sems, dsems):
    lvl = lev_ref[0]

    def T(j):
        return tbl_ref[lvl, j]

    win = T(0)
    cp_a = pltpu.make_async_copy(accf_hbm.at[pl.ds(win, KL)], accw, sems.at[0])
    cp_a.start()
    cp_d = [pltpu.make_async_copy(dinv_hbm.at[win + k], dbuf.at[k], dsems.at[k])
            for k in range(KL)]
    cp_j = pltpu.make_async_copy(jac_hbm.at[pl.ds(win, KL)], jbuf, sems.at[1])
    cp_b = pltpu.make_async_copy(base_hbm.at[pl.ds(win, KL)], bbuf, sems.at[2])
    cp_c = pltpu.make_async_copy(cur_hbm.at[pl.ds(win, KL)], cbuf, sems.at[3])
    acts = [T(1 + k) > 0 for k in range(KL)]
    for k in range(KL):
        pl.when(acts[k])(cp_d[k].start)
    cp_j.start()
    cp_b.start()
    cp_c.start()

    cp_a.wait()
    lane = lax.broadcasted_iota(jnp.int32, (16, 128), 1)
    low_half = lane < 64

    for src, (off, chunk, keep_low) in zip((rxp, rxm, ryp, rym), RECV):
        for k in range(KL):
            j = T(off + k) - win

            @pl.when((j >= 0) & (j < KL))
            def _():
                moved = pltpu.roll(src[k], 64, 1)
                keep = low_half if keep_low else jnp.logical_not(low_half)
                sl = pl.ds(chunk * 128, 128)
                accw[j, :, sl] = accw[j, :, sl] + jnp.where(keep, moved, 0.0)

    cp_j.wait()
    cp_b.wait()
    cp_c.wait()

    nr = KL * 16
    acc_win = accw[...].reshape(nr, NF * FW)
    lower = dot_exact01(acc_win, smat[...])
    base = bbuf[...].reshape(nr, SIDE**3)

    for k in range(KL):

        @pl.when(acts[k])
        def _():
            cp_d[k].wait()
            bk = base[16 * k:16 * (k + 1)]
            lk = lower[16 * k:16 * (k + 1)]
            vk = bk - lk if forward else lk
            parts = []
            for c0 in range(0, 16, 4):
                d = dbuf[k, c0:c0 + 4].astype(jnp.float32)
                parts.append(jnp.sum(d * vk[None], axis=1))
            y = jnp.concatenate(parts, axis=0)
            cbuf[k] = y if forward else bk - y

    cp_o = pltpu.make_async_copy(cbuf, cur_out.at[pl.ds(win, KL)], sems.at[4])
    cp_o.start()
    new = cbuf[...].reshape(nr, SIDE**3)
    sx[...] = jnp.zeros(sx.shape, jnp.float32)
    sy[...] = jnp.zeros(sy.shape, jnp.float32)
    zc[...] = jnp.zeros(zc.shape, jnp.float32)

    faces = dot_exact01(new, gmat[...])
    flane = lax.broadcasted_iota(jnp.int32, (16, NF * FW), 1) // FW
    for k in range(KL):

        @pl.when(acts[k])
        def _():
            prod = dot_full(jbuf[k], faces[16 * k:16 * (k + 1)])
            inc = jnp.zeros((16, NF * FW), jnp.float32)
            for d in range(NF):
                inc = inc + jnp.where(flane == d, prod[16 * d:16 * (d + 1)], 0.0)
            sx[k] = inc[:, 0:128]
            sy[k] = inc[:, 128:256]
            zc[k] = pltpu.roll(inc[:, 256:384], 64, 1)

    cp_o.wait()


def update_kernel(lev_ref, tbl_ref, accf_in, rxp, rxm, ryp, rym, zc, accf_out, accf, sems):
    lvl = lev_ref[0]

    def T(j):
        return tbl_ref[lvl, j]

    cp_a = pltpu.make_async_copy(accf_in, accf, sems.at[0])
    cp_a.start()
    cp_a.wait()
    lane = lax.broadcasted_iota(jnp.int32, (16, 128), 1)
    low_half = lane < 64
    for src, (off, chunk, keep_low) in zip((rxp, rxm, ryp, rym), RECV):
        for k in range(KL):
            t = T(off + k)

            @pl.when(t >= 0)
            def _():
                moved = pltpu.roll(src[k], 64, 1)
                keep = low_half if keep_low else jnp.logical_not(low_half)
                sl = pl.ds(chunk * 128, 128)
                accf[t, :, sl] = accf[t, :, sl] + jnp.where(keep, moved, 0.0)

    for k in range(KL):
        for off, keep_low in ((7, False), (13, True)):
            t = T(off + k)

            @pl.when(t >= 0)
            def _():
                keep = low_half if keep_low else jnp.logical_not(low_half)
                sl = pl.ds(256, 128)
                accf[t, :, sl] = accf[t, :, sl] + jnp.where(keep, zc[k], 0.0)

    cp_w = pltpu.make_async_copy(accf, accf_out, sems.at[1])
    cp_w.start()
    cp_w.wait()


SMEM_SPEC = pl.BlockSpec(memory_space=pltpu.SMEM)
VMEM_SPEC = pl.BlockSpec(memory_space=pltpu.VMEM)
ANY_SPEC = pl.BlockSpec(memory_space=pl.ANY)
LIMITS = pltpu.CompilerParams(vmem_limit_bytes=48 * 1024 * 1024)


def run_compute(forward, lev, tbl, accf, base, cur, dinv, jac, recv, gmat, smat):
    face = jax.ShapeDtypeStruct((KL, 16, 128), jnp.float32)
    return pl.pallas_call(
        functools.partial(compute_kernel, forward),
        out_shape=(jax.ShapeDtypeStruct(cur.shape, jnp.float32), face, face, face),
        in_specs=[SMEM_SPEC, SMEM_SPEC] + [ANY_SPEC] * 5 + [VMEM_SPEC] * 6,
        out_specs=(ANY_SPEC, VMEM_SPEC, VMEM_SPEC, VMEM_SPEC),
        scratch_shapes=[
            pltpu.VMEM((KL,) + accf.shape[1:], jnp.float32),
            pltpu.VMEM((KL,) + dinv.shape[1:], dinv.dtype),
            pltpu.VMEM((KL,) + jac.shape[1:], jnp.float32),
            pltpu.VMEM((KL,) + base.shape[1:], jnp.float32),
            pltpu.VMEM((KL,) + cur.shape[1:], jnp.float32),
            pltpu.SemaphoreType.DMA((5,)),
            pltpu.SemaphoreType.DMA((KL,)),
        ],
        input_output_aliases={4: 0},
        compiler_params=LIMITS,
    )(lev, tbl, accf, base, cur, dinv, jac, *recv, gmat, smat)


def run_update(lev, tbl, accf, recv, zc):
    return pl.pallas_call(
        update_kernel,
        out_shape=jax.ShapeDtypeStruct(accf.shape, jnp.float32),
        in_specs=[SMEM_SPEC, SMEM_SPEC, ANY_SPEC] + [VMEM_SPEC] * 5,
        out_specs=ANY_SPEC,
        scratch_shapes=[pltpu.VMEM(accf.shape, jnp.float32), pltpu.SemaphoreType.DMA((2,))],
        input_output_aliases={2: 0},
        compiler_params=LIMITS,
    )(lev, tbl, accf, *recv, zc)


def shift_along(value, axis, steps):
    count = lax.axis_size(axis)
    pairs = [(source, (source + steps) % count) for source in range(count)]
    return lax.ppermute(value, axis, pairs)


def exchange(sx, sy):
    return (
        shift_along(sx, "gx", 1),
        shift_along(sx, "gx", -1),
        shift_along(sy, "gy", 1),
        shift_along(sy, "gy", -1),
    )


def pick(vec, idx):
    ids = jnp.arange(vec.shape[0], dtype=jnp.int32).reshape((-1,) + (1,) * idx.ndim)
    return jnp.sum(jnp.where(idx[None] == ids, vec.reshape(ids.shape), 0), axis=0)


def pick_row(mat, row):
    ids = jnp.arange(mat.shape[0], dtype=jnp.int32)
    return jnp.sum(jnp.where(ids[:, None] == row, mat, 0), axis=0)


def build_tables(level_counts, slot_count):
    count_x = lax.axis_size("gx")
    count_y = lax.axis_size("gy")
    place_x = lax.axis_index("gx")
    place_y = lax.axis_index("gy")
    coords, where_slot = slot_layout(count_x, count_y, RX, RY, NBZ)
    nbs = [jnp.asarray(step_table(coords, where_slot, dm, st)) for dm, st in DIRECTION_MOVES]
    ends_all = jnp.cumsum(level_counts, axis=1)
    begins_all = ends_all - level_counts
    slots = jnp.arange(slot_count, dtype=jnp.int32)
    all_levels = jnp.sum(slots[None, :, None] >= ends_all[:, None, :], axis=2).astype(jnp.int32)
    own_row = place_x * count_y + place_y
    source_rows = [
        (place_x - 1) % count_x * count_y + place_y,
        (place_x + 1) % count_x * count_y + place_y,
        place_x * count_y + (place_y - 1) % count_y,
        place_x * count_y + (place_y + 1) % count_y,
    ]
    at_edge = [place_x == 0, place_x == count_x - 1, place_y == 0, place_y == count_y - 1]
    my_lv = pick_row(all_levels, own_row)
    levels = jnp.arange(LEVELS, dtype=jnp.int32)
    offsets = jnp.arange(KL, dtype=jnp.int32)

    def window(row, now):
        begin = pick(pick_row(begins_all, row), now)
        return jnp.clip(begin, 0, slot_count - KL)

    win = window(own_row, levels)
    wslots = win[:, None] + offsets[None, :]
    act = pick(my_lv, wslots) == levels[:, None]
    head = [win[:, None], act.astype(jnp.int32)]
    cols_f = list(head)
    cols_b = list(head)
    for d in (4, 5):
        tgt = pick(nbs[d], wslots)
        t_lv = pick(my_lv, tgt)
        live = (tgt >= 0) & act
        cols_f.append(jnp.where(live & (t_lv > levels[:, None]), tgt, -1))
        cols_b.append(jnp.where(live & (t_lv < levels[:, None]), tgt, -1))
    rows = jnp.stack(source_rows)
    row_hot = jnp.arange(ends_all.shape[0], dtype=jnp.int32)[None, :] == rows[:, None]
    src_begins = jnp.sum(jnp.where(row_hot[:, :, None], begins_all[None], 0), axis=1)
    src_levels = jnp.sum(jnp.where(row_hot[:, :, None], all_levels[None], 0), axis=1)
    lv_hot = levels[None, :] == levels[:, None]
    swin = jnp.sum(jnp.where(lv_hot[None], src_begins[:, None, :], 0), axis=2)
    swin = jnp.clip(swin, 0, slot_count - KL)
    sslots = swin[:, :, None] + offsets[None, None, :]
    slot_hot = sslots[..., None] == slots
    s_lv = jnp.sum(jnp.where(slot_hot, src_levels[:, None, None, :], 0), axis=3)
    s_act = s_lv == levels[None, :, None]
    nb_remote = jnp.stack(nbs[:4])
    stepped = jnp.sum(jnp.where(slot_hot, nb_remote[:, None, None, :], 0), axis=3)
    tgt = jnp.where(jnp.stack(at_edge)[:, None, None], stepped, sslots)
    tgt_hot = tgt[..., None] == slots
    t_lv = jnp.sum(jnp.where(tgt_hot, my_lv[None, None, None, :], 0), axis=3)
    live = (tgt >= 0) & s_act
    sent = levels[None, :, None]
    remote_f = jnp.where(live & (t_lv > sent), tgt, -1)
    remote_b = jnp.where(live & (t_lv < sent), tgt, -1)
    none_row = jnp.full((4, 1, KL), -1, jnp.int32)
    remote_f = jnp.concatenate([none_row, remote_f[:, :-1]], axis=1)
    remote_b = jnp.concatenate([remote_b[:, 1:], none_row], axis=1)
    for d in range(4):
        cols_f.append(remote_f[d])
        cols_b.append(remote_b[d])

    def finish(cols):
        table = jnp.concatenate(cols, axis=1).astype(jnp.int32)
        return jnp.pad(table, ((0, 0), (0, TW - table.shape[1])), constant_values=-1)

    return finish(cols_f), finish(cols_b)


def body(right_side, diag_inverse, face_jac, level_counts):
    slot_count = right_side.shape[0]
    unknowns = right_side.shape[1]
    gather_np, scatter_np = face_matrices(SIDE)
    gmat = jnp.asarray(gather_np, dtype=jnp.bfloat16)
    smat = jnp.asarray(scatter_np, dtype=jnp.bfloat16)
    jac = jnp.transpose(face_jac, (3, 0, 1, 2)).reshape(slot_count, NF * unknowns, unknowns)
    tbl_f, tbl_b = build_tables(level_counts, slot_count)
    zero_recv = tuple(jnp.zeros((KL, 16, 128), jnp.float32) for _ in range(4))

    def lev_arr(v):
        return jnp.reshape(jnp.asarray(v, jnp.int32), (1,))

    def sweep(forward, tbl, order, base, carry):

        def step(i, carry):
            accf, cur, sx, sy, zc, prev = carry
            recv = exchange(sx, sy)
            accf = run_update(lev_arr(order(i - 1)), tbl, accf, prev, zc)
            cur, sx, sy, zc = run_compute(forward, lev_arr(order(i)), tbl, accf, base, cur,
                                          diag_inverse, jac, recv, gmat, smat)
            return accf, cur, sx, sy, zc, recv

        return lax.fori_loop(1, LEVELS, step, carry)

    def blank_acc():
        return jnp.zeros((slot_count, unknowns, NF * FW), jnp.float32)

    cur = jnp.zeros(right_side.shape, jnp.float32)
    cur, sx, sy, zc = run_compute(True, lev_arr(0), tbl_f, blank_acc(), right_side, cur,
                                  diag_inverse, jac, zero_recv, gmat, smat)
    carry = (blank_acc(), cur, sx, sy, zc, zero_recv)
    _, half, sx, sy, zc, _ = sweep(True, tbl_f, lambda i: i, right_side, carry)
    carry = (blank_acc(), half, sx, sy, zc, zero_recv)
    result = sweep(False, tbl_b, lambda i: LEVELS - 1 - i, half, carry)[1]
    return result


def solution(mesh):
    return jax.shard_map(
        body,
        mesh=mesh,
        in_specs=(
            P(("gx", "gy"), None, None),
            P(("gx", "gy"), None, None, None),
            P(None, None, None, ("gx", "gy")),
            P(),
        ),
        out_specs=P(("gx", "gy"), None, None),
        check_vma=False,
    )
```

```python
import functools

import jax
import jax.numpy as jnp
import numpy as np
from jax import lax
from jax.experimental import pallas as pl
from jax.experimental.pallas import tpu as pltpu
from jax.sharding import PartitionSpec as P

SIDE = 8
LEVELS = 12
RX = 2
RY = 2
NBZ = 8
KL = 6
NF = 6
FW = SIDE * SIDE
TW = 48

OPPOSITE = (1, 0, 3, 2, 5, 4)
DIRECTION_MOVES = ((0, 1), (0, -1), (1, 1), (1, -1), (2, 1), (2, -1))


def slot_layout(step_x, step_y, count_x, count_y, count_z):
    ordering = sorted(
        (
            (step_x * along_x + step_y * along_y + along_z, along_x, along_y, along_z)
            for along_x in range(count_x)
            for along_y in range(count_y)
            for along_z in range(count_z)
        )
    )
    coords = np.array([record[1:] for record in ordering], dtype=np.int64)
    where_slot = np.zeros((count_x, count_y, count_z), dtype=np.int64)
    where_slot[coords[:, 0], coords[:, 1], coords[:, 2]] = np.arange(len(ordering))
    return (coords, where_slot)


def step_table(coords, where_slot, dimension, offset_step):
    moved = coords.copy()
    moved[:, dimension] += offset_step
    bound_size = where_slot.shape[dimension]
    inside = (moved[:, dimension] >= 0) & (moved[:, dimension] < bound_size)
    clipped = np.clip(moved, 0, np.array(where_slot.shape) - 1)
    target = where_slot[clipped[:, 0], clipped[:, 1], clipped[:, 2]]
    return np.where(inside, target, -1).astype(np.int32)


def face_matrices(edge_cells):
    cell_ids = np.arange(edge_cells**3).reshape(edge_cells, edge_cells, edge_cells)
    layers = [
        cell_ids[edge_cells - 1],
        cell_ids[0],
        cell_ids[:, edge_cells - 1],
        cell_ids[:, 0],
        cell_ids[:, :, edge_cells - 1],
        cell_ids[:, :, 0],
    ]
    outward = np.stack([layer_ids.reshape(-1) for layer_ids in layers])
    cell_total = edge_cells**3
    face_width = edge_cells * edge_cells
    gather = np.zeros((cell_total, NF * face_width), dtype=np.float32)
    for face_index in range(NF):
        gather[outward[face_index], face_index * face_width + np.arange(face_width)] = 1.0
    return gather, np.ascontiguousarray(gather.T)


def split3(x):
    hi = x.astype(jnp.bfloat16)
    rest = x - hi.astype(jnp.float32)
    mid = rest.astype(jnp.bfloat16)
    low = (rest - mid.astype(jnp.float32)).astype(jnp.bfloat16)
    return hi, mid, low


def mm(a, b):
    return jnp.dot(a, b, preferred_element_type=jnp.float32)


def dot_exact01(x, table):
    hi, mid, low = split3(x)
    return mm(hi, table) + mm(mid, table) + mm(low, table)


def split2(x):
    hi = x.astype(jnp.bfloat16)
    return hi, (x - hi.astype(jnp.float32)).astype(jnp.bfloat16)


def dot_full(a, b):
    ah, al = split2(a)
    bh, bl = split2(b)
    return mm(ah, bh) + (mm(ah, bl) + mm(al, bh))


RECV = ((19, 0, False), (25, 0, True), (31, 1, False), (37, 1, True))


def compute_kernel(forward, lev_ref, tbl_ref, accf_hbm, base_hbm, cur_hbm, dinv_hbm, jac_hbm,
                   rxp, rxm, ryp, rym, gmat, smat,
                   cur_out, sx, sy, zc,
                   accw, dbuf, jbuf, bbuf, cbuf, sems, dsems):
    lvl = lev_ref[0]

    def T(j):
        return tbl_ref[lvl, j]

    win = T(0)
    cp_a = pltpu.make_async_copy(accf_hbm.at[pl.ds(win, KL)], accw, sems.at[0])
    cp_a.start()
    cp_d = [pltpu.make_async_copy(dinv_hbm.at[win + k], dbuf.at[k], dsems.at[k])
            for k in range(KL)]
    cp_j = pltpu.make_async_copy(jac_hbm.at[pl.ds(win, KL)], jbuf, sems.at[1])
    cp_b = pltpu.make_async_copy(base_hbm.at[pl.ds(win, KL)], bbuf, sems.at[2])
    cp_c = pltpu.make_async_copy(cur_hbm.at[pl.ds(win, KL)], cbuf, sems.at[3])
    acts = [T(1 + k) > 0 for k in range(KL)]
    for k in range(KL):
        pl.when(acts[k])(cp_d[k].start)
    cp_j.start()
    if forward:
        cp_b.start()
    cp_c.start()

    cp_a.wait()
    lane = lax.broadcasted_iota(jnp.int32, (16, 128), 1)
    low_half = lane < 64

    for src, (off, chunk, keep_low) in zip((rxp, rxm, ryp, rym), RECV):
        for k in range(KL):
            j = T(off + k) - win

            @pl.when((j >= 0) & (j < KL))
            def _():
                moved = pltpu.roll(src[k], 64, 1)
                keep = low_half if keep_low else jnp.logical_not(low_half)
                sl = pl.ds(chunk * 128, 128)
                accw[j, :, sl] = accw[j, :, sl] + jnp.where(keep, moved, 0.0)

    cp_j.wait()
    if forward:
        cp_b.wait()
    cp_c.wait()

    nr = KL * 16
    acc_win = accw[...].reshape(nr, NF * FW)
    lower = dot_exact01(acc_win, smat[...])
    base = (bbuf if forward else cbuf)[...].reshape(nr, SIDE**3)

    for k in range(KL):

        @pl.when(acts[k])
        def _():
            cp_d[k].wait()
            bk = base[16 * k:16 * (k + 1)]
            lk = lower[16 * k:16 * (k + 1)]
            vk = bk - lk if forward else lk
            parts = []
            for c0 in range(0, 16, 4):
                d = dbuf[k, c0:c0 + 4].astype(jnp.float32)
                parts.append(jnp.sum(d * vk[None], axis=1))
            y = jnp.concatenate(parts, axis=0)
            cbuf[k] = y if forward else bk - y

    cp_o = pltpu.make_async_copy(cbuf, cur_out.at[pl.ds(win, KL)], sems.at[4])
    cp_o.start()
    new = cbuf[...].reshape(nr, SIDE**3)
    sx[...] = jnp.zeros(sx.shape, jnp.float32)
    sy[...] = jnp.zeros(sy.shape, jnp.float32)
    zc[...] = jnp.zeros(zc.shape, jnp.float32)

    faces = dot_exact01(new, gmat[...])
    flane = lax.broadcasted_iota(jnp.int32, (16, NF * FW), 1) // FW
    for k in range(KL):

        @pl.when(acts[k])
        def _():
            prod = dot_full(jbuf[k], faces[16 * k:16 * (k + 1)])
            inc = jnp.zeros((16, NF * FW), jnp.float32)
            for d in range(NF):
                inc = inc + jnp.where(flane == d, prod[16 * d:16 * (d + 1)], 0.0)
            sx[k] = inc[:, 0:128]
            sy[k] = inc[:, 128:256]
            zc[k] = pltpu.roll(inc[:, 256:384], 64, 1)

    cp_o.wait()


def update_kernel(lev_ref, tbl_ref, accf_in, rxp, rxm, ryp, rym, zc, accf_out, accf, sems):
    lvl = lev_ref[0]

    def T(j):
        return tbl_ref[lvl, j]

    cp_a = pltpu.make_async_copy(accf_in, accf, sems.at[0])
    cp_a.start()
    cp_a.wait()
    lane = lax.broadcasted_iota(jnp.int32, (16, 128), 1)
    low_half = lane < 64
    for src, (off, chunk, keep_low) in zip((rxp, rxm, ryp, rym), RECV):
        for k in range(KL):
            t = T(off + k)

            @pl.when(t >= 0)
            def _():
                moved = pltpu.roll(src[k], 64, 1)
                keep = low_half if keep_low else jnp.logical_not(low_half)
                sl = pl.ds(chunk * 128, 128)
                accf[t, :, sl] = accf[t, :, sl] + jnp.where(keep, moved, 0.0)

    for k in range(KL):
        for off, keep_low in ((7, False), (13, True)):
            t = T(off + k)

            @pl.when(t >= 0)
            def _():
                keep = low_half if keep_low else jnp.logical_not(low_half)
                sl = pl.ds(256, 128)
                accf[t, :, sl] = accf[t, :, sl] + jnp.where(keep, zc[k], 0.0)

    cp_w = pltpu.make_async_copy(accf, accf_out, sems.at[1])
    cp_w.start()
    cp_w.wait()


SMEM_SPEC = pl.BlockSpec(memory_space=pltpu.SMEM)
VMEM_SPEC = pl.BlockSpec(memory_space=pltpu.VMEM)
ANY_SPEC = pl.BlockSpec(memory_space=pl.ANY)
LIMITS = pltpu.CompilerParams(vmem_limit_bytes=48 * 1024 * 1024)


def run_compute(forward, lev, tbl, accf, base, cur, dinv, jac, recv, gmat, smat):
    face = jax.ShapeDtypeStruct((KL, 16, 128), jnp.float32)
    return pl.pallas_call(
        functools.partial(compute_kernel, forward),
        out_shape=(jax.ShapeDtypeStruct(cur.shape, jnp.float32), face, face, face),
        in_specs=[SMEM_SPEC, SMEM_SPEC] + [ANY_SPEC] * 5 + [VMEM_SPEC] * 6,
        out_specs=(ANY_SPEC, VMEM_SPEC, VMEM_SPEC, VMEM_SPEC),
        scratch_shapes=[
            pltpu.VMEM((KL,) + accf.shape[1:], jnp.float32),
            pltpu.VMEM((KL,) + dinv.shape[1:], dinv.dtype),
            pltpu.VMEM((KL,) + jac.shape[1:], jnp.float32),
            pltpu.VMEM((KL,) + base.shape[1:], jnp.float32),
            pltpu.VMEM((KL,) + cur.shape[1:], jnp.float32),
            pltpu.SemaphoreType.DMA((5,)),
            pltpu.SemaphoreType.DMA((KL,)),
        ],
        input_output_aliases={4: 0},
        compiler_params=LIMITS,
    )(lev, tbl, accf, base, cur, dinv, jac, *recv, gmat, smat)


def run_update(lev, tbl, accf, recv, zc):
    return pl.pallas_call(
        update_kernel,
        out_shape=jax.ShapeDtypeStruct(accf.shape, jnp.float32),
        in_specs=[SMEM_SPEC, SMEM_SPEC, ANY_SPEC] + [VMEM_SPEC] * 5,
        out_specs=ANY_SPEC,
        scratch_shapes=[pltpu.VMEM(accf.shape, jnp.float32), pltpu.SemaphoreType.DMA((2,))],
        input_output_aliases={2: 0},
        compiler_params=LIMITS,
    )(lev, tbl, accf, *recv, zc)


def shift_along(value, axis, steps):
    count = lax.axis_size(axis)
    pairs = [(source, (source + steps) % count) for source in range(count)]
    return lax.ppermute(value, axis, pairs)


def exchange(sx, sy):
    return (
        shift_along(sx, "gx", 1),
        shift_along(sx, "gx", -1),
        shift_along(sy, "gy", 1),
        shift_along(sy, "gy", -1),
    )


def pick(vec, idx):
    ids = jnp.arange(vec.shape[0], dtype=jnp.int32).reshape((-1,) + (1,) * idx.ndim)
    return jnp.sum(jnp.where(idx[None] == ids, vec.reshape(ids.shape), 0), axis=0)


def pick_row(mat, row):
    ids = jnp.arange(mat.shape[0], dtype=jnp.int32)
    return jnp.sum(jnp.where(ids[:, None] == row, mat, 0), axis=0)


def build_tables(level_counts, slot_count):
    count_x = lax.axis_size("gx")
    count_y = lax.axis_size("gy")
    place_x = lax.axis_index("gx")
    place_y = lax.axis_index("gy")
    coords, where_slot = slot_layout(count_x, count_y, RX, RY, NBZ)
    nbs = [jnp.asarray(step_table(coords, where_slot, dm, st)) for dm, st in DIRECTION_MOVES]
    ends_all = jnp.cumsum(level_counts, axis=1)
    begins_all = ends_all - level_counts
    slots = jnp.arange(slot_count, dtype=jnp.int32)
    all_levels = jnp.sum(slots[None, :, None] >= ends_all[:, None, :], axis=2).astype(jnp.int32)
    own_row = place_x * count_y + place_y
    source_rows = [
        (place_x - 1) % count_x * count_y + place_y,
        (place_x + 1) % count_x * count_y + place_y,
        place_x * count_y + (place_y - 1) % count_y,
        place_x * count_y + (place_y + 1) % count_y,
    ]
    at_edge = [place_x == 0, place_x == count_x - 1, place_y == 0, place_y == count_y - 1]
    my_lv = pick_row(all_levels, own_row)
    levels = jnp.arange(LEVELS, dtype=jnp.int32)
    offsets = jnp.arange(KL, dtype=jnp.int32)

    def window(row, now):
        begin = pick(pick_row(begins_all, row), now)
        return jnp.clip(begin, 0, slot_count - KL)

    win = window(own_row, levels)
    wslots = win[:, None] + offsets[None, :]
    act = pick(my_lv, wslots) == levels[:, None]
    head = [win[:, None], act.astype(jnp.int32)]
    cols_f = list(head)
    cols_b = list(head)
    for d in (4, 5):
        tgt = pick(nbs[d], wslots)
        t_lv = pick(my_lv, tgt)
        live = (tgt >= 0) & act
        cols_f.append(jnp.where(live & (t_lv > levels[:, None]), tgt, -1))
        cols_b.append(jnp.where(live & (t_lv < levels[:, None]), tgt, -1))
    rows = jnp.stack(source_rows)
    row_hot = jnp.arange(ends_all.shape[0], dtype=jnp.int32)[None, :] == rows[:, None]
    src_begins = jnp.sum(jnp.where(row_hot[:, :, None], begins_all[None], 0), axis=1)
    src_levels = jnp.sum(jnp.where(row_hot[:, :, None], all_levels[None], 0), axis=1)
    lv_hot = levels[None, :] == levels[:, None]
    swin = jnp.sum(jnp.where(lv_hot[None], src_begins[:, None, :], 0), axis=2)
    swin = jnp.clip(swin, 0, slot_count - KL)
    sslots = swin[:, :, None] + offsets[None, None, :]
    slot_hot = sslots[..., None] == slots
    s_lv = jnp.sum(jnp.where(slot_hot, src_levels[:, None, None, :], 0), axis=3)
    s_act = s_lv == levels[None, :, None]
    nb_remote = jnp.stack(nbs[:4])
    stepped = jnp.sum(jnp.where(slot_hot, nb_remote[:, None, None, :], 0), axis=3)
    tgt = jnp.where(jnp.stack(at_edge)[:, None, None], stepped, sslots)
    tgt_hot = tgt[..., None] == slots
    t_lv = jnp.sum(jnp.where(tgt_hot, my_lv[None, None, None, :], 0), axis=3)
    live = (tgt >= 0) & s_act
    sent = levels[None, :, None]
    remote_f = jnp.where(live & (t_lv > sent), tgt, -1)
    remote_b = jnp.where(live & (t_lv < sent), tgt, -1)
    none_row = jnp.full((4, 1, KL), -1, jnp.int32)
    remote_f = jnp.concatenate([none_row, remote_f[:, :-1]], axis=1)
    remote_b = jnp.concatenate([remote_b[:, 1:], none_row], axis=1)
    for d in range(4):
        cols_f.append(remote_f[d])
        cols_b.append(remote_b[d])

    def finish(cols):
        table = jnp.concatenate(cols, axis=1).astype(jnp.int32)
        return jnp.pad(table, ((0, 0), (0, TW - table.shape[1])), constant_values=-1)

    return finish(cols_f), finish(cols_b)


def body(right_side, diag_inverse, face_jac, level_counts):
    slot_count = right_side.shape[0]
    unknowns = right_side.shape[1]
    gather_np, scatter_np = face_matrices(SIDE)
    gmat = jnp.asarray(gather_np, dtype=jnp.bfloat16)
    smat = jnp.asarray(scatter_np, dtype=jnp.bfloat16)
    jac = jnp.transpose(face_jac, (3, 0, 1, 2)).reshape(slot_count, NF * unknowns, unknowns)
    tbl_f, tbl_b = build_tables(level_counts, slot_count)
    zero_recv = tuple(jnp.zeros((KL, 16, 128), jnp.float32) for _ in range(4))

    def lev_arr(v):
        return jnp.reshape(jnp.asarray(v, jnp.int32), (1,))

    def sweep(forward, tbl, order, base, carry):

        def step(i, carry):
            accf, cur, sx, sy, zc, prev = carry
            recv = exchange(sx, sy)
            accf = run_update(lev_arr(order(i - 1)), tbl, accf, prev, zc)
            cur, sx, sy, zc = run_compute(forward, lev_arr(order(i)), tbl, accf, base, cur,
                                          diag_inverse, jac, recv, gmat, smat)
            return accf, cur, sx, sy, zc, recv

        return lax.fori_loop(1, LEVELS, step, carry)

    def blank_acc():
        return jnp.zeros((slot_count, unknowns, NF * FW), jnp.float32)

    cur = jnp.zeros(right_side.shape, jnp.float32)
    cur, sx, sy, zc = run_compute(True, lev_arr(0), tbl_f, blank_acc(), right_side, cur,
                                  diag_inverse, jac, zero_recv, gmat, smat)
    carry = (blank_acc(), cur, sx, sy, zc, zero_recv)
    _, half, sx, sy, zc, _ = sweep(True, tbl_f, lambda i: i, right_side, carry)
    carry = (blank_acc(), half, sx, sy, zc, zero_recv)
    result = sweep(False, tbl_b, lambda i: LEVELS - 1 - i, right_side, carry)[1]
    return result


def solution(mesh):
    return jax.shard_map(
        body,
        mesh=mesh,
        in_specs=(
            P(("gx", "gy"), None, None),
            P(("gx", "gy"), None, None, None),
            P(None, None, None, ("gx", "gy")),
            P(),
        ),
        out_specs=P(("gx", "gy"), None, None),
        check_vma=False,
    )
```

```python
import functools

import jax
import jax.numpy as jnp
import numpy as np
from jax import lax
from jax.experimental import pallas as pl
from jax.experimental.pallas import tpu as pltpu
from jax.sharding import PartitionSpec as P

SIDE = 8
LEVELS = 12
RX = 2
RY = 2
NBZ = 8
KL = 6
NF = 6
FW = SIDE * SIDE
TW = 48

OPPOSITE = (1, 0, 3, 2, 5, 4)
DIRECTION_MOVES = ((0, 1), (0, -1), (1, 1), (1, -1), (2, 1), (2, -1))


def slot_layout(step_x, step_y, count_x, count_y, count_z):
    ordering = sorted(
        (
            (step_x * along_x + step_y * along_y + along_z, along_x, along_y, along_z)
            for along_x in range(count_x)
            for along_y in range(count_y)
            for along_z in range(count_z)
        )
    )
    coords = np.array([record[1:] for record in ordering], dtype=np.int64)
    where_slot = np.zeros((count_x, count_y, count_z), dtype=np.int64)
    where_slot[coords[:, 0], coords[:, 1], coords[:, 2]] = np.arange(len(ordering))
    return (coords, where_slot)


def step_table(coords, where_slot, dimension, offset_step):
    moved = coords.copy()
    moved[:, dimension] += offset_step
    bound_size = where_slot.shape[dimension]
    inside = (moved[:, dimension] >= 0) & (moved[:, dimension] < bound_size)
    clipped = np.clip(moved, 0, np.array(where_slot.shape) - 1)
    target = where_slot[clipped[:, 0], clipped[:, 1], clipped[:, 2]]
    return np.where(inside, target, -1).astype(np.int32)


def face_matrices(edge_cells):
    cell_ids = np.arange(edge_cells**3).reshape(edge_cells, edge_cells, edge_cells)
    layers = [
        cell_ids[edge_cells - 1],
        cell_ids[0],
        cell_ids[:, edge_cells - 1],
        cell_ids[:, 0],
        cell_ids[:, :, edge_cells - 1],
        cell_ids[:, :, 0],
    ]
    outward = np.stack([layer_ids.reshape(-1) for layer_ids in layers])
    cell_total = edge_cells**3
    face_width = edge_cells * edge_cells
    gather = np.zeros((cell_total, NF * face_width), dtype=np.float32)
    for face_index in range(NF):
        gather[outward[face_index], face_index * face_width + np.arange(face_width)] = 1.0
    return gather, np.ascontiguousarray(gather.T)


def split3(x):
    hi = x.astype(jnp.bfloat16)
    rest = x - hi.astype(jnp.float32)
    mid = rest.astype(jnp.bfloat16)
    low = (rest - mid.astype(jnp.float32)).astype(jnp.bfloat16)
    return hi, mid, low


def mm(a, b):
    return jnp.dot(a, b, preferred_element_type=jnp.float32)


def dot_exact01(x, table):
    hi, mid, low = split3(x)
    return mm(hi, table) + mm(mid, table) + mm(low, table)


def split2(x):
    hi = x.astype(jnp.bfloat16)
    return hi, (x - hi.astype(jnp.float32)).astype(jnp.bfloat16)


def dot_full(a, b):
    ah, al = split2(a)
    bh, bl = split2(b)
    return mm(ah, bh) + (mm(ah, bl) + mm(al, bh))


RECV = ((19, 0, False), (25, 0, True), (31, 1, False), (37, 1, True))


def compute_kernel(forward, lev_ref, tbl_ref, accf_hbm, base_hbm, cur_hbm, dinv_hbm, jac_hbm,
                   rxp, rxm, ryp, rym, gmat, smat,
                   cur_out, sx, sy, zc,
                   accw, dbuf, jbuf, bbuf, cbuf, gbuf, sbuf, sems, dsems):
    lvl = lev_ref[0]

    def T(j):
        return tbl_ref[lvl, j]

    win = T(0)
    cp_a = pltpu.make_async_copy(accf_hbm.at[pl.ds(win, KL)], accw, sems.at[0])
    cp_a.start()
    cp_d = [pltpu.make_async_copy(dinv_hbm.at[win + k], dbuf.at[k], dsems.at[k])
            for k in range(KL)]
    cp_j = pltpu.make_async_copy(jac_hbm.at[pl.ds(win, KL)], jbuf, sems.at[1])
    cp_b = pltpu.make_async_copy(base_hbm.at[pl.ds(win, KL)], bbuf, sems.at[2])
    cp_c = pltpu.make_async_copy(cur_hbm.at[pl.ds(win, KL)], cbuf, sems.at[3])
    cp_s = pltpu.make_async_copy(smat, sbuf, sems.at[5])
    cp_g = pltpu.make_async_copy(gmat, gbuf, sems.at[6])
    cp_s.start()
    cp_g.start()
    acts = [T(1 + k) > 0 for k in range(KL)]
    for k in range(KL):
        pl.when(acts[k])(cp_d[k].start)
    cp_j.start()
    cp_b.start()
    cp_c.start()

    cp_a.wait()
    lane = lax.broadcasted_iota(jnp.int32, (16, 128), 1)
    low_half = lane < 64

    for src, (off, chunk, keep_low) in zip((rxp, rxm, ryp, rym), RECV):
        for k in range(KL):
            j = T(off + k) - win

            @pl.when((j >= 0) & (j < KL))
            def _():
                moved = pltpu.roll(src[k], 64, 1)
                keep = low_half if keep_low else jnp.logical_not(low_half)
                sl = pl.ds(chunk * 128, 128)
                accw[j, :, sl] = accw[j, :, sl] + jnp.where(keep, moved, 0.0)

    cp_j.wait()
    cp_b.wait()
    cp_c.wait()

    nr = KL * 16
    acc_win = accw[...].reshape(nr, NF * FW)
    cp_s.wait()
    lower = dot_exact01(acc_win, sbuf[...])
    base = bbuf[...].reshape(nr, SIDE**3)

    for k in range(KL):

        @pl.when(acts[k])
        def _():
            cp_d[k].wait()
            bk = base[16 * k:16 * (k + 1)]
            lk = lower[16 * k:16 * (k + 1)]
            vk = bk - lk if forward else lk
            parts = []
            for c0 in range(0, 16, 4):
                d = dbuf[k, c0:c0 + 4].astype(jnp.float32)
                parts.append(jnp.sum(d * vk[None], axis=1))
            y = jnp.concatenate(parts, axis=0)
            cbuf[k] = y if forward else bk - y

    cp_o = pltpu.make_async_copy(cbuf, cur_out.at[pl.ds(win, KL)], sems.at[4])
    cp_o.start()
    new = cbuf[...].reshape(nr, SIDE**3)
    sx[...] = jnp.zeros(sx.shape, jnp.float32)
    sy[...] = jnp.zeros(sy.shape, jnp.float32)
    zc[...] = jnp.zeros(zc.shape, jnp.float32)

    cp_g.wait()
    faces = dot_exact01(new, gbuf[...])
    flane = lax.broadcasted_iota(jnp.int32, (16, NF * FW), 1) // FW
    for k in range(KL):

        @pl.when(acts[k])
        def _():
            prod = dot_full(jbuf[k], faces[16 * k:16 * (k + 1)])
            inc = jnp.zeros((16, NF * FW), jnp.float32)
            for d in range(NF):
                inc = inc + jnp.where(flane == d, prod[16 * d:16 * (d + 1)], 0.0)
            sx[k] = inc[:, 0:128]
            sy[k] = inc[:, 128:256]
            zc[k] = pltpu.roll(inc[:, 256:384], 64, 1)

    cp_o.wait()


def update_kernel(lev_ref, tbl_ref, accf_in, rxp, rxm, ryp, rym, zc, accf_out, accf, sems):
    lvl = lev_ref[0]

    def T(j):
        return tbl_ref[lvl, j]

    cp_a = pltpu.make_async_copy(accf_in, accf, sems.at[0])
    cp_a.start()
    cp_a.wait()
    lane = lax.broadcasted_iota(jnp.int32, (16, 128), 1)
    low_half = lane < 64
    for src, (off, chunk, keep_low) in zip((rxp, rxm, ryp, rym), RECV):
        for k in range(KL):
            t = T(off + k)

            @pl.when(t >= 0)
            def _():
                moved = pltpu.roll(src[k], 64, 1)
                keep = low_half if keep_low else jnp.logical_not(low_half)
                sl = pl.ds(chunk * 128, 128)
                accf[t, :, sl] = accf[t, :, sl] + jnp.where(keep, moved, 0.0)

    for k in range(KL):
        for off, keep_low in ((7, False), (13, True)):
            t = T(off + k)

            @pl.when(t >= 0)
            def _():
                keep = low_half if keep_low else jnp.logical_not(low_half)
                sl = pl.ds(256, 128)
                accf[t, :, sl] = accf[t, :, sl] + jnp.where(keep, zc[k], 0.0)

    cp_w = pltpu.make_async_copy(accf, accf_out, sems.at[1])
    cp_w.start()
    cp_w.wait()


SMEM_SPEC = pl.BlockSpec(memory_space=pltpu.SMEM)
VMEM_SPEC = pl.BlockSpec(memory_space=pltpu.VMEM)
ANY_SPEC = pl.BlockSpec(memory_space=pl.ANY)
LIMITS = pltpu.CompilerParams(vmem_limit_bytes=48 * 1024 * 1024)


def run_compute(forward, lev, tbl, accf, base, cur, dinv, jac, recv, gmat, smat):
    face = jax.ShapeDtypeStruct((KL, 16, 128), jnp.float32)
    return pl.pallas_call(
        functools.partial(compute_kernel, forward),
        out_shape=(jax.ShapeDtypeStruct(cur.shape, jnp.float32), face, face, face),
        in_specs=[SMEM_SPEC, SMEM_SPEC] + [ANY_SPEC] * 5 + [VMEM_SPEC] * 4 + [ANY_SPEC] * 2,
        out_specs=(ANY_SPEC, VMEM_SPEC, VMEM_SPEC, VMEM_SPEC),
        scratch_shapes=[
            pltpu.VMEM((KL,) + accf.shape[1:], jnp.float32),
            pltpu.VMEM((KL,) + dinv.shape[1:], dinv.dtype),
            pltpu.VMEM((KL,) + jac.shape[1:], jnp.float32),
            pltpu.VMEM((KL,) + base.shape[1:], jnp.float32),
            pltpu.VMEM((KL,) + cur.shape[1:], jnp.float32),
            pltpu.VMEM(gmat.shape, gmat.dtype),
            pltpu.VMEM(smat.shape, smat.dtype),
            pltpu.SemaphoreType.DMA((7,)),
            pltpu.SemaphoreType.DMA((KL,)),
        ],
        input_output_aliases={4: 0},
        compiler_params=LIMITS,
    )(lev, tbl, accf, base, cur, dinv, jac, *recv, gmat, smat)


def run_update(lev, tbl, accf, recv, zc):
    return pl.pallas_call(
        update_kernel,
        out_shape=jax.ShapeDtypeStruct(accf.shape, jnp.float32),
        in_specs=[SMEM_SPEC, SMEM_SPEC, ANY_SPEC] + [VMEM_SPEC] * 5,
        out_specs=ANY_SPEC,
        scratch_shapes=[pltpu.VMEM(accf.shape, jnp.float32), pltpu.SemaphoreType.DMA((2,))],
        input_output_aliases={2: 0},
        compiler_params=LIMITS,
    )(lev, tbl, accf, *recv, zc)


def shift_along(value, axis, steps):
    count = lax.axis_size(axis)
    pairs = [(source, (source + steps) % count) for source in range(count)]
    return lax.ppermute(value, axis, pairs)


def exchange(sx, sy):
    return (
        shift_along(sx, "gx", 1),
        shift_along(sx, "gx", -1),
        shift_along(sy, "gy", 1),
        shift_along(sy, "gy", -1),
    )


def pick(vec, idx):
    ids = jnp.arange(vec.shape[0], dtype=jnp.int32).reshape((-1,) + (1,) * idx.ndim)
    return jnp.sum(jnp.where(idx[None] == ids, vec.reshape(ids.shape), 0), axis=0)


def pick_row(mat, row):
    ids = jnp.arange(mat.shape[0], dtype=jnp.int32)
    return jnp.sum(jnp.where(ids[:, None] == row, mat, 0), axis=0)


def build_tables(level_counts, slot_count):
    count_x = lax.axis_size("gx")
    count_y = lax.axis_size("gy")
    place_x = lax.axis_index("gx")
    place_y = lax.axis_index("gy")
    coords, where_slot = slot_layout(count_x, count_y, RX, RY, NBZ)
    nbs = [jnp.asarray(step_table(coords, where_slot, dm, st)) for dm, st in DIRECTION_MOVES]
    ends_all = jnp.cumsum(level_counts, axis=1)
    begins_all = ends_all - level_counts
    slots = jnp.arange(slot_count, dtype=jnp.int32)
    all_levels = jnp.sum(slots[None, :, None] >= ends_all[:, None, :], axis=2).astype(jnp.int32)
    own_row = place_x * count_y + place_y
    source_rows = [
        (place_x - 1) % count_x * count_y + place_y,
        (place_x + 1) % count_x * count_y + place_y,
        place_x * count_y + (place_y - 1) % count_y,
        place_x * count_y + (place_y + 1) % count_y,
    ]
    at_edge = [place_x == 0, place_x == count_x - 1, place_y == 0, place_y == count_y - 1]
    my_lv = pick_row(all_levels, own_row)
    levels = jnp.arange(LEVELS, dtype=jnp.int32)
    offsets = jnp.arange(KL, dtype=jnp.int32)

    def window(row, now):
        begin = pick(pick_row(begins_all, row), now)
        return jnp.clip(begin, 0, slot_count - KL)

    win = window(own_row, levels)
    wslots = win[:, None] + offsets[None, :]
    act = pick(my_lv, wslots) == levels[:, None]
    head = [win[:, None], act.astype(jnp.int32)]
    cols_f = list(head)
    cols_b = list(head)
    for d in (4, 5):
        tgt = pick(nbs[d], wslots)
        t_lv = pick(my_lv, tgt)
        live = (tgt >= 0) & act
        cols_f.append(jnp.where(live & (t_lv > levels[:, None]), tgt, -1))
        cols_b.append(jnp.where(live & (t_lv < levels[:, None]), tgt, -1))
    rows = jnp.stack(source_rows)
    row_hot = jnp.arange(ends_all.shape[0], dtype=jnp.int32)[None, :] == rows[:, None]
    src_begins = jnp.sum(jnp.where(row_hot[:, :, None], begins_all[None], 0), axis=1)
    src_levels = jnp.sum(jnp.where(row_hot[:, :, None], all_levels[None], 0), axis=1)
    lv_hot = levels[None, :] == levels[:, None]
    swin = jnp.sum(jnp.where(lv_hot[None], src_begins[:, None, :], 0), axis=2)
    swin = jnp.clip(swin, 0, slot_count - KL)
    sslots = swin[:, :, None] + offsets[None, None, :]
    slot_hot = sslots[..., None] == slots
    s_lv = jnp.sum(jnp.where(slot_hot, src_levels[:, None, None, :], 0), axis=3)
    s_act = s_lv == levels[None, :, None]
    nb_remote = jnp.stack(nbs[:4])
    stepped = jnp.sum(jnp.where(slot_hot, nb_remote[:, None, None, :], 0), axis=3)
    tgt = jnp.where(jnp.stack(at_edge)[:, None, None], stepped, sslots)
    tgt_hot = tgt[..., None] == slots
    t_lv = jnp.sum(jnp.where(tgt_hot, my_lv[None, None, None, :], 0), axis=3)
    live = (tgt >= 0) & s_act
    sent = levels[None, :, None]
    remote_f = jnp.where(live & (t_lv > sent), tgt, -1)
    remote_b = jnp.where(live & (t_lv < sent), tgt, -1)
    none_row = jnp.full((4, 1, KL), -1, jnp.int32)
    remote_f = jnp.concatenate([none_row, remote_f[:, :-1]], axis=1)
    remote_b = jnp.concatenate([remote_b[:, 1:], none_row], axis=1)
    for d in range(4):
        cols_f.append(remote_f[d])
        cols_b.append(remote_b[d])

    def finish(cols):
        table = jnp.concatenate(cols, axis=1).astype(jnp.int32)
        return jnp.pad(table, ((0, 0), (0, TW - table.shape[1])), constant_values=-1)

    return finish(cols_f), finish(cols_b)


def body(right_side, diag_inverse, face_jac, level_counts):
    slot_count = right_side.shape[0]
    unknowns = right_side.shape[1]
    gather_np, scatter_np = face_matrices(SIDE)
    gmat = jnp.asarray(gather_np, dtype=jnp.bfloat16)
    smat = jnp.asarray(scatter_np, dtype=jnp.bfloat16)
    jac = jnp.transpose(face_jac, (3, 0, 1, 2)).reshape(slot_count, NF * unknowns, unknowns)
    tbl_f, tbl_b = build_tables(level_counts, slot_count)
    zero_recv = tuple(jnp.zeros((KL, 16, 128), jnp.float32) for _ in range(4))

    def lev_arr(v):
        return jnp.reshape(jnp.asarray(v, jnp.int32), (1,))

    def sweep(forward, tbl, order, base, carry):

        def step(i, carry):
            accf, cur, sx, sy, zc, prev = carry
            recv = exchange(sx, sy)
            accf = run_update(lev_arr(order(i - 1)), tbl, accf, prev, zc)
            cur, sx, sy, zc = run_compute(forward, lev_arr(order(i)), tbl, accf, base, cur,
                                          diag_inverse, jac, recv, gmat, smat)
            return accf, cur, sx, sy, zc, recv

        return lax.fori_loop(1, LEVELS, step, carry)

    def blank_acc():
        return jnp.zeros((slot_count, unknowns, NF * FW), jnp.float32)

    cur = jnp.zeros(right_side.shape, jnp.float32)
    cur, sx, sy, zc = run_compute(True, lev_arr(0), tbl_f, blank_acc(), right_side, cur,
                                  diag_inverse, jac, zero_recv, gmat, smat)
    carry = (blank_acc(), cur, sx, sy, zc, zero_recv)
    _, half, sx, sy, zc, _ = sweep(True, tbl_f, lambda i: i, right_side, carry)
    carry = (blank_acc(), half, sx, sy, zc, zero_recv)
    result = sweep(False, tbl_b, lambda i: LEVELS - 1 - i, half, carry)[1]
    return result


def solution(mesh):
    return jax.shard_map(
        body,
        mesh=mesh,
        in_specs=(
            P(("gx", "gy"), None, None),
            P(("gx", "gy"), None, None, None),
            P(None, None, None, ("gx", "gy")),
            P(),
        ),
        out_specs=P(("gx", "gy"), None, None),
        check_vma=False,
    )
```

```python
import functools

import jax
import jax.numpy as jnp
import numpy as np
from jax import lax
from jax.experimental import pallas as pl
from jax.experimental.pallas import tpu as pltpu
from jax.sharding import PartitionSpec as P

SIDE = 8
LEVELS = 12
RX = 2
RY = 2
NBZ = 8
KL = 6
NF = 6
FW = SIDE * SIDE
TW = 48

OPPOSITE = (1, 0, 3, 2, 5, 4)
DIRECTION_MOVES = ((0, 1), (0, -1), (1, 1), (1, -1), (2, 1), (2, -1))


def slot_layout(step_x, step_y, count_x, count_y, count_z):
    ordering = sorted(
        (
            (step_x * along_x + step_y * along_y + along_z, along_x, along_y, along_z)
            for along_x in range(count_x)
            for along_y in range(count_y)
            for along_z in range(count_z)
        )
    )
    coords = np.array([record[1:] for record in ordering], dtype=np.int64)
    where_slot = np.zeros((count_x, count_y, count_z), dtype=np.int64)
    where_slot[coords[:, 0], coords[:, 1], coords[:, 2]] = np.arange(len(ordering))
    return (coords, where_slot)


def step_table(coords, where_slot, dimension, offset_step):
    moved = coords.copy()
    moved[:, dimension] += offset_step
    bound_size = where_slot.shape[dimension]
    inside = (moved[:, dimension] >= 0) & (moved[:, dimension] < bound_size)
    clipped = np.clip(moved, 0, np.array(where_slot.shape) - 1)
    target = where_slot[clipped[:, 0], clipped[:, 1], clipped[:, 2]]
    return np.where(inside, target, -1).astype(np.int32)


def face_matrices(edge_cells):
    cell_ids = np.arange(edge_cells**3).reshape(edge_cells, edge_cells, edge_cells)
    layers = [
        cell_ids[edge_cells - 1],
        cell_ids[0],
        cell_ids[:, edge_cells - 1],
        cell_ids[:, 0],
        cell_ids[:, :, edge_cells - 1],
        cell_ids[:, :, 0],
    ]
    outward = np.stack([layer_ids.reshape(-1) for layer_ids in layers])
    cell_total = edge_cells**3
    face_width = edge_cells * edge_cells
    gather = np.zeros((cell_total, NF * face_width), dtype=np.float32)
    for face_index in range(NF):
        gather[outward[face_index], face_index * face_width + np.arange(face_width)] = 1.0
    return gather, np.ascontiguousarray(gather.T)


def split3(x):
    hi = x.astype(jnp.bfloat16)
    rest = x - hi.astype(jnp.float32)
    mid = rest.astype(jnp.bfloat16)
    low = (rest - mid.astype(jnp.float32)).astype(jnp.bfloat16)
    return hi, mid, low


def mm(a, b):
    return jnp.dot(a, b, preferred_element_type=jnp.float32)


def dot_exact01(x, table):
    hi, mid, low = split3(x)
    return mm(hi, table) + mm(mid, table) + mm(low, table)


def split2(x):
    hi = x.astype(jnp.bfloat16)
    return hi, (x - hi.astype(jnp.float32)).astype(jnp.bfloat16)


def dot_full(a, b):
    ah, al = split2(a)
    bh, bl = split2(b)
    return mm(ah, bh) + (mm(ah, bl) + mm(al, bh))


RECV = ((19, 0, False), (25, 0, True), (31, 1, False), (37, 1, True))


def compute_kernel(forward, lev_ref, tbl_ref, accf_hbm, base_hbm, cur_hbm, dinv_hbm, jac_hbm,
                   rxp_hbm, rxm_hbm, ryp_hbm, rym_hbm, gmat, smat,
                   cur_out, sx, sy, zc,
                   accw, dbuf, jbuf, bbuf, cbuf, gbuf, sbuf, rbuf, sems, dsems, rsems):
    lvl = lev_ref[0]

    def T(j):
        return tbl_ref[lvl, j]

    win = T(0)
    cp_a = pltpu.make_async_copy(accf_hbm.at[pl.ds(win, KL)], accw, sems.at[0])
    cp_a.start()
    cp_d = [pltpu.make_async_copy(dinv_hbm.at[win + k], dbuf.at[k], dsems.at[k])
            for k in range(KL)]
    cp_j = pltpu.make_async_copy(jac_hbm.at[pl.ds(win, KL)], jbuf, sems.at[1])
    cp_b = pltpu.make_async_copy(base_hbm.at[pl.ds(win, KL)], bbuf, sems.at[2])
    cp_c = pltpu.make_async_copy(cur_hbm.at[pl.ds(win, KL)], cbuf, sems.at[3])
    cp_s = pltpu.make_async_copy(smat, sbuf, sems.at[5])
    cp_g = pltpu.make_async_copy(gmat, gbuf, sems.at[6])
    cp_s.start()
    cp_g.start()
    cp_r = [pltpu.make_async_copy(src, rbuf.at[i], rsems.at[i])
            for i, src in enumerate((rxp_hbm, rxm_hbm, ryp_hbm, rym_hbm))]
    for cp in cp_r:
        cp.start()
    acts = [T(1 + k) > 0 for k in range(KL)]
    for k in range(KL):
        pl.when(acts[k])(cp_d[k].start)
    cp_j.start()
    cp_b.start()
    cp_c.start()

    cp_a.wait()
    for cp in cp_r:
        cp.wait()
    lane = lax.broadcasted_iota(jnp.int32, (16, 128), 1)
    low_half = lane < 64

    for src, (off, chunk, keep_low) in zip([rbuf.at[i] for i in range(4)], RECV):
        for k in range(KL):
            j = T(off + k) - win

            @pl.when((j >= 0) & (j < KL))
            def _():
                moved = pltpu.roll(src[k], 64, 1)
                keep = low_half if keep_low else jnp.logical_not(low_half)
                sl = pl.ds(chunk * 128, 128)
                accw[j, :, sl] = accw[j, :, sl] + jnp.where(keep, moved, 0.0)

    cp_j.wait()
    cp_b.wait()
    cp_c.wait()

    nr = KL * 16
    acc_win = accw[...].reshape(nr, NF * FW)
    cp_s.wait()
    lower = dot_exact01(acc_win, sbuf[...])
    base = bbuf[...].reshape(nr, SIDE**3)

    for k in range(KL):

        @pl.when(acts[k])
        def _():
            cp_d[k].wait()
            bk = base[16 * k:16 * (k + 1)]
            lk = lower[16 * k:16 * (k + 1)]
            vk = bk - lk if forward else lk
            parts = []
            for c0 in range(0, 16, 4):
                d = dbuf[k, c0:c0 + 4].astype(jnp.float32)
                parts.append(jnp.sum(d * vk[None], axis=1))
            y = jnp.concatenate(parts, axis=0)
            cbuf[k] = y if forward else bk - y

    cp_o = pltpu.make_async_copy(cbuf, cur_out.at[pl.ds(win, KL)], sems.at[4])
    cp_o.start()
    new = cbuf[...].reshape(nr, SIDE**3)
    sx[...] = jnp.zeros(sx.shape, jnp.float32)
    sy[...] = jnp.zeros(sy.shape, jnp.float32)
    zc[...] = jnp.zeros(zc.shape, jnp.float32)

    cp_g.wait()
    faces = dot_exact01(new, gbuf[...])
    flane = lax.broadcasted_iota(jnp.int32, (16, NF * FW), 1) // FW
    for k in range(KL):

        @pl.when(acts[k])
        def _():
            prod = dot_full(jbuf[k], faces[16 * k:16 * (k + 1)])
            inc = jnp.zeros((16, NF * FW), jnp.float32)
            for d in range(NF):
                inc = inc + jnp.where(flane == d, prod[16 * d:16 * (d + 1)], 0.0)
            sx[k] = inc[:, 0:128]
            sy[k] = inc[:, 128:256]
            zc[k] = pltpu.roll(inc[:, 256:384], 64, 1)

    cp_o.wait()


def update_kernel(lev_ref, tbl_ref, accf_in, rxp, rxm, ryp, rym, zc, accf_out, accf, sems):
    lvl = lev_ref[0]

    def T(j):
        return tbl_ref[lvl, j]

    cp_a = pltpu.make_async_copy(accf_in, accf, sems.at[0])
    cp_a.start()
    cp_a.wait()
    lane = lax.broadcasted_iota(jnp.int32, (16, 128), 1)
    low_half = lane < 64
    for src, (off, chunk, keep_low) in zip((rxp, rxm, ryp, rym), RECV):
        for k in range(KL):
            t = T(off + k)

            @pl.when(t >= 0)
            def _():
                moved = pltpu.roll(src[k], 64, 1)
                keep = low_half if keep_low else jnp.logical_not(low_half)
                sl = pl.ds(chunk * 128, 128)
                accf[t, :, sl] = accf[t, :, sl] + jnp.where(keep, moved, 0.0)

    for k in range(KL):
        for off, keep_low in ((7, False), (13, True)):
            t = T(off + k)

            @pl.when(t >= 0)
            def _():
                keep = low_half if keep_low else jnp.logical_not(low_half)
                sl = pl.ds(256, 128)
                accf[t, :, sl] = accf[t, :, sl] + jnp.where(keep, zc[k], 0.0)

    cp_w = pltpu.make_async_copy(accf, accf_out, sems.at[1])
    cp_w.start()
    cp_w.wait()


SMEM_SPEC = pl.BlockSpec(memory_space=pltpu.SMEM)
VMEM_SPEC = pl.BlockSpec(memory_space=pltpu.VMEM)
ANY_SPEC = pl.BlockSpec(memory_space=pl.ANY)
LIMITS = pltpu.CompilerParams(vmem_limit_bytes=48 * 1024 * 1024)


def run_compute(forward, lev, tbl, accf, base, cur, dinv, jac, recv, gmat, smat):
    face = jax.ShapeDtypeStruct((KL, 16, 128), jnp.float32)
    return pl.pallas_call(
        functools.partial(compute_kernel, forward),
        out_shape=(jax.ShapeDtypeStruct(cur.shape, jnp.float32), face, face, face),
        in_specs=[SMEM_SPEC, SMEM_SPEC] + [ANY_SPEC] * 11,
        out_specs=(ANY_SPEC, VMEM_SPEC, VMEM_SPEC, VMEM_SPEC),
        scratch_shapes=[
            pltpu.VMEM((KL,) + accf.shape[1:], jnp.float32),
            pltpu.VMEM((KL,) + dinv.shape[1:], dinv.dtype),
            pltpu.VMEM((KL,) + jac.shape[1:], jnp.float32),
            pltpu.VMEM((KL,) + base.shape[1:], jnp.float32),
            pltpu.VMEM((KL,) + cur.shape[1:], jnp.float32),
            pltpu.VMEM(gmat.shape, gmat.dtype),
            pltpu.VMEM(smat.shape, smat.dtype),
            pltpu.VMEM((4, KL, 16, 128), jnp.float32),
            pltpu.SemaphoreType.DMA((7,)),
            pltpu.SemaphoreType.DMA((KL,)),
            pltpu.SemaphoreType.DMA((4,)),
        ],
        input_output_aliases={4: 0},
        compiler_params=LIMITS,
    )(lev, tbl, accf, base, cur, dinv, jac, *recv, gmat, smat)


def run_update(lev, tbl, accf, recv, zc):
    return pl.pallas_call(
        update_kernel,
        out_shape=jax.ShapeDtypeStruct(accf.shape, jnp.float32),
        in_specs=[SMEM_SPEC, SMEM_SPEC, ANY_SPEC] + [VMEM_SPEC] * 5,
        out_specs=ANY_SPEC,
        scratch_shapes=[pltpu.VMEM(accf.shape, jnp.float32), pltpu.SemaphoreType.DMA((2,))],
        input_output_aliases={2: 0},
        compiler_params=LIMITS,
    )(lev, tbl, accf, *recv, zc)


def shift_along(value, axis, steps):
    count = lax.axis_size(axis)
    pairs = [(source, (source + steps) % count) for source in range(count)]
    return lax.ppermute(value, axis, pairs)


def exchange(sx, sy):
    return (
        shift_along(sx, "gx", 1),
        shift_along(sx, "gx", -1),
        shift_along(sy, "gy", 1),
        shift_along(sy, "gy", -1),
    )


def pick(vec, idx):
    ids = jnp.arange(vec.shape[0], dtype=jnp.int32).reshape((-1,) + (1,) * idx.ndim)
    return jnp.sum(jnp.where(idx[None] == ids, vec.reshape(ids.shape), 0), axis=0)


def pick_row(mat, row):
    ids = jnp.arange(mat.shape[0], dtype=jnp.int32)
    return jnp.sum(jnp.where(ids[:, None] == row, mat, 0), axis=0)


def build_tables(level_counts, slot_count):
    count_x = lax.axis_size("gx")
    count_y = lax.axis_size("gy")
    place_x = lax.axis_index("gx")
    place_y = lax.axis_index("gy")
    coords, where_slot = slot_layout(count_x, count_y, RX, RY, NBZ)
    nbs = [jnp.asarray(step_table(coords, where_slot, dm, st)) for dm, st in DIRECTION_MOVES]
    ends_all = jnp.cumsum(level_counts, axis=1)
    begins_all = ends_all - level_counts
    slots = jnp.arange(slot_count, dtype=jnp.int32)
    all_levels = jnp.sum(slots[None, :, None] >= ends_all[:, None, :], axis=2).astype(jnp.int32)
    own_row = place_x * count_y + place_y
    source_rows = [
        (place_x - 1) % count_x * count_y + place_y,
        (place_x + 1) % count_x * count_y + place_y,
        place_x * count_y + (place_y - 1) % count_y,
        place_x * count_y + (place_y + 1) % count_y,
    ]
    at_edge = [place_x == 0, place_x == count_x - 1, place_y == 0, place_y == count_y - 1]
    my_lv = pick_row(all_levels, own_row)
    levels = jnp.arange(LEVELS, dtype=jnp.int32)
    offsets = jnp.arange(KL, dtype=jnp.int32)

    def window(row, now):
        begin = pick(pick_row(begins_all, row), now)
        return jnp.clip(begin, 0, slot_count - KL)

    win = window(own_row, levels)
    wslots = win[:, None] + offsets[None, :]
    act = pick(my_lv, wslots) == levels[:, None]
    head = [win[:, None], act.astype(jnp.int32)]
    cols_f = list(head)
    cols_b = list(head)
    for d in (4, 5):
        tgt = pick(nbs[d], wslots)
        t_lv = pick(my_lv, tgt)
        live = (tgt >= 0) & act
        cols_f.append(jnp.where(live & (t_lv > levels[:, None]), tgt, -1))
        cols_b.append(jnp.where(live & (t_lv < levels[:, None]), tgt, -1))
    rows = jnp.stack(source_rows)
    row_hot = jnp.arange(ends_all.shape[0], dtype=jnp.int32)[None, :] == rows[:, None]
    src_begins = jnp.sum(jnp.where(row_hot[:, :, None], begins_all[None], 0), axis=1)
    src_levels = jnp.sum(jnp.where(row_hot[:, :, None], all_levels[None], 0), axis=1)
    lv_hot = levels[None, :] == levels[:, None]
    swin = jnp.sum(jnp.where(lv_hot[None], src_begins[:, None, :], 0), axis=2)
    swin = jnp.clip(swin, 0, slot_count - KL)
    sslots = swin[:, :, None] + offsets[None, None, :]
    slot_hot = sslots[..., None] == slots
    s_lv = jnp.sum(jnp.where(slot_hot, src_levels[:, None, None, :], 0), axis=3)
    s_act = s_lv == levels[None, :, None]
    nb_remote = jnp.stack(nbs[:4])
    stepped = jnp.sum(jnp.where(slot_hot, nb_remote[:, None, None, :], 0), axis=3)
    tgt = jnp.where(jnp.stack(at_edge)[:, None, None], stepped, sslots)
    tgt_hot = tgt[..., None] == slots
    t_lv = jnp.sum(jnp.where(tgt_hot, my_lv[None, None, None, :], 0), axis=3)
    live = (tgt >= 0) & s_act
    sent = levels[None, :, None]
    remote_f = jnp.where(live & (t_lv > sent), tgt, -1)
    remote_b = jnp.where(live & (t_lv < sent), tgt, -1)
    none_row = jnp.full((4, 1, KL), -1, jnp.int32)
    remote_f = jnp.concatenate([none_row, remote_f[:, :-1]], axis=1)
    remote_b = jnp.concatenate([remote_b[:, 1:], none_row], axis=1)
    for d in range(4):
        cols_f.append(remote_f[d])
        cols_b.append(remote_b[d])

    def finish(cols):
        table = jnp.concatenate(cols, axis=1).astype(jnp.int32)
        return jnp.pad(table, ((0, 0), (0, TW - table.shape[1])), constant_values=-1)

    return finish(cols_f), finish(cols_b)


def body(right_side, diag_inverse, face_jac, level_counts):
    slot_count = right_side.shape[0]
    unknowns = right_side.shape[1]
    gather_np, scatter_np = face_matrices(SIDE)
    gmat = jnp.asarray(gather_np, dtype=jnp.bfloat16)
    smat = jnp.asarray(scatter_np, dtype=jnp.bfloat16)
    jac = jnp.transpose(face_jac, (3, 0, 1, 2)).reshape(slot_count, NF * unknowns, unknowns)
    tbl_f, tbl_b = build_tables(level_counts, slot_count)
    zero_recv = tuple(jnp.zeros((KL, 16, 128), jnp.float32) for _ in range(4))

    def lev_arr(v):
        return jnp.reshape(jnp.asarray(v, jnp.int32), (1,))

    def sweep(forward, tbl, order, base, carry):

        def step(i, carry):
            accf, cur, sx, sy, zc, prev = carry
            recv = exchange(sx, sy)
            accf = run_update(lev_arr(order(i - 1)), tbl, accf, prev, zc)
            cur, sx, sy, zc = run_compute(forward, lev_arr(order(i)), tbl, accf, base, cur,
                                          diag_inverse, jac, recv, gmat, smat)
            return accf, cur, sx, sy, zc, recv

        return lax.fori_loop(1, LEVELS, step, carry)

    def blank_acc():
        return jnp.zeros((slot_count, unknowns, NF * FW), jnp.float32)

    cur = jnp.zeros(right_side.shape, jnp.float32)
    cur, sx, sy, zc = run_compute(True, lev_arr(0), tbl_f, blank_acc(), right_side, cur,
                                  diag_inverse, jac, zero_recv, gmat, smat)
    carry = (blank_acc(), cur, sx, sy, zc, zero_recv)
    _, half, sx, sy, zc, _ = sweep(True, tbl_f, lambda i: i, right_side, carry)
    carry = (blank_acc(), half, sx, sy, zc, zero_recv)
    result = sweep(False, tbl_b, lambda i: LEVELS - 1 - i, half, carry)[1]
    return result


def solution(mesh):
    return jax.shard_map(
        body,
        mesh=mesh,
        in_specs=(
            P(("gx", "gy"), None, None),
            P(("gx", "gy"), None, None, None),
            P(None, None, None, ("gx", "gy")),
            P(),
        ),
        out_specs=P(("gx", "gy"), None, None),
        check_vma=False,
    )
```

```python
import functools

import jax
import jax.numpy as jnp
import numpy as np
from jax import lax
from jax.experimental import pallas as pl
from jax.experimental.pallas import tpu as pltpu
from jax.sharding import PartitionSpec as P

SIDE = 8
LEVELS = 12
RX = 2
RY = 2
NBZ = 8
KL = 6
NF = 6
FW = SIDE * SIDE
TW = 48

OPPOSITE = (1, 0, 3, 2, 5, 4)
DIRECTION_MOVES = ((0, 1), (0, -1), (1, 1), (1, -1), (2, 1), (2, -1))


def slot_layout(step_x, step_y, count_x, count_y, count_z):
    ordering = sorted(
        (
            (step_x * along_x + step_y * along_y + along_z, along_x, along_y, along_z)
            for along_x in range(count_x)
            for along_y in range(count_y)
            for along_z in range(count_z)
        )
    )
    coords = np.array([record[1:] for record in ordering], dtype=np.int64)
    where_slot = np.zeros((count_x, count_y, count_z), dtype=np.int64)
    where_slot[coords[:, 0], coords[:, 1], coords[:, 2]] = np.arange(len(ordering))
    return (coords, where_slot)


def step_table(coords, where_slot, dimension, offset_step):
    moved = coords.copy()
    moved[:, dimension] += offset_step
    bound_size = where_slot.shape[dimension]
    inside = (moved[:, dimension] >= 0) & (moved[:, dimension] < bound_size)
    clipped = np.clip(moved, 0, np.array(where_slot.shape) - 1)
    target = where_slot[clipped[:, 0], clipped[:, 1], clipped[:, 2]]
    return np.where(inside, target, -1).astype(np.int32)


def face_matrices(edge_cells):
    cell_ids = np.arange(edge_cells**3).reshape(edge_cells, edge_cells, edge_cells)
    layers = [
        cell_ids[edge_cells - 1],
        cell_ids[0],
        cell_ids[:, edge_cells - 1],
        cell_ids[:, 0],
        cell_ids[:, :, edge_cells - 1],
        cell_ids[:, :, 0],
    ]
    outward = np.stack([layer_ids.reshape(-1) for layer_ids in layers])
    cell_total = edge_cells**3
    face_width = edge_cells * edge_cells
    gather = np.zeros((cell_total, NF * face_width), dtype=np.float32)
    for face_index in range(NF):
        gather[outward[face_index], face_index * face_width + np.arange(face_width)] = 1.0
    return gather, np.ascontiguousarray(gather.T)


def split3(x):
    hi = x.astype(jnp.bfloat16)
    rest = x - hi.astype(jnp.float32)
    mid = rest.astype(jnp.bfloat16)
    low = (rest - mid.astype(jnp.float32)).astype(jnp.bfloat16)
    return hi, mid, low


def mm(a, b):
    return jnp.dot(a, b, preferred_element_type=jnp.float32)


def dot_exact01(x, table):
    hi, mid, low = split3(x)
    return mm(hi, table) + mm(mid, table) + mm(low, table)


def split2(x):
    hi = x.astype(jnp.bfloat16)
    return hi, (x - hi.astype(jnp.float32)).astype(jnp.bfloat16)


def dot_full(a, b):
    ah, al = split2(a)
    bh, bl = split2(b)
    return mm(ah, bh) + (mm(ah, bl) + mm(al, bh))


RECV = ((19, 0, False), (25, 0, True), (31, 1, False), (37, 1, True))


def compute_kernel(forward, lev_ref, tbl_ref, accf_hbm, base_hbm, cur_hbm, dinv_hbm, jac_hbm,
                   rxp, rxm, ryp, rym, gmat, smat,
                   cur_out, sx, sy, zc,
                   accw, dbuf, jbuf, bbuf, cbuf, gbuf, sbuf, sems, dsems):
    lvl = lev_ref[0]

    def T(j):
        return tbl_ref[lvl, j]

    win = T(0)
    cp_a = pltpu.make_async_copy(accf_hbm.at[pl.ds(win, KL)], accw, sems.at[0])
    cp_a.start()
    cp_d = [pltpu.make_async_copy(dinv_hbm.at[win + k], dbuf.at[k], dsems.at[k])
            for k in range(KL)]
    cp_j = pltpu.make_async_copy(jac_hbm.at[pl.ds(win, KL)], jbuf, sems.at[1])
    cp_b = pltpu.make_async_copy(base_hbm.at[pl.ds(win, KL)], bbuf, sems.at[2])
    cp_c = pltpu.make_async_copy(cur_hbm.at[pl.ds(win, KL)], cbuf, sems.at[3])
    cp_s = pltpu.make_async_copy(smat, sbuf, sems.at[5])
    cp_g = pltpu.make_async_copy(gmat, gbuf, sems.at[6])
    cp_b.start()
    cp_c.start()
    cp_j.start()
    cp_s.start()
    acts = [T(1 + k) > 0 for k in range(KL)]
    for k in range(KL):
        pl.when(acts[k])(cp_d[k].start)
    cp_g.start()

    cp_a.wait()
    lane = lax.broadcasted_iota(jnp.int32, (16, 128), 1)
    low_half = lane < 64

    for src, (off, chunk, keep_low) in zip((rxp, rxm, ryp, rym), RECV):
        for k in range(KL):
            j = T(off + k) - win

            @pl.when((j >= 0) & (j < KL))
            def _():
                moved = pltpu.roll(src[k], 64, 1)
                keep = low_half if keep_low else jnp.logical_not(low_half)
                sl = pl.ds(chunk * 128, 128)
                accw[j, :, sl] = accw[j, :, sl] + jnp.where(keep, moved, 0.0)

    cp_j.wait()
    cp_b.wait()
    cp_c.wait()

    nr = KL * 16
    acc_win = accw[...].reshape(nr, NF * FW)
    cp_s.wait()
    lower = dot_exact01(acc_win, sbuf[...])
    base = bbuf[...].reshape(nr, SIDE**3)

    for k in range(KL):

        @pl.when(acts[k])
        def _():
            cp_d[k].wait()
            bk = base[16 * k:16 * (k + 1)]
            lk = lower[16 * k:16 * (k + 1)]
            vk = bk - lk if forward else lk
            parts = []
            for c0 in range(0, 16, 4):
                d = dbuf[k, c0:c0 + 4].astype(jnp.float32)
                parts.append(jnp.sum(d * vk[None], axis=1))
            y = jnp.concatenate(parts, axis=0)
            cbuf[k] = y if forward else bk - y

    cp_o = pltpu.make_async_copy(cbuf, cur_out.at[pl.ds(win, KL)], sems.at[4])
    cp_o.start()
    new = cbuf[...].reshape(nr, SIDE**3)
    sx[...] = jnp.zeros(sx.shape, jnp.float32)
    sy[...] = jnp.zeros(sy.shape, jnp.float32)
    zc[...] = jnp.zeros(zc.shape, jnp.float32)

    cp_g.wait()
    faces = dot_exact01(new, gbuf[...])
    flane = lax.broadcasted_iota(jnp.int32, (16, NF * FW), 1) // FW
    for k in range(KL):

        @pl.when(acts[k])
        def _():
            prod = dot_full(jbuf[k], faces[16 * k:16 * (k + 1)])
            inc = jnp.zeros((16, NF * FW), jnp.float32)
            for d in range(NF):
                inc = inc + jnp.where(flane == d, prod[16 * d:16 * (d + 1)], 0.0)
            sx[k] = inc[:, 0:128]
            sy[k] = inc[:, 128:256]
            zc[k] = pltpu.roll(inc[:, 256:384], 64, 1)

    cp_o.wait()


def update_kernel(lev_ref, tbl_ref, accf_in, rxp, rxm, ryp, rym, zc, accf_out, accf, sems):
    lvl = lev_ref[0]

    def T(j):
        return tbl_ref[lvl, j]

    cp_a = pltpu.make_async_copy(accf_in, accf, sems.at[0])
    cp_a.start()
    cp_a.wait()
    lane = lax.broadcasted_iota(jnp.int32, (16, 128), 1)
    low_half = lane < 64
    for src, (off, chunk, keep_low) in zip((rxp, rxm, ryp, rym), RECV):
        for k in range(KL):
            t = T(off + k)

            @pl.when(t >= 0)
            def _():
                moved = pltpu.roll(src[k], 64, 1)
                keep = low_half if keep_low else jnp.logical_not(low_half)
                sl = pl.ds(chunk * 128, 128)
                accf[t, :, sl] = accf[t, :, sl] + jnp.where(keep, moved, 0.0)

    for k in range(KL):
        for off, keep_low in ((7, False), (13, True)):
            t = T(off + k)

            @pl.when(t >= 0)
            def _():
                keep = low_half if keep_low else jnp.logical_not(low_half)
                sl = pl.ds(256, 128)
                accf[t, :, sl] = accf[t, :, sl] + jnp.where(keep, zc[k], 0.0)

    cp_w = pltpu.make_async_copy(accf, accf_out, sems.at[1])
    cp_w.start()
    cp_w.wait()


SMEM_SPEC = pl.BlockSpec(memory_space=pltpu.SMEM)
VMEM_SPEC = pl.BlockSpec(memory_space=pltpu.VMEM)
ANY_SPEC = pl.BlockSpec(memory_space=pl.ANY)
LIMITS = pltpu.CompilerParams(vmem_limit_bytes=48 * 1024 * 1024)


def run_compute(forward, lev, tbl, accf, base, cur, dinv, jac, recv, gmat, smat):
    face = jax.ShapeDtypeStruct((KL, 16, 128), jnp.float32)
    return pl.pallas_call(
        functools.partial(compute_kernel, forward),
        out_shape=(jax.ShapeDtypeStruct(cur.shape, jnp.float32), face, face, face),
        in_specs=[SMEM_SPEC, SMEM_SPEC] + [ANY_SPEC] * 5 + [VMEM_SPEC] * 4 + [ANY_SPEC] * 2,
        out_specs=(ANY_SPEC, VMEM_SPEC, VMEM_SPEC, VMEM_SPEC),
        scratch_shapes=[
            pltpu.VMEM((KL,) + accf.shape[1:], jnp.float32),
            pltpu.VMEM((KL,) + dinv.shape[1:], dinv.dtype),
            pltpu.VMEM((KL,) + jac.shape[1:], jnp.float32),
            pltpu.VMEM((KL,) + base.shape[1:], jnp.float32),
            pltpu.VMEM((KL,) + cur.shape[1:], jnp.float32),
            pltpu.VMEM(gmat.shape, gmat.dtype),
            pltpu.VMEM(smat.shape, smat.dtype),
            pltpu.SemaphoreType.DMA((7,)),
            pltpu.SemaphoreType.DMA((KL,)),
        ],
        input_output_aliases={4: 0},
        compiler_params=LIMITS,
    )(lev, tbl, accf, base, cur, dinv, jac, *recv, gmat, smat)


def run_update(lev, tbl, accf, recv, zc):
    return pl.pallas_call(
        update_kernel,
        out_shape=jax.ShapeDtypeStruct(accf.shape, jnp.float32),
        in_specs=[SMEM_SPEC, SMEM_SPEC, ANY_SPEC] + [VMEM_SPEC] * 5,
        out_specs=ANY_SPEC,
        scratch_shapes=[pltpu.VMEM(accf.shape, jnp.float32), pltpu.SemaphoreType.DMA((2,))],
        input_output_aliases={2: 0},
        compiler_params=LIMITS,
    )(lev, tbl, accf, *recv, zc)


def shift_along(value, axis, steps):
    count = lax.axis_size(axis)
    pairs = [(source, (source + steps) % count) for source in range(count)]
    return lax.ppermute(value, axis, pairs)


def exchange(sx, sy):
    return (
        shift_along(sx, "gx", 1),
        shift_along(sx, "gx", -1),
        shift_along(sy, "gy", 1),
        shift_along(sy, "gy", -1),
    )


def pick(vec, idx):
    ids = jnp.arange(vec.shape[0], dtype=jnp.int32).reshape((-1,) + (1,) * idx.ndim)
    return jnp.sum(jnp.where(idx[None] == ids, vec.reshape(ids.shape), 0), axis=0)


def pick_row(mat, row):
    ids = jnp.arange(mat.shape[0], dtype=jnp.int32)
    return jnp.sum(jnp.where(ids[:, None] == row, mat, 0), axis=0)


def build_tables(level_counts, slot_count):
    count_x = lax.axis_size("gx")
    count_y = lax.axis_size("gy")
    place_x = lax.axis_index("gx")
    place_y = lax.axis_index("gy")
    coords, where_slot = slot_layout(count_x, count_y, RX, RY, NBZ)
    nbs = [jnp.asarray(step_table(coords, where_slot, dm, st)) for dm, st in DIRECTION_MOVES]
    ends_all = jnp.cumsum(level_counts, axis=1)
    begins_all = ends_all - level_counts
    slots = jnp.arange(slot_count, dtype=jnp.int32)
    all_levels = jnp.sum(slots[None, :, None] >= ends_all[:, None, :], axis=2).astype(jnp.int32)
    own_row = place_x * count_y + place_y
    source_rows = [
        (place_x - 1) % count_x * count_y + place_y,
        (place_x + 1) % count_x * count_y + place_y,
        place_x * count_y + (place_y - 1) % count_y,
        place_x * count_y + (place_y + 1) % count_y,
    ]
    at_edge = [place_x == 0, place_x == count_x - 1, place_y == 0, place_y == count_y - 1]
    my_lv = pick_row(all_levels, own_row)
    levels = jnp.arange(LEVELS, dtype=jnp.int32)
    offsets = jnp.arange(KL, dtype=jnp.int32)

    def window(row, now):
        begin = pick(pick_row(begins_all, row), now)
        return jnp.clip(begin, 0, slot_count - KL)

    win = window(own_row, levels)
    wslots = win[:, None] + offsets[None, :]
    act = pick(my_lv, wslots) == levels[:, None]
    head = [win[:, None], act.astype(jnp.int32)]
    cols_f = list(head)
    cols_b = list(head)
    for d in (4, 5):
        tgt = pick(nbs[d], wslots)
        t_lv = pick(my_lv, tgt)
        live = (tgt >= 0) & act
        cols_f.append(jnp.where(live & (t_lv > levels[:, None]), tgt, -1))
        cols_b.append(jnp.where(live & (t_lv < levels[:, None]), tgt, -1))
    rows = jnp.stack(source_rows)
    row_hot = jnp.arange(ends_all.shape[0], dtype=jnp.int32)[None, :] == rows[:, None]
    src_begins = jnp.sum(jnp.where(row_hot[:, :, None], begins_all[None], 0), axis=1)
    src_levels = jnp.sum(jnp.where(row_hot[:, :, None], all_levels[None], 0), axis=1)
    lv_hot = levels[None, :] == levels[:, None]
    swin = jnp.sum(jnp.where(lv_hot[None], src_begins[:, None, :], 0), axis=2)
    swin = jnp.clip(swin, 0, slot_count - KL)
    sslots = swin[:, :, None] + offsets[None, None, :]
    slot_hot = sslots[..., None] == slots
    s_lv = jnp.sum(jnp.where(slot_hot, src_levels[:, None, None, :], 0), axis=3)
    s_act = s_lv == levels[None, :, None]
    nb_remote = jnp.stack(nbs[:4])
    stepped = jnp.sum(jnp.where(slot_hot, nb_remote[:, None, None, :], 0), axis=3)
    tgt = jnp.where(jnp.stack(at_edge)[:, None, None], stepped, sslots)
    tgt_hot = tgt[..., None] == slots
    t_lv = jnp.sum(jnp.where(tgt_hot, my_lv[None, None, None, :], 0), axis=3)
    live = (tgt >= 0) & s_act
    sent = levels[None, :, None]
    remote_f = jnp.where(live & (t_lv > sent), tgt, -1)
    remote_b = jnp.where(live & (t_lv < sent), tgt, -1)
    none_row = jnp.full((4, 1, KL), -1, jnp.int32)
    remote_f = jnp.concatenate([none_row, remote_f[:, :-1]], axis=1)
    remote_b = jnp.concatenate([remote_b[:, 1:], none_row], axis=1)
    for d in range(4):
        cols_f.append(remote_f[d])
        cols_b.append(remote_b[d])

    def finish(cols):
        table = jnp.concatenate(cols, axis=1).astype(jnp.int32)
        return jnp.pad(table, ((0, 0), (0, TW - table.shape[1])), constant_values=-1)

    return finish(cols_f), finish(cols_b)


def body(right_side, diag_inverse, face_jac, level_counts):
    slot_count = right_side.shape[0]
    unknowns = right_side.shape[1]
    gather_np, scatter_np = face_matrices(SIDE)
    gmat = jnp.asarray(gather_np, dtype=jnp.bfloat16)
    smat = jnp.asarray(scatter_np, dtype=jnp.bfloat16)
    jac = jnp.transpose(face_jac, (3, 0, 1, 2)).reshape(slot_count, NF * unknowns, unknowns)
    tbl_f, tbl_b = build_tables(level_counts, slot_count)
    zero_recv = tuple(jnp.zeros((KL, 16, 128), jnp.float32) for _ in range(4))

    def lev_arr(v):
        return jnp.reshape(jnp.asarray(v, jnp.int32), (1,))

    def sweep(forward, tbl, order, base, carry):

        def step(i, carry):
            accf, cur, sx, sy, zc, prev = carry
            recv = exchange(sx, sy)
            accf = run_update(lev_arr(order(i - 1)), tbl, accf, prev, zc)
            cur, sx, sy, zc = run_compute(forward, lev_arr(order(i)), tbl, accf, base, cur,
                                          diag_inverse, jac, recv, gmat, smat)
            return accf, cur, sx, sy, zc, recv

        return lax.fori_loop(1, LEVELS, step, carry)

    def blank_acc():
        return jnp.zeros((slot_count, unknowns, NF * FW), jnp.float32)

    cur = jnp.zeros(right_side.shape, jnp.float32)
    cur, sx, sy, zc = run_compute(True, lev_arr(0), tbl_f, blank_acc(), right_side, cur,
                                  diag_inverse, jac, zero_recv, gmat, smat)
    carry = (blank_acc(), cur, sx, sy, zc, zero_recv)
    _, half, sx, sy, zc, _ = sweep(True, tbl_f, lambda i: i, right_side, carry)
    carry = (blank_acc(), half, sx, sy, zc, zero_recv)
    result = sweep(False, tbl_b, lambda i: LEVELS - 1 - i, half, carry)[1]
    return result


def solution(mesh):
    return jax.shard_map(
        body,
        mesh=mesh,
        in_specs=(
            P(("gx", "gy"), None, None),
            P(("gx", "gy"), None, None, None),
            P(None, None, None, ("gx", "gy")),
            P(),
        ),
        out_specs=P(("gx", "gy"), None, None),
        check_vma=False,
    )
```
